32 devices in a mesh: copies: 2 (over y), dom: 8 (over z, x), cls: 2 (over core).
Axes of the slice: x: 2, y: 2, z: 4, core: 2. Of those that a mesh axis runs over, the one named last changes fastest.
Arguments:
- images: bfloat16 [512, 256, 256], P(('copies', 'dom', 'cls')), parts along dimension 0, may hold values from -100 to 100
- references: bfloat16 [128, 2, 128, 128], P(('copies', 'dom')), parts along dimension 0, may hold values from -6 to 6
- particle_class: int32 [512], P(('copies', 'dom', 'cls')), parts along dimension 0, may hold values from 0 to 63, as said below
- rotation: int32 [512], P(('copies', 'dom', 'cls')), parts along dimension 0, may hold values from 0 to 7
- defocus_bin: int32 [512], P(('copies', 'dom', 'cls')), parts along dimension 0, may hold values from 0 to 15
- window_anchor: int32 [2, 512], P(None, ('copies', 'dom', 'cls')), parts along dimension 1, may hold values from -12 to 12
Outputs:
- new_references: float32 [128, 2, 128, 128], P(('copies', 'dom'), None, 'cls'), parts along dimension 0
- particle_stats: float32 [3, 512], P(None, ('copies', 'dom', 'cls')), parts along dimension 1
The draws below stay inside these ranges and needn't reach their ends.
There are 2 independent parts, one for each index of `copies`. The reference program is written for one: setup_inputs(seed, part) draws one part's arguments, and reference() takes and returns one part's arrays. A program takes and returns all parts, laid end to end along the dimension named above; each array names one. Nothing has to cross between parts.
Inputs may be any that keep to these rules, and one draw needn't show every extreme that they name: `particle_class`: among the particles of one device, at most 4 have classes c with the same c // 8; in every draw some value of c // 8 is taken by exactly 4 particles of every device.
All inputs are finite; a program needn't handle non-finite values.
Results may differ from the reference program's by a relative error of at most 0.012.
The reference program's roundings to bfloat16 on the way count: a program that leaves them out, or rounds other values in their place, can miss the bound.
Values may be sent and summed in bfloat16 or wider, within the bound.
No kernel may reach another device: no remote copies, remote signals or barrier semaphores. Data moves between devices by JAX's collectives and lax.ppermute only.
A program may use at most 128 MiB of HBM per device.

```python
import math
import jax
import jax.numpy as jnp
from jax import lax

IMG = 256
FWIN = 128
CLASS_DEV = 8
P_DEV = 16
TW = 8
NBINS = 16
CLASSES = 64
PARTICLES = 256
CAP = 4


def draw_particle_class(key, part):
    owners = CLASSES // CLASS_DEV
    blocks = PARTICLES // P_DEV
    slot_total = owners * CAP
    key_hot, key_favour, key_noise, key_local, key_order = jax.random.split(jax.random.fold_in(key, 11), 5)
    hot_owner = jax.random.randint(key_hot, (), 0, owners)
    favour = jax.random.randint(key_favour, (owners,), 0, 2)
    noise = jax.random.randint(key_noise, (blocks, slot_total), 0, 2 ** 20)
    slot_ids = jnp.arange(slot_total, dtype=jnp.int32)
    owner_of = slot_ids // CAP
    scores = (favour[owner_of][None, :] * 2 ** 19 + noise) * slot_total + slot_ids[None, :]
    scores = jnp.where((owner_of == hot_owner)[None, :], 2 ** 30 + slot_ids[None, :], scores)
    unused, picked = lax.top_k(scores, P_DEV)
    owner_ids = picked // CAP
    local_ids = jax.random.randint(key_local, (blocks, P_DEV), 0, CLASS_DEV)
    classes = owner_ids * CLASS_DEV + local_ids
    order_keys = jax.random.randint(key_order, (blocks, P_DEV), 0, 2 ** 20) * P_DEV + jnp.arange(P_DEV, dtype=jnp.int32)[None, :]
    order = jnp.argsort(order_keys, axis=1)
    classes = jnp.take_along_axis(classes, order, axis=1)
    return classes.reshape(PARTICLES).astype(jnp.int32)


def draw_images(key, part):
    key_noise = jax.random.fold_in(jax.random.fold_in(key, 23), 0)
    noise = jax.random.normal(key_noise, (PARTICLES, IMG, IMG), jnp.float32)
    values = jnp.clip(noise, -6.0, 6.0)
    return values.astype(jnp.bfloat16)


def plant(entries, stream_key, low, high):
    place = [jax.random.randint(jax.random.fold_in(stream_key, axis), (), 0, length) for axis, length in enumerate(entries.shape)]
    main_axis = entries.shape.index(max(entries.shape))
    beside = place[:main_axis] + [(place[main_axis] + 1) % entries.shape[main_axis]] + place[main_axis + 1:]
    return entries.at[tuple(place)].set(low).at[tuple(beside)].set(high)


def shard_levels(key, extent, shards, low, top_value):
    gain, own = 1.0, jax.random.fold_in(key, 6)
    for axis_at, blocks in shards:
        draws = jnp.exp(jax.random.uniform(jax.random.fold_in(own, axis_at), (blocks,), jnp.float32, low / len(shards), top_value / len(shards)))
        gain = gain * jnp.repeat(draws, extent[axis_at] // blocks).reshape([-1 if axis == axis_at else 1 for axis in range(len(extent))])
    return gain


def normal_values(rng, extent, deviation, reach, cuts=(), held_as=jnp.bfloat16):
    values = jax.random.normal(rng, extent, jnp.float32) * deviation
    if len(cuts) > 0:
        values = shard_levels(rng, extent, cuts, -0.22, 0.18) * values
    return jnp.clip(values, min=-reach, max=reach).astype(held_as)


def setup_inputs(seed: int = 0, part: int = 0) -> dict:
    arg_keys = jax.random.split(jax.random.key(seed), 7)
    part_splits = jax.random.split(jax.random.fold_in(arg_keys[6], part), 7)
    return {
        "images": draw_images(jax.random.fold_in(jax.random.fold_in(arg_keys[6], part), 71), part),
        "references": normal_values(part_splits[1], (CLASSES, 2, FWIN, FWIN), 1.0, 6.0, ((0, 8),)),
        "particle_class": draw_particle_class(jax.random.fold_in(jax.random.fold_in(arg_keys[6], part), 71), part),
        "rotation": plant(jax.random.randint(part_splits[3], (PARTICLES,), 0, 8), jax.random.fold_in(part_splits[3], 1), 0, 7).astype(jnp.int32),
        "defocus_bin": plant(jax.random.randint(part_splits[4], (PARTICLES,), 0, NBINS), jax.random.fold_in(part_splits[4], 1), 0, NBINS - 1).astype(jnp.int32),
        "window_anchor": plant(jax.random.randint(part_splits[5], (2, PARTICLES), -12, 13), jax.random.fold_in(part_splits[5], 1), -12, 12).astype(jnp.int32),
    }


score_scale = 0.02
ridge_term = 1.0
highest = lax.Precision.HIGHEST

def freq_ids(win_side):
    return jnp.arange(win_side, dtype=jnp.int32) - win_side // 2

def dft_tables(img_side, win_side):
    phase_int = freq_ids(win_side)[:, None] * jnp.arange(img_side, dtype=jnp.int32)[None, :] % img_side
    angles = phase_int.astype(jnp.float32) * (2.0 * math.pi / img_side)
    scale_by = 1.0 / math.sqrt(img_side)
    return ((jnp.cos(angles) * scale_by).astype(jnp.bfloat16), (-jnp.sin(angles) * scale_by).astype(jnp.bfloat16))

def shift_tables(anchor, img_side, win_side, span_len):
    shifts = anchor[:, None] + jnp.arange(span_len, dtype=jnp.int32)[None, :] - span_len // 2
    phase_int = freq_ids(win_side)[None, :, None] * shifts[:, None, :] % img_side
    angles = phase_int.astype(jnp.float32) * (2.0 * math.pi / img_side)
    return (jnp.cos(angles).astype(jnp.bfloat16), jnp.sin(angles).astype(jnp.bfloat16), shifts.astype(jnp.float32))

def ctf_table(bin_ids, win_side):
    freqs = freq_ids(win_side).astype(jnp.float32)
    radius = (freqs[:, None] * freqs[:, None] + freqs[None, :] * freqs[None, :]) / float(win_side * win_side)
    strength = 20.0 + 6.0 * bin_ids.astype(jnp.float32)
    return -jnp.sin(strength[:, None, None] * radius[None, :, :] + 0.1)

def rotate_grid(stack_in, rot_ids):
    flag_bits = rot_ids[:, None, None]
    result = jnp.where(flag_bits & 4 != 0, jnp.swapaxes(stack_in, 1, 2), stack_in)
    result = jnp.where(flag_bits & 1 != 0, result[:, ::-1, :], result)
    return jnp.where(flag_bits & 2 != 0, result[:, :, ::-1], result)

def transform(aligned, dft_cos, dft_sin):
    win_side = dft_cos.shape[0]
    stacked = jnp.concatenate([dft_cos, dft_sin], axis=0).astype(jnp.float32)
    half_done = jnp.einsum('nyx,kx->nyk', aligned.astype(jnp.float32), stacked, precision=highest).astype(jnp.bfloat16)
    from_cos = jnp.einsum('jy,nyk->njk', dft_cos.astype(jnp.float32), half_done.astype(jnp.float32), precision=highest)
    from_sin = jnp.einsum('jy,nyk->njk', dft_sin.astype(jnp.float32), half_done.astype(jnp.float32), precision=highest)
    real_part = from_cos[..., :win_side] - from_sin[..., win_side:]
    imag_part = from_cos[..., win_side:] + from_sin[..., :win_side]
    return jnp.stack([real_part, imag_part], axis=1).astype(jnp.bfloat16)

def evaluate(fourier, chosen, ctf_map, row_cos, row_sin, col_cos, col_sin, row_shift, col_shift):
    span_len = col_cos.shape[2]
    coef_re = fourier[:, 0].astype(jnp.float32)
    coef_im = fourier[:, 1].astype(jnp.float32)
    pred_re = ctf_map * chosen[:, 0].astype(jnp.float32)
    pred_im = ctf_map * chosen[:, 1].astype(jnp.float32)
    prod_re = (coef_re * pred_re + coef_im * pred_im).astype(jnp.bfloat16)
    prod_im = (coef_im * pred_re - coef_re * pred_im).astype(jnp.bfloat16)
    shift_col = jnp.concatenate([col_cos, col_sin], axis=2).astype(jnp.float32)
    from_real = jnp.einsum('nuv,nvb->nub', prod_re.astype(jnp.float32), shift_col, precision=highest)
    from_imag = jnp.einsum('nuv,nvb->nub', prod_im.astype(jnp.float32), shift_col, precision=highest)
    part_re = from_real[..., :span_len] - from_imag[..., span_len:]
    part_im = from_real[..., span_len:] + from_imag[..., :span_len]
    cos_rows = row_cos.astype(jnp.float32)
    sin_rows = row_sin.astype(jnp.float32)
    cos_cols = col_cos.astype(jnp.float32)
    sin_cols = col_sin.astype(jnp.float32)
    correl = jnp.einsum('nua,nub->nab', cos_rows, part_re, precision=highest) - jnp.einsum('nua,nub->nab', sin_rows, part_im, precision=highest)
    score = score_scale * correl.reshape(fourier.shape[0], span_len * span_len)
    peak = lax.optimization_barrier(jnp.max(score, axis=1, keepdims=True))
    evidence = peak[:, 0] + jnp.log(lax.optimization_barrier(jnp.sum(jnp.exp(score - peak), axis=1)))
    weight = jnp.exp(score - evidence[:, None]).reshape(fourier.shape[0], span_len, span_len)
    mean_row = lax.optimization_barrier(jnp.sum(lax.optimization_barrier(jnp.sum(weight, axis=2)) * row_shift, axis=1))
    mean_col = lax.optimization_barrier(jnp.sum(lax.optimization_barrier(jnp.sum(weight, axis=1)) * col_shift, axis=1))
    qpart_re = jnp.einsum('nab,nvb->nav', weight, cos_cols, precision=highest)
    qpart_im = jnp.einsum('nab,nvb->nav', weight, sin_cols, precision=highest)
    back_re = jnp.einsum('nua,nav->nuv', cos_rows, qpart_re, precision=highest) - jnp.einsum('nua,nav->nuv', sin_rows, qpart_im, precision=highest)
    back_im = jnp.einsum('nua,nav->nuv', cos_rows, qpart_im, precision=highest) + jnp.einsum('nua,nav->nuv', sin_rows, qpart_re, precision=highest)
    term_re = ctf_map * (coef_re * back_re - coef_im * back_im)
    term_im = ctf_map * (coef_re * back_im + coef_im * back_re)
    class_terms = jnp.stack([term_re, term_im, ctf_map * ctf_map], axis=1)
    particle_info = jnp.stack([evidence, mean_row, mean_col], axis=1)
    return (class_terms, particle_info)

def reference(images, references, particle_class, rotation, defocus_bin, window_anchor):
    img_side = images.shape[1]
    win_side = references.shape[2]
    dft_cos, dft_sin = dft_tables(img_side, win_side)
    blocks = PARTICLES // P_DEV

    def one_block(summed, block):
        pictures, cls_ids, rot_ids, bin_ids, anchors = block
        aligned = rotate_grid(pictures, rot_ids)
        fourier = transform(aligned, dft_cos, dft_sin)
        chosen = jnp.take(references, cls_ids, axis=0)
        ctf_map = ctf_table(bin_ids, win_side)
        row_cos, row_sin, row_shift = shift_tables(anchors[0], img_side, win_side, TW)
        col_cos, col_sin, col_shift = shift_tables(anchors[1], img_side, win_side, TW)
        class_terms, particle_info = evaluate(fourier, chosen, ctf_map, row_cos, row_sin, col_cos, col_sin, row_shift, col_shift)
        summed = summed.at[cls_ids].add(class_terms)
        return (summed, particle_info)
    inputs = (images.reshape(blocks, P_DEV, img_side, img_side), particle_class.reshape(blocks, P_DEV), rotation.reshape(blocks, P_DEV), defocus_bin.reshape(blocks, P_DEV), jnp.transpose(window_anchor.reshape(2, blocks, P_DEV), (1, 0, 2)))
    initial = jnp.zeros((CLASSES, 3, win_side, win_side), jnp.float32)
    summed, info_rows = lax.scan(one_block, initial, inputs)
    divisor = summed[:, 2] + ridge_term
    new_refs = summed[:, :2] / divisor[:, None]
    return (new_refs, info_rows.reshape(PARTICLES, 3).T)
```

```python
import math

import jax
import jax.numpy as jnp
from jax import lax
from jax.sharding import PartitionSpec as P

TW = 8


score_scale = 0.02
ridge_term = 1.0
highest = lax.Precision.HIGHEST


def freq_ids(win_side):
    return jnp.arange(win_side, dtype=jnp.int32) - win_side // 2


def dft_tables(img_side, win_side):
    phase_int = (
        freq_ids(win_side)[:, None] * jnp.arange(img_side, dtype=jnp.int32)[None, :] % img_side
    )
    angles = phase_int.astype(jnp.float32) * (2.0 * math.pi / img_side)
    scale_by = 1.0 / math.sqrt(img_side)
    return (
        (jnp.cos(angles) * scale_by).astype(jnp.bfloat16),
        (-jnp.sin(angles) * scale_by).astype(jnp.bfloat16),
    )


def shift_tables(anchor, img_side, win_side, span_len):
    shifts = anchor[:, None] + jnp.arange(span_len, dtype=jnp.int32)[None, :] - span_len // 2
    phase_int = freq_ids(win_side)[None, :, None] * shifts[:, None, :] % img_side
    angles = phase_int.astype(jnp.float32) * (2.0 * math.pi / img_side)
    return (
        jnp.cos(angles).astype(jnp.bfloat16),
        jnp.sin(angles).astype(jnp.bfloat16),
        shifts.astype(jnp.float32),
    )


def ctf_table(bin_ids, win_side):
    freqs = freq_ids(win_side).astype(jnp.float32)
    radius = (freqs[:, None] * freqs[:, None] + freqs[None, :] * freqs[None, :]) / float(
        win_side * win_side
    )
    strength = 20.0 + 6.0 * bin_ids.astype(jnp.float32)
    return -jnp.sin(strength[:, None, None] * radius[None, :, :] + 0.1)


def rotate_grid(stack_in, rot_ids):
    flag_bits = rot_ids[:, None, None]
    result = jnp.where(flag_bits & 4 != 0, jnp.swapaxes(stack_in, 1, 2), stack_in)
    result = jnp.where(flag_bits & 1 != 0, result[:, ::-1, :], result)
    return jnp.where(flag_bits & 2 != 0, result[:, :, ::-1], result)


def transform(images, rot_ids, dft_cos, dft_sin):
    win_side = dft_cos.shape[0]
    stacked = jnp.concatenate([dft_cos, dft_sin], axis=0)
    flag_bits = rot_ids[:, None, None]
    col_table = jnp.where(flag_bits & 2 != 0, stacked[None, :, ::-1], stacked[None])
    plain = jnp.einsum("nyx,nkx->nyk", images, col_table, preferred_element_type=jnp.float32)
    turned = jnp.einsum("nxy,nkx->nyk", images, col_table, preferred_element_type=jnp.float32)
    half_done = jnp.where(flag_bits & 4 != 0, turned, plain).astype(jnp.bfloat16)
    row_cos = jnp.where(flag_bits & 1 != 0, dft_cos[None, :, ::-1], dft_cos[None])
    row_sin = jnp.where(flag_bits & 1 != 0, dft_sin[None, :, ::-1], dft_sin[None])
    from_cos = jnp.einsum("njy,nyk->njk", row_cos, half_done, preferred_element_type=jnp.float32)
    from_sin = jnp.einsum("njy,nyk->njk", row_sin, half_done, preferred_element_type=jnp.float32)
    real_part = from_cos[..., :win_side] - from_sin[..., win_side:]
    imag_part = from_cos[..., win_side:] + from_sin[..., :win_side]
    return jnp.stack([real_part, imag_part], axis=1).astype(jnp.bfloat16)


def evaluate(fourier, chosen, ctf_map, row_cos, row_sin, col_cos, col_sin, row_shift, col_shift):
    span_len = col_cos.shape[2]
    coef_re = fourier[:, 0].astype(jnp.float32)
    coef_im = fourier[:, 1].astype(jnp.float32)
    pred_re = ctf_map * chosen[:, 0].astype(jnp.float32)
    pred_im = ctf_map * chosen[:, 1].astype(jnp.float32)
    prod_re = (coef_re * pred_re + coef_im * pred_im).astype(jnp.bfloat16)
    prod_im = (coef_im * pred_re - coef_re * pred_im).astype(jnp.bfloat16)
    shift_col = jnp.concatenate([col_cos, col_sin], axis=2)
    from_real = jnp.einsum("nuv,nvb->nub", prod_re, shift_col, preferred_element_type=jnp.float32)
    from_imag = jnp.einsum("nuv,nvb->nub", prod_im, shift_col, preferred_element_type=jnp.float32)
    part_re = from_real[..., :span_len] - from_imag[..., span_len:]
    part_im = from_real[..., span_len:] + from_imag[..., :span_len]
    cos_rows = row_cos.astype(jnp.float32)
    sin_rows = row_sin.astype(jnp.float32)
    cos_cols = col_cos.astype(jnp.float32)
    sin_cols = col_sin.astype(jnp.float32)
    correl = jnp.einsum("nua,nub->nab", cos_rows, part_re, precision=highest) - jnp.einsum(
        "nua,nub->nab", sin_rows, part_im, precision=highest
    )
    score = score_scale * correl.reshape(fourier.shape[0], span_len * span_len)
    peak = jnp.max(score, axis=1, keepdims=True)
    evidence = peak[:, 0] + jnp.log(jnp.sum(jnp.exp(score - peak), axis=1))
    weight = jnp.exp(score - evidence[:, None]).reshape(fourier.shape[0], span_len, span_len)
    mean_row = jnp.sum(jnp.sum(weight, axis=2) * row_shift, axis=1)
    mean_col = jnp.sum(jnp.sum(weight, axis=1) * col_shift, axis=1)
    qpart_re = jnp.einsum("nab,nvb->nav", weight, cos_cols, precision=highest)
    qpart_im = jnp.einsum("nab,nvb->nav", weight, sin_cols, precision=highest)
    rows_both = jnp.concatenate([cos_rows, sin_rows], axis=2)
    for_real = jnp.concatenate([qpart_re, -qpart_im], axis=1)
    for_imag = jnp.concatenate([qpart_im, qpart_re], axis=1)
    back_re = jnp.einsum("nua,nav->nuv", rows_both, for_real, precision=highest)
    back_im = jnp.einsum("nua,nav->nuv", rows_both, for_imag, precision=highest)
    term_re = ctf_map * (coef_re * back_re - coef_im * back_im)
    term_im = ctf_map * (coef_re * back_im + coef_im * back_re)
    class_terms = jnp.stack([term_re, term_im, ctf_map * ctf_map], axis=1)
    particle_info = jnp.stack([evidence, mean_row, mean_col], axis=1)
    return (class_terms, particle_info)


def assess(fourier, tag_block, references, owners, img_side):
    win_side = references.shape[2]
    items = tag_block.shape[1]
    tag_flat = tag_block.reshape(owners * items, 4).astype(jnp.int32)
    class_tag = tag_flat[:, 0]
    chosen = jnp.take(references, jnp.maximum(class_tag - 1, 0), axis=0)
    ctf_map = ctf_table(tag_flat[:, 1], win_side)
    row_cos, row_sin, row_shift = shift_tables(tag_flat[:, 2], img_side, win_side, TW)
    col_cos, col_sin, col_shift = shift_tables(tag_flat[:, 3], img_side, win_side, TW)
    class_terms, particle_info = evaluate(
        fourier, chosen, ctf_map, row_cos, row_sin, col_cos, col_sin, row_shift, col_shift
    )
    returned = lax.all_to_all(
        particle_info.reshape(owners, items, 3), "dom", split_axis=0, concat_axis=0, tiled=True
    )
    return (
        class_terms.reshape(owners, items, 3, win_side, win_side),
        class_tag.reshape(owners, items),
        returned,
    )


def on_device(images, references, particle_class, rotation, defocus_bin, window_anchor):
    part_count = images.shape[0]
    img_side = images.shape[1]
    win_side = references.shape[2]
    per_owner = references.shape[0]
    owners = lax.axis_size("dom")
    capacity = max(2, 2 * part_count // owners)
    slot_count = owners * capacity
    target = particle_class // per_owner
    local_class = particle_class - target * per_owner
    positions = jnp.arange(part_count, dtype=jnp.int32)
    same_owner = (target[:, None] == target[None, :]) & (positions[None, :] < positions[:, None])
    slot_rank = jnp.sum(same_owner.astype(jnp.int32), axis=1)
    slot_place = target * capacity + slot_rank
    slot_tags = jnp.stack(
        [local_class + 1, defocus_bin, window_anchor[0], window_anchor[1]], axis=1
    ).astype(jnp.bfloat16)
    tag_buffer = (
        jnp.zeros((slot_count, 4), jnp.bfloat16)
        .at[slot_place]
        .set(slot_tags)
        .reshape(owners, capacity, 4)
    )
    dft_cos, dft_sin = dft_tables(img_side, win_side)
    fourier_own = transform(images, rotation, dft_cos, dft_sin)
    buffer = (
        jnp.zeros((slot_count, 2, win_side, win_side), jnp.bfloat16).at[slot_place].set(fourier_own)
    )
    buffer = buffer.reshape(owners, capacity, 2, win_side, win_side)
    coeff_block = lax.all_to_all(buffer, "dom", split_axis=0, concat_axis=0, tiled=True)
    tag_block = lax.all_to_all(tag_buffer, "dom", split_axis=0, concat_axis=0, tiled=True)
    items = coeff_block.shape[1]
    class_terms, labels, returned = assess(
        coeff_block.reshape(owners * items, 2, win_side, win_side),
        tag_block,
        references,
        owners,
        img_side,
    )
    class_terms = class_terms.reshape(slot_count, 3, win_side, win_side)
    labels = labels.reshape(slot_count)
    member = (labels[None, :] == jnp.arange(1, per_owner + 1, dtype=jnp.int32)[:, None]).astype(
        jnp.float32
    )
    partial_value = jnp.einsum("cs,srjk->crjk", member, class_terms, precision=highest)
    summed = lax.psum_scatter(partial_value, "cls", scatter_dimension=2, tiled=True)
    divisor = summed[:, 2] + ridge_term
    new_refs = summed[:, :2] / divisor[:, None]
    particle_info = returned.reshape(slot_count, 3)[slot_place]
    return (new_refs, particle_info.T)


def solution(mesh):
    return jax.shard_map(
        on_device,
        mesh=mesh,
        in_specs=(
            P(("copies", "dom", "cls"), None, None),
            P(("copies", "dom"), None, None, None),
            P(("copies", "dom", "cls")),
            P(("copies", "dom", "cls")),
            P(("copies", "dom", "cls")),
            P(None, ("copies", "dom", "cls")),
        ),
        out_specs=(P(("copies", "dom"), None, "cls", None), P(None, ("copies", "dom", "cls"))),
        check_vma=False,
    )
```

```python
import math

import jax
import jax.numpy as jnp
from jax import lax
from jax.sharding import PartitionSpec as P


TW = 8


score_scale = 0.02
ridge_term = 1.0
highest = lax.Precision.HIGHEST


def freq_ids(win_side):
    return jnp.arange(win_side, dtype=jnp.int32) - win_side // 2


def dft_tables(img_side, win_side):
    phase_int = (
        freq_ids(win_side)[:, None] * jnp.arange(img_side, dtype=jnp.int32)[None, :] % img_side
    )
    angles = phase_int.astype(jnp.float32) * (2.0 * math.pi / img_side)
    scale_by = 1.0 / math.sqrt(img_side)
    return (
        (jnp.cos(angles) * scale_by).astype(jnp.bfloat16),
        (-jnp.sin(angles) * scale_by).astype(jnp.bfloat16),
    )


def shift_tables(anchor, img_side, win_side, span_len):
    shifts = anchor[:, None] + jnp.arange(span_len, dtype=jnp.int32)[None, :] - span_len // 2
    phase_int = freq_ids(win_side)[None, :, None] * shifts[:, None, :] % img_side
    angles = phase_int.astype(jnp.float32) * (2.0 * math.pi / img_side)
    return (
        jnp.cos(angles).astype(jnp.bfloat16),
        jnp.sin(angles).astype(jnp.bfloat16),
        shifts.astype(jnp.float32),
    )


def ctf_table(bin_ids, win_side):
    freqs = freq_ids(win_side).astype(jnp.float32)
    radius = (freqs[:, None] * freqs[:, None] + freqs[None, :] * freqs[None, :]) / float(
        win_side * win_side
    )
    strength = 20.0 + 6.0 * bin_ids.astype(jnp.float32)
    return -jnp.sin(strength[:, None, None] * radius[None, :, :] + 0.1)


def transform(images, rot_ids, dft_cos, dft_sin):
    win_side = dft_cos.shape[0]
    stacked = jnp.concatenate([dft_cos, dft_sin], axis=0)
    flag_bits = rot_ids[:, None, None]
    col_table = jnp.where(flag_bits & 2 != 0, stacked[None, :, ::-1], stacked[None])
    plain = jnp.einsum("nyx,nkx->nyk", images, col_table, preferred_element_type=jnp.float32)
    turned = jnp.einsum("nxy,nkx->nyk", images, col_table, preferred_element_type=jnp.float32)
    half_done = jnp.where(flag_bits & 4 != 0, turned, plain).astype(jnp.bfloat16)
    row_cos = jnp.where(flag_bits & 1 != 0, dft_cos[None, :, ::-1], dft_cos[None])
    row_sin = jnp.where(flag_bits & 1 != 0, dft_sin[None, :, ::-1], dft_sin[None])
    from_cos = jnp.einsum("njy,nyk->njk", row_cos, half_done, preferred_element_type=jnp.float32)
    from_sin = jnp.einsum("njy,nyk->njk", row_sin, half_done, preferred_element_type=jnp.float32)
    real_part = from_cos[..., :win_side] - from_sin[..., win_side:]
    imag_part = from_cos[..., win_side:] + from_sin[..., :win_side]
    return jnp.stack([real_part, imag_part], axis=1).astype(jnp.bfloat16)


def evaluate(fourier, chosen, ctf_map, row_cos, row_sin, col_cos, col_sin, row_shift, col_shift):
    span_len = col_cos.shape[2]
    coef_re = fourier[:, 0].astype(jnp.float32)
    coef_im = fourier[:, 1].astype(jnp.float32)
    pred_re = ctf_map * chosen[:, 0].astype(jnp.float32)
    pred_im = ctf_map * chosen[:, 1].astype(jnp.float32)
    prod_re = (coef_re * pred_re + coef_im * pred_im).astype(jnp.bfloat16)
    prod_im = (coef_im * pred_re - coef_re * pred_im).astype(jnp.bfloat16)
    shift_col = jnp.concatenate([col_cos, col_sin], axis=2)
    from_real = jnp.einsum("nuv,nvb->nub", prod_re, shift_col, preferred_element_type=jnp.float32)
    from_imag = jnp.einsum("nuv,nvb->nub", prod_im, shift_col, preferred_element_type=jnp.float32)
    part_re = from_real[..., :span_len] - from_imag[..., span_len:]
    part_im = from_real[..., span_len:] + from_imag[..., :span_len]
    cos_rows = row_cos.astype(jnp.float32)
    sin_rows = row_sin.astype(jnp.float32)
    cos_cols = col_cos.astype(jnp.float32)
    sin_cols = col_sin.astype(jnp.float32)
    correl = jnp.einsum("nua,nub->nab", cos_rows, part_re, precision=highest) - jnp.einsum(
        "nua,nub->nab", sin_rows, part_im, precision=highest
    )
    score = score_scale * correl.reshape(fourier.shape[0], span_len * span_len)
    peak = jnp.max(score, axis=1, keepdims=True)
    evidence = peak[:, 0] + jnp.log(jnp.sum(jnp.exp(score - peak), axis=1))
    weight = jnp.exp(score - evidence[:, None]).reshape(fourier.shape[0], span_len, span_len)
    mean_row = jnp.sum(jnp.sum(weight, axis=2) * row_shift, axis=1)
    mean_col = jnp.sum(jnp.sum(weight, axis=1) * col_shift, axis=1)
    qpart_re = jnp.einsum("nab,nvb->nav", weight, cos_cols, precision=highest)
    qpart_im = jnp.einsum("nab,nvb->nav", weight, sin_cols, precision=highest)
    rows_both = jnp.concatenate([cos_rows, sin_rows], axis=2)
    for_real = jnp.concatenate([qpart_re, -qpart_im], axis=1)
    for_imag = jnp.concatenate([qpart_im, qpart_re], axis=1)
    back_re = jnp.einsum("nua,nav->nuv", rows_both, for_real, precision=highest)
    back_im = jnp.einsum("nua,nav->nuv", rows_both, for_imag, precision=highest)
    term_re = ctf_map * (coef_re * back_re - coef_im * back_im)
    term_im = ctf_map * (coef_re * back_im + coef_im * back_re)
    class_terms = jnp.stack([term_re, term_im, ctf_map * ctf_map], axis=1)
    particle_info = jnp.stack([evidence, mean_row, mean_col], axis=1)
    return (class_terms, particle_info)


def assess(fourier, tag_block, references, img_side):
    win_side = references.shape[2]
    tag_flat = tag_block.reshape(-1, 4).astype(jnp.int32)
    class_tag = tag_flat[:, 0]
    chosen = jnp.take(references, jnp.maximum(class_tag - 1, 0), axis=0)
    ctf_map = ctf_table(tag_flat[:, 1], win_side)
    row_cos, row_sin, row_shift = shift_tables(tag_flat[:, 2], img_side, win_side, TW)
    col_cos, col_sin, col_shift = shift_tables(tag_flat[:, 3], img_side, win_side, TW)
    class_terms, particle_info = evaluate(
        fourier, chosen, ctf_map, row_cos, row_sin, col_cos, col_sin, row_shift, col_shift
    )
    per_owner = references.shape[0]
    member = (class_tag[None, :] == jnp.arange(1, per_owner + 1, dtype=jnp.int32)[:, None]).astype(
        jnp.float32
    )
    partial_value = jnp.einsum("cs,srjk->crjk", member, class_terms, precision=highest)
    return partial_value, particle_info


def on_device(images, references, particle_class, rotation, defocus_bin, window_anchor):
    part_count = images.shape[0]
    img_side = images.shape[1]
    win_side = references.shape[2]
    per_owner = references.shape[0]
    owners = lax.axis_size("dom")
    capacity = max(2, 2 * part_count // owners)
    slot_count = owners * capacity
    target = particle_class // per_owner
    local_class = particle_class - target * per_owner
    positions = jnp.arange(part_count, dtype=jnp.int32)
    same_owner = (target[:, None] == target[None, :]) & (positions[None, :] < positions[:, None])
    slot_rank = jnp.sum(same_owner.astype(jnp.int32), axis=1)
    slot_place = target * capacity + slot_rank
    slot_tags = jnp.stack(
        [local_class + 1, defocus_bin, window_anchor[0], window_anchor[1]], axis=1
    ).astype(jnp.bfloat16)
    tag_buffer = (
        jnp.zeros((slot_count, 4), jnp.bfloat16)
        .at[slot_place]
        .set(slot_tags)
        .reshape(owners, capacity, 4)
    )
    tag_block = lax.all_to_all(tag_buffer, "dom", split_axis=0, concat_axis=0, tiled=True)
    dft_cos, dft_sin = dft_tables(img_side, win_side)
    fourier_own = transform(images, rotation, dft_cos, dft_sin)
    buffer = (
        jnp.zeros((slot_count, 2, win_side, win_side), jnp.bfloat16).at[slot_place].set(fourier_own)
    )
    buffer = buffer.reshape(owners, capacity, 2, win_side, win_side)
    first = capacity // 2
    bounds = ((0, first), (first, capacity))
    received = []
    for lo, hi in bounds:
        received.append(
            lax.all_to_all(buffer[:, lo:hi], "dom", split_axis=0, concat_axis=0, tiled=True)
        )
    partial_value = None
    infos = []
    for (lo, hi), coeff_block in zip(bounds, received):
        value, info = assess(
            coeff_block.reshape(owners * (hi - lo), 2, win_side, win_side),
            tag_block[:, lo:hi],
            references,
            img_side,
        )
        partial_value = value if partial_value is None else partial_value + value
        infos.append(info.reshape(owners, hi - lo, 3))
    returned = lax.all_to_all(
        jnp.concatenate(infos, axis=1), "dom", split_axis=0, concat_axis=0, tiled=True
    )
    summed = lax.psum_scatter(partial_value, "cls", scatter_dimension=2, tiled=True)
    divisor = summed[:, 2] + ridge_term
    new_refs = summed[:, :2] / divisor[:, None]
    particle_info = returned.reshape(slot_count, 3)[slot_place]
    return (new_refs, particle_info.T)


def solution(mesh):
    return jax.shard_map(
        on_device,
        mesh=mesh,
        in_specs=(
            P(("copies", "dom", "cls"), None, None),
            P(("copies", "dom"), None, None, None),
            P(("copies", "dom", "cls")),
            P(("copies", "dom", "cls")),
            P(("copies", "dom", "cls")),
            P(None, ("copies", "dom", "cls")),
        ),
        out_specs=(P(("copies", "dom"), None, "cls", None), P(None, ("copies", "dom", "cls"))),
        check_vma=False,
    )
```

```python
import math

import jax
import jax.numpy as jnp
from jax import lax
from jax.experimental import pallas as pl
from jax.experimental.pallas import tpu as pltpu
from jax.sharding import PartitionSpec as P

TW = 8


score_scale = 0.02
ridge_term = 1.0
highest = lax.Precision.HIGHEST


def freq_ids(win_side):
    return jnp.arange(win_side, dtype=jnp.int32) - win_side // 2


def dft_tables(img_side, win_side):
    phase_int = (
        freq_ids(win_side)[:, None] * jnp.arange(img_side, dtype=jnp.int32)[None, :] % img_side
    )
    angles = phase_int.astype(jnp.float32) * (2.0 * math.pi / img_side)
    scale_by = 1.0 / math.sqrt(img_side)
    return (
        (jnp.cos(angles) * scale_by).astype(jnp.bfloat16),
        (-jnp.sin(angles) * scale_by).astype(jnp.bfloat16),
    )


def shift_tables(anchor, img_side, win_side, span_len):
    shifts = anchor[:, None] + jnp.arange(span_len, dtype=jnp.int32)[None, :] - span_len // 2
    phase_int = freq_ids(win_side)[None, :, None] * shifts[:, None, :] % img_side
    angles = phase_int.astype(jnp.float32) * (2.0 * math.pi / img_side)
    return (
        jnp.cos(angles).astype(jnp.bfloat16),
        jnp.sin(angles).astype(jnp.bfloat16),
        shifts.astype(jnp.float32),
    )


def ctf_table(bin_ids, win_side):
    freqs = freq_ids(win_side).astype(jnp.float32)
    radius = (freqs[:, None] * freqs[:, None] + freqs[None, :] * freqs[None, :]) / float(
        win_side * win_side
    )
    strength = 20.0 + 6.0 * bin_ids.astype(jnp.float32)
    return -jnp.sin(strength[:, None, None] * radius[None, :, :] + 0.1)


def rotate_grid(stack_in, rot_ids):
    flag_bits = rot_ids[:, None, None]
    result = jnp.where(flag_bits & 4 != 0, jnp.swapaxes(stack_in, 1, 2), stack_in)
    result = jnp.where(flag_bits & 1 != 0, result[:, ::-1, :], result)
    return jnp.where(flag_bits & 2 != 0, result[:, :, ::-1], result)


def transform(images, rot_ids, dft_cos, dft_sin):
    win_side = dft_cos.shape[0]
    stacked = jnp.concatenate([dft_cos, dft_sin], axis=0)
    flag_bits = rot_ids[:, None, None]
    col_table = jnp.where(flag_bits & 2 != 0, stacked[None, :, ::-1], stacked[None])
    plain = jnp.einsum("nyx,nkx->nyk", images, col_table, preferred_element_type=jnp.float32)
    turned = jnp.einsum("nxy,nkx->nyk", images, col_table, preferred_element_type=jnp.float32)
    half_done = jnp.where(flag_bits & 4 != 0, turned, plain).astype(jnp.bfloat16)
    row_cos = jnp.where(flag_bits & 1 != 0, dft_cos[None, :, ::-1], dft_cos[None])
    row_sin = jnp.where(flag_bits & 1 != 0, dft_sin[None, :, ::-1], dft_sin[None])
    from_cos = jnp.einsum("njy,nyk->njk", row_cos, half_done, preferred_element_type=jnp.float32)
    from_sin = jnp.einsum("njy,nyk->njk", row_sin, half_done, preferred_element_type=jnp.float32)
    real_part = from_cos[..., :win_side] - from_sin[..., win_side:]
    imag_part = from_cos[..., win_side:] + from_sin[..., :win_side]
    return jnp.stack([real_part, imag_part], axis=1).astype(jnp.bfloat16)


def evaluate(fourier, chosen, ctf_map, row_cos, row_sin, col_cos, col_sin, row_shift, col_shift):
    span_len = col_cos.shape[2]
    coef_re = fourier[:, 0].astype(jnp.float32)
    coef_im = fourier[:, 1].astype(jnp.float32)
    pred_re = ctf_map * chosen[:, 0].astype(jnp.float32)
    pred_im = ctf_map * chosen[:, 1].astype(jnp.float32)
    prod_re = (coef_re * pred_re + coef_im * pred_im).astype(jnp.bfloat16)
    prod_im = (coef_im * pred_re - coef_re * pred_im).astype(jnp.bfloat16)
    shift_col = jnp.concatenate([col_cos, col_sin], axis=2)
    from_real = jnp.einsum("nuv,nvb->nub", prod_re, shift_col, preferred_element_type=jnp.float32)
    from_imag = jnp.einsum("nuv,nvb->nub", prod_im, shift_col, preferred_element_type=jnp.float32)
    part_re = from_real[..., :span_len] - from_imag[..., span_len:]
    part_im = from_real[..., span_len:] + from_imag[..., :span_len]
    cos_rows = row_cos.astype(jnp.float32)
    sin_rows = row_sin.astype(jnp.float32)
    cos_cols = col_cos.astype(jnp.float32)
    sin_cols = col_sin.astype(jnp.float32)
    correl = jnp.einsum("nua,nub->nab", cos_rows, part_re, precision=highest) - jnp.einsum(
        "nua,nub->nab", sin_rows, part_im, precision=highest
    )
    score = score_scale * correl.reshape(fourier.shape[0], span_len * span_len)
    peak = jnp.max(score, axis=1, keepdims=True)
    evidence = peak[:, 0] + jnp.log(jnp.sum(jnp.exp(score - peak), axis=1))
    weight = jnp.exp(score - evidence[:, None]).reshape(fourier.shape[0], span_len, span_len)
    mean_row = jnp.sum(jnp.sum(weight, axis=2) * row_shift, axis=1)
    mean_col = jnp.sum(jnp.sum(weight, axis=1) * col_shift, axis=1)
    qpart_re = jnp.einsum("nab,nvb->nav", weight, cos_cols, precision=highest)
    qpart_im = jnp.einsum("nab,nvb->nav", weight, sin_cols, precision=highest)
    rows_both = jnp.concatenate([cos_rows, sin_rows], axis=2)
    for_real = jnp.concatenate([qpart_re, -qpart_im], axis=1)
    for_imag = jnp.concatenate([qpart_im, qpart_re], axis=1)
    back_re = jnp.einsum("nua,nav->nuv", rows_both, for_real, precision=highest)
    back_im = jnp.einsum("nua,nav->nuv", rows_both, for_imag, precision=highest)
    term_re = ctf_map * (coef_re * back_re - coef_im * back_im)
    term_im = ctf_map * (coef_re * back_im + coef_im * back_re)
    class_terms = jnp.stack([term_re, term_im, ctf_map * ctf_map], axis=1)
    particle_info = jnp.stack([evidence, mean_row, mean_col], axis=1)
    return (class_terms, particle_info)


def _slot_kernel(meta_ref, coef_ref, ref_ref, ctf_ref, pack_ref, total_ref, info_ref):
    s = pl.program_id(0)
    span = 8

    @pl.when(s == 0)
    def _():
        total_ref[...] = jnp.zeros(total_ref.shape, total_ref.dtype)

    valid = meta_ref[0, s] > 0
    info_ref[...] = jnp.zeros(info_ref.shape, info_ref.dtype)

    @pl.when(valid)
    def _():
        cls = jnp.maximum(meta_ref[0, s] - 1, 0)
        coef_re = coef_ref[0, 0].astype(jnp.float32)
        coef_im = coef_ref[0, 1].astype(jnp.float32)
        ctf = ctf_ref[0]
        pred_re = ctf * ref_ref[0, 0].astype(jnp.float32)
        pred_im = ctf * ref_ref[0, 1].astype(jnp.float32)
        prod_re = (coef_re * pred_re + coef_im * pred_im).astype(jnp.bfloat16)
        prod_im = (coef_im * pred_re - coef_re * pred_im).astype(jnp.bfloat16)
        rows = pack_ref[0, 0]
        rows_t = pack_ref[0, 1].astype(jnp.float32)
        cols = pack_ref[0, 2]
        cols_b = pack_ref[0, 3]
        both = jnp.concatenate([prod_re, prod_im], axis=1)
        mix = jnp.concatenate([cols, cols_b], axis=0)
        part = jnp.dot(both, mix, preferred_element_type=jnp.float32)
        corr = jnp.dot(rows_t[0:16], part, precision=highest, preferred_element_type=jnp.float32)
        upper = corr[0:8]
        lower = pltpu.roll(corr[8:16], 128 - span, 1)
        lane = lax.broadcasted_iota(jnp.int32, (8, 128), 1)
        sub = lax.broadcasted_iota(jnp.int32, (8, 128), 0)
        inside = lane < span
        score = jnp.where(inside, score_scale * (upper - lower), -jnp.inf)
        peak = jnp.max(jnp.max(score, axis=1, keepdims=True), axis=0, keepdims=True)
        total = jnp.sum(jnp.sum(jnp.exp(score - peak), axis=1, keepdims=True), axis=0, keepdims=True)
        evidence = peak + jnp.log(total)
        weight = jnp.where(inside, jnp.exp(score - evidence), 0.0)
        row_shift = (jnp.full((8, 128), meta_ref[2, s], jnp.int32) + sub - span // 2).astype(jnp.float32)
        col_shift = (jnp.full((8, 128), meta_ref[3, s], jnp.int32) + lane - span // 2).astype(jnp.float32)
        by_row = jnp.sum(weight, axis=1, keepdims=True)
        mean_row = jnp.sum(by_row * row_shift[:, 0:1], axis=0, keepdims=True)
        by_col = jnp.sum(weight, axis=0, keepdims=True)
        mean_col = jnp.sum(jnp.where(inside[0:1], by_col * col_shift[0:1], 0.0), axis=1, keepdims=True)
        lane1 = lane[0:1]
        info_ref[0] = jnp.where(
            sub == 0,
            jnp.where(lane == 0, evidence, jnp.where(lane == 1, mean_row, jnp.where(lane == 2, mean_col, 0.0))),
            0.0,
        )
        shifted = pltpu.roll(weight, span, 1)
        stacked_w = jnp.concatenate([weight, shifted], axis=0)
        cols_f = cols.astype(jnp.float32)
        qpart = lax.dot_general(
            stacked_w, cols_f, (((1,), (1,)), ((), ())), precision=highest,
            preferred_element_type=jnp.float32,
        )
        q_re = qpart[0:8]
        q_im = qpart[8:16]
        pad = jnp.zeros((112, 128), jnp.float32)
        for_re = jnp.concatenate([q_re, -q_im, pad], axis=0)
        for_im = jnp.concatenate([q_im, q_re, pad], axis=0)
        rows_f = rows.astype(jnp.float32)
        back_re = jnp.dot(rows_f, for_re, precision=highest, preferred_element_type=jnp.float32)
        back_im = jnp.dot(rows_f, for_im, precision=highest, preferred_element_type=jnp.float32)
        term_re = ctf * (coef_re * back_re - coef_im * back_im)
        term_im = ctf * (coef_re * back_im + coef_im * back_re)
        total_ref[cls, 0] = total_ref[cls, 0] + term_re
        total_ref[cls, 1] = total_ref[cls, 1] + term_im
        total_ref[cls, 2] = total_ref[cls, 2] + ctf * ctf


def slot_eval(meta, coef, refs, ctf_tab, pack, interpret=False):
    slots = coef.shape[0]
    per_owner = refs.shape[0]
    win = coef.shape[2]
    bins = ctf_tab.shape[0]

    def coef_map(s, meta):
        return (s, 0, 0, 0)

    def ref_map(s, meta):
        return (jnp.clip(meta[0, s] - 1, 0, per_owner - 1), 0, 0, 0)

    def ctf_map(s, meta):
        return (jnp.clip(meta[1, s], 0, bins - 1), 0, 0)

    grid_spec = pltpu.PrefetchScalarGridSpec(
        num_scalar_prefetch=1,
        grid=(slots,),
        in_specs=[
            pl.BlockSpec((1, 2, win, win), coef_map),
            pl.BlockSpec((1, 2, win, win), ref_map),
            pl.BlockSpec((1, win, win), ctf_map),
            pl.BlockSpec((1, 4, win, win), coef_map),
        ],
        out_specs=[
            pl.BlockSpec((per_owner, 3, win, win), lambda s, meta: (0, 0, 0, 0)),
            pl.BlockSpec((1, 8, 128), lambda s, meta: (s, 0, 0)),
        ],
    )
    return pl.pallas_call(
        _slot_kernel,
        grid_spec=grid_spec,
        out_shape=[
            jax.ShapeDtypeStruct((per_owner, 3, win, win), jnp.float32),
            jax.ShapeDtypeStruct((slots, 8, 128), jnp.float32),
        ],
        compiler_params=pltpu.CompilerParams(dimension_semantics=("arbitrary",)),
        interpret=interpret,
    )(meta, coef, refs, ctf_tab, pack)


def phase_pack(tag_flat, img_side, win_side):
    rc, rs, _ = shift_tables(tag_flat[:, 2], img_side, win_side, TW)
    cc, cs, _ = shift_tables(tag_flat[:, 3], img_side, win_side, TW)
    spare = jnp.zeros(rc.shape[:2] + (win_side - 2 * TW,), jnp.bfloat16)
    rows = jnp.concatenate([rc, rs, spare], axis=2)
    cols = jnp.concatenate([cc, cs, spare], axis=2)
    cols_b = jnp.concatenate([-cs, cc, spare], axis=2)
    return jnp.stack([rows, jnp.swapaxes(rows, 1, 2), cols, cols_b], axis=1)


def on_device(images, references, particle_class, rotation, defocus_bin, window_anchor):
    part_count = images.shape[0]
    img_side = images.shape[1]
    win_side = references.shape[2]
    per_owner = references.shape[0]
    owners = lax.axis_size("dom")
    capacity = max(2, 2 * part_count // owners)
    slot_count = owners * capacity
    target = particle_class // per_owner
    local_class = particle_class - target * per_owner
    positions = jnp.arange(part_count, dtype=jnp.int32)
    same_owner = (target[:, None] == target[None, :]) & (positions[None, :] < positions[:, None])
    slot_rank = jnp.sum(same_owner.astype(jnp.int32), axis=1)
    slot_place = target * capacity + slot_rank
    slot_tags = jnp.stack(
        [local_class + 1, defocus_bin, window_anchor[0], window_anchor[1]], axis=1
    ).astype(jnp.bfloat16)
    tag_buffer = (
        jnp.zeros((slot_count, 4), jnp.bfloat16)
        .at[slot_place]
        .set(slot_tags)
        .reshape(owners, capacity, 4)
    )
    dft_cos, dft_sin = dft_tables(img_side, win_side)
    fourier_own = transform(images, rotation, dft_cos, dft_sin)
    buffer = (
        jnp.zeros((slot_count, 2, win_side, win_side), jnp.bfloat16).at[slot_place].set(fourier_own)
    )
    buffer = buffer.reshape(owners, capacity, 2, win_side, win_side)
    ctf_bins = ctf_table(jnp.arange(16, dtype=jnp.int32), win_side)
    coeff_block = lax.all_to_all(buffer, "dom", split_axis=0, concat_axis=0, tiled=True)
    tag_block = lax.all_to_all(tag_buffer, "dom", split_axis=0, concat_axis=0, tiled=True)
    tag_flat = tag_block.reshape(slot_count, 4).astype(jnp.int32)
    pack = phase_pack(tag_flat, img_side, win_side)
    partial_value, info = slot_eval(
        tag_flat.T,
        coeff_block.reshape(slot_count, 2, win_side, win_side),
        references,
        ctf_bins,
        pack,
    )
    returned = lax.all_to_all(
        info[:, 0, :3].reshape(owners, capacity, 3), "dom", split_axis=0, concat_axis=0, tiled=True
    )
    summed = lax.psum_scatter(partial_value, "cls", scatter_dimension=2, tiled=True)
    divisor = summed[:, 2] + ridge_term
    new_refs = summed[:, :2] / divisor[:, None]
    particle_info = returned.reshape(slot_count, 3)[slot_place]
    return (new_refs, particle_info.T)


def solution(mesh):
    return jax.shard_map(
        on_device,
        mesh=mesh,
        in_specs=(
            P(("copies", "dom", "cls"), None, None),
            P(("copies", "dom"), None, None, None),
            P(("copies", "dom", "cls")),
            P(("copies", "dom", "cls")),
            P(("copies", "dom", "cls")),
            P(None, ("copies", "dom", "cls")),
        ),
        out_specs=(P(("copies", "dom"), None, "cls", None), P(None, ("copies", "dom", "cls"))),
        check_vma=False,
    )
```

```python
import math

import jax
import jax.numpy as jnp
from jax import lax
from jax.experimental import pallas as pl
from jax.experimental.pallas import tpu as pltpu
from jax.sharding import PartitionSpec as P

TW = 8


score_scale = 0.02
ridge_term = 1.0
highest = lax.Precision.HIGHEST


def freq_ids(win_side):
    return jnp.arange(win_side, dtype=jnp.int32) - win_side // 2


def dft_tables(img_side, win_side):
    phase_int = (
        freq_ids(win_side)[:, None] * jnp.arange(img_side, dtype=jnp.int32)[None, :] % img_side
    )
    angles = phase_int.astype(jnp.float32) * (2.0 * math.pi / img_side)
    scale_by = 1.0 / math.sqrt(img_side)
    return (
        (jnp.cos(angles) * scale_by).astype(jnp.bfloat16),
        (-jnp.sin(angles) * scale_by).astype(jnp.bfloat16),
    )


def shift_tables(anchor, img_side, win_side, span_len):
    shifts = anchor[:, None] + jnp.arange(span_len, dtype=jnp.int32)[None, :] - span_len // 2
    phase_int = freq_ids(win_side)[None, :, None] * shifts[:, None, :] % img_side
    angles = phase_int.astype(jnp.float32) * (2.0 * math.pi / img_side)
    return (
        jnp.cos(angles).astype(jnp.bfloat16),
        jnp.sin(angles).astype(jnp.bfloat16),
        shifts.astype(jnp.float32),
    )


def ctf_table(bin_ids, win_side):
    freqs = freq_ids(win_side).astype(jnp.float32)
    radius = (freqs[:, None] * freqs[:, None] + freqs[None, :] * freqs[None, :]) / float(
        win_side * win_side
    )
    strength = 20.0 + 6.0 * bin_ids.astype(jnp.float32)
    return -jnp.sin(strength[:, None, None] * radius[None, :, :] + 0.1)


def rotate_grid(stack_in, rot_ids):
    flag_bits = rot_ids[:, None, None]
    result = jnp.where(flag_bits & 4 != 0, jnp.swapaxes(stack_in, 1, 2), stack_in)
    result = jnp.where(flag_bits & 1 != 0, result[:, ::-1, :], result)
    return jnp.where(flag_bits & 2 != 0, result[:, :, ::-1], result)


def transform(images, rot_ids, dft_cos, dft_sin):
    win_side = dft_cos.shape[0]
    stacked = jnp.concatenate([dft_cos, dft_sin], axis=0)
    flag_bits = rot_ids[:, None, None]
    col_table = jnp.where(flag_bits & 2 != 0, stacked[None, :, ::-1], stacked[None])
    plain = jnp.einsum("nyx,nkx->nyk", images, col_table, preferred_element_type=jnp.float32)
    turned = jnp.einsum("nxy,nkx->nyk", images, col_table, preferred_element_type=jnp.float32)
    half_done = jnp.where(flag_bits & 4 != 0, turned, plain).astype(jnp.bfloat16)
    row_cos = jnp.where(flag_bits & 1 != 0, dft_cos[None, :, ::-1], dft_cos[None])
    row_sin = jnp.where(flag_bits & 1 != 0, dft_sin[None, :, ::-1], dft_sin[None])
    from_cos = jnp.einsum("njy,nyk->njk", row_cos, half_done, preferred_element_type=jnp.float32)
    from_sin = jnp.einsum("njy,nyk->njk", row_sin, half_done, preferred_element_type=jnp.float32)
    real_part = from_cos[..., :win_side] - from_sin[..., win_side:]
    imag_part = from_cos[..., win_side:] + from_sin[..., :win_side]
    return jnp.stack([real_part, imag_part], axis=1).astype(jnp.bfloat16)


def evaluate(fourier, chosen, ctf_map, row_cos, row_sin, col_cos, col_sin, row_shift, col_shift):
    span_len = col_cos.shape[2]
    coef_re = fourier[:, 0].astype(jnp.float32)
    coef_im = fourier[:, 1].astype(jnp.float32)
    pred_re = ctf_map * chosen[:, 0].astype(jnp.float32)
    pred_im = ctf_map * chosen[:, 1].astype(jnp.float32)
    prod_re = (coef_re * pred_re + coef_im * pred_im).astype(jnp.bfloat16)
    prod_im = (coef_im * pred_re - coef_re * pred_im).astype(jnp.bfloat16)
    shift_col = jnp.concatenate([col_cos, col_sin], axis=2)
    from_real = jnp.einsum("nuv,nvb->nub", prod_re, shift_col, preferred_element_type=jnp.float32)
    from_imag = jnp.einsum("nuv,nvb->nub", prod_im, shift_col, preferred_element_type=jnp.float32)
    part_re = from_real[..., :span_len] - from_imag[..., span_len:]
    part_im = from_real[..., span_len:] + from_imag[..., :span_len]
    cos_rows = row_cos.astype(jnp.float32)
    sin_rows = row_sin.astype(jnp.float32)
    cos_cols = col_cos.astype(jnp.float32)
    sin_cols = col_sin.astype(jnp.float32)
    correl = jnp.einsum("nua,nub->nab", cos_rows, part_re, precision=highest) - jnp.einsum(
        "nua,nub->nab", sin_rows, part_im, precision=highest
    )
    score = score_scale * correl.reshape(fourier.shape[0], span_len * span_len)
    peak = jnp.max(score, axis=1, keepdims=True)
    evidence = peak[:, 0] + jnp.log(jnp.sum(jnp.exp(score - peak), axis=1))
    weight = jnp.exp(score - evidence[:, None]).reshape(fourier.shape[0], span_len, span_len)
    mean_row = jnp.sum(jnp.sum(weight, axis=2) * row_shift, axis=1)
    mean_col = jnp.sum(jnp.sum(weight, axis=1) * col_shift, axis=1)
    qpart_re = jnp.einsum("nab,nvb->nav", weight, cos_cols, precision=highest)
    qpart_im = jnp.einsum("nab,nvb->nav", weight, sin_cols, precision=highest)
    rows_both = jnp.concatenate([cos_rows, sin_rows], axis=2)
    for_real = jnp.concatenate([qpart_re, -qpart_im], axis=1)
    for_imag = jnp.concatenate([qpart_im, qpart_re], axis=1)
    back_re = jnp.einsum("nua,nav->nuv", rows_both, for_real, precision=highest)
    back_im = jnp.einsum("nua,nav->nuv", rows_both, for_imag, precision=highest)
    term_re = ctf_map * (coef_re * back_re - coef_im * back_im)
    term_im = ctf_map * (coef_re * back_im + coef_im * back_re)
    class_terms = jnp.stack([term_re, term_im, ctf_map * ctf_map], axis=1)
    particle_info = jnp.stack([evidence, mean_row, mean_col], axis=1)
    return (class_terms, particle_info)


def _split3(value):
    high = value.astype(jnp.bfloat16)
    rest = value - high.astype(jnp.float32)
    middle = rest.astype(jnp.bfloat16)
    low = (rest - middle.astype(jnp.float32)).astype(jnp.bfloat16)
    return high, middle, low


def _exact_dot(lhs, rhs):
    if lhs.dtype == jnp.bfloat16:
        parts = [jnp.dot(lhs, piece, preferred_element_type=jnp.float32) for piece in _split3(rhs)]
    else:
        parts = [jnp.dot(piece, rhs, preferred_element_type=jnp.float32) for piece in _split3(lhs)]
    return parts[0] + parts[1] + parts[2]


def _slot_kernel(meta_ref, coef_ref, ref_ref, ctf_ref, pack_ref, total_ref, info_ref):
    s = pl.program_id(0)
    span = 8

    @pl.when(s == 0)
    def _():
        total_ref[...] = jnp.zeros(total_ref.shape, total_ref.dtype)

    valid = meta_ref[0, s] > 0
    info_ref[...] = jnp.zeros(info_ref.shape, info_ref.dtype)

    @pl.when(valid)
    def _():
        cls = jnp.maximum(meta_ref[0, s] - 1, 0)
        coef_re = coef_ref[0, 0].astype(jnp.float32)
        coef_im = coef_ref[0, 1].astype(jnp.float32)
        ctf = ctf_ref[0]
        pred_re = ctf * ref_ref[0, 0].astype(jnp.float32)
        pred_im = ctf * ref_ref[0, 1].astype(jnp.float32)
        prod_re = (coef_re * pred_re + coef_im * pred_im).astype(jnp.bfloat16)
        prod_im = (coef_im * pred_re - coef_re * pred_im).astype(jnp.bfloat16)
        rows = pack_ref[0, 0]
        cols = pack_ref[0, 1]
        cols_b = pack_ref[0, 2]
        flat = pack_ref[0, 3]
        both = jnp.concatenate([prod_re, prod_im], axis=1)
        mix = jnp.concatenate([cols, cols_b], axis=0)
        part = jnp.dot(both, mix, preferred_element_type=jnp.float32)
        corr = _exact_dot(flat[0:16], part)
        upper = corr[0:8]
        lower = pltpu.roll(corr[8:16], 128 - span, 1)
        lane = lax.broadcasted_iota(jnp.int32, (8, 128), 1)
        sub = lax.broadcasted_iota(jnp.int32, (8, 128), 0)
        inside = lane < span
        score = jnp.where(inside, score_scale * (upper - lower), -jnp.inf)
        peak = jnp.max(jnp.max(score, axis=1, keepdims=True), axis=0, keepdims=True)
        total = jnp.sum(jnp.sum(jnp.exp(score - peak), axis=1, keepdims=True), axis=0, keepdims=True)
        evidence = peak + jnp.log(total)
        weight = jnp.where(inside, jnp.exp(score - evidence), 0.0)
        row_shift = (jnp.full((8, 128), meta_ref[2, s], jnp.int32) + sub - span // 2).astype(jnp.float32)
        col_shift = (jnp.full((8, 128), meta_ref[3, s], jnp.int32) + lane - span // 2).astype(jnp.float32)
        by_row = jnp.sum(weight, axis=1, keepdims=True)
        mean_row = jnp.sum(by_row * row_shift[:, 0:1], axis=0, keepdims=True)
        by_col = jnp.sum(weight, axis=0, keepdims=True)
        mean_col = jnp.sum(jnp.where(inside[0:1], by_col * col_shift[0:1], 0.0), axis=1, keepdims=True)
        info_ref[0] = jnp.where(
            sub == 0,
            jnp.where(lane == 0, evidence, jnp.where(lane == 1, mean_row, jnp.where(lane == 2, mean_col, 0.0))),
            0.0,
        )
        shifted = pltpu.roll(weight, span, 1)
        stacked_w = jnp.concatenate([weight, shifted], axis=0)
        pad = jnp.zeros((112, 128), jnp.bfloat16)
        col_rows = jnp.concatenate([flat[16:32], pad], axis=0)
        qpart = _exact_dot(stacked_w, col_rows)
        q_re = qpart[0:8]
        q_im = qpart[8:16]
        zeros = jnp.zeros((112, 128), jnp.float32)
        for_re = jnp.concatenate([q_re, -q_im, zeros], axis=0)
        for_im = jnp.concatenate([q_im, q_re, zeros], axis=0)
        back_re = _exact_dot(rows, for_re)
        back_im = _exact_dot(rows, for_im)
        term_re = ctf * (coef_re * back_re - coef_im * back_im)
        term_im = ctf * (coef_re * back_im + coef_im * back_re)
        total_ref[cls, 0] = total_ref[cls, 0] + term_re
        total_ref[cls, 1] = total_ref[cls, 1] + term_im
        total_ref[cls, 2] = total_ref[cls, 2] + ctf * ctf


def slot_eval(meta, coef, refs, ctf_tab, pack, interpret=False):
    slots = coef.shape[0]
    per_owner = refs.shape[0]
    win = coef.shape[2]
    bins = ctf_tab.shape[0]

    def coef_map(s, meta):
        return (s, 0, 0, 0)

    def ref_map(s, meta):
        return (jnp.clip(meta[0, s] - 1, 0, per_owner - 1), 0, 0, 0)

    def ctf_map(s, meta):
        return (jnp.clip(meta[1, s], 0, bins - 1), 0, 0)

    grid_spec = pltpu.PrefetchScalarGridSpec(
        num_scalar_prefetch=1,
        grid=(slots,),
        in_specs=[
            pl.BlockSpec((1, 2, win, win), coef_map),
            pl.BlockSpec((1, 2, win, win), ref_map),
            pl.BlockSpec((1, win, win), ctf_map),
            pl.BlockSpec((1, 4, win, win), coef_map),
        ],
        out_specs=[
            pl.BlockSpec((per_owner, 3, win, win), lambda s, meta: (0, 0, 0, 0)),
            pl.BlockSpec((1, 8, 128), lambda s, meta: (s, 0, 0)),
        ],
    )
    return pl.pallas_call(
        _slot_kernel,
        grid_spec=grid_spec,
        out_shape=[
            jax.ShapeDtypeStruct((per_owner, 3, win, win), jnp.float32),
            jax.ShapeDtypeStruct((slots, 8, 128), jnp.float32),
        ],
        compiler_params=pltpu.CompilerParams(dimension_semantics=("arbitrary",)),
        interpret=interpret,
    )(meta, coef, refs, ctf_tab, pack)


def phase_rows(anchor, img_side, win_side):
    shifts = anchor[:, None] + jnp.arange(TW, dtype=jnp.int32)[None, :] - TW // 2
    phase_int = shifts[:, :, None] * freq_ids(win_side)[None, None, :] % img_side
    angles = phase_int.astype(jnp.float32) * (2.0 * math.pi / img_side)
    return jnp.concatenate(
        [jnp.cos(angles).astype(jnp.bfloat16), jnp.sin(angles).astype(jnp.bfloat16)], axis=1
    )


def phase_pack(tag_flat, img_side, win_side):
    rows_t = phase_rows(tag_flat[:, 2], img_side, win_side)
    cols_t = phase_rows(tag_flat[:, 3], img_side, win_side)
    cols_bt = jnp.concatenate([-cols_t[:, TW:], cols_t[:, :TW]], axis=1)
    spare = jnp.zeros((rows_t.shape[0], win_side - 4 * TW, win_side), jnp.bfloat16)
    flat = jnp.concatenate([rows_t, cols_t, spare], axis=1)
    planes = [
        jnp.pad(jnp.swapaxes(t, 1, 2), ((0, 0), (0, 0), (0, win_side - 2 * TW)))
        for t in (rows_t, cols_t, cols_bt)
    ]
    return jnp.stack(planes + [flat], axis=1)


def on_device(images, references, particle_class, rotation, defocus_bin, window_anchor):
    part_count = images.shape[0]
    img_side = images.shape[1]
    win_side = references.shape[2]
    per_owner = references.shape[0]
    owners = lax.axis_size("dom")
    capacity = max(2, 2 * part_count // owners)
    slot_count = owners * capacity
    target = particle_class // per_owner
    local_class = particle_class - target * per_owner
    positions = jnp.arange(part_count, dtype=jnp.int32)
    same_owner = (target[:, None] == target[None, :]) & (positions[None, :] < positions[:, None])
    slot_rank = jnp.sum(same_owner.astype(jnp.int32), axis=1)
    slot_place = target * capacity + slot_rank
    slot_tags = jnp.stack(
        [local_class + 1, defocus_bin, window_anchor[0], window_anchor[1]], axis=1
    ).astype(jnp.bfloat16)
    tag_buffer = (
        jnp.zeros((slot_count, 4), jnp.bfloat16)
        .at[slot_place]
        .set(slot_tags)
        .reshape(owners, capacity, 4)
    )
    dft_cos, dft_sin = dft_tables(img_side, win_side)
    fourier_own = transform(images, rotation, dft_cos, dft_sin)
    buffer = (
        jnp.zeros((slot_count, 2, win_side, win_side), jnp.bfloat16).at[slot_place].set(fourier_own)
    )
    buffer = buffer.reshape(owners, capacity, 2, win_side, win_side)
    ctf_bins = ctf_table(jnp.arange(16, dtype=jnp.int32), win_side)
    coeff_block = lax.all_to_all(buffer, "dom", split_axis=0, concat_axis=0, tiled=True)
    tag_block = lax.all_to_all(tag_buffer, "dom", split_axis=0, concat_axis=0, tiled=True)
    tag_flat = tag_block.reshape(slot_count, 4).astype(jnp.int32)
    pack = phase_pack(tag_flat, img_side, win_side)
    partial_value, info = slot_eval(
        tag_flat.T,
        coeff_block.reshape(slot_count, 2, win_side, win_side),
        references,
        ctf_bins,
        pack,
    )
    returned = lax.all_to_all(
        info[:, 0, :3].reshape(owners, capacity, 3), "dom", split_axis=0, concat_axis=0, tiled=True
    )
    summed = lax.psum_scatter(partial_value, "cls", scatter_dimension=2, tiled=True)
    divisor = summed[:, 2] + ridge_term
    new_refs = summed[:, :2] / divisor[:, None]
    particle_info = returned.reshape(slot_count, 3)[slot_place]
    return (new_refs, particle_info.T)


def solution(mesh):
    return jax.shard_map(
        on_device,
        mesh=mesh,
        in_specs=(
            P(("copies", "dom", "cls"), None, None),
            P(("copies", "dom"), None, None, None),
            P(("copies", "dom", "cls")),
            P(("copies", "dom", "cls")),
            P(("copies", "dom", "cls")),
            P(None, ("copies", "dom", "cls")),
        ),
        out_specs=(P(("copies", "dom"), None, "cls", None), P(None, ("copies", "dom", "cls"))),
        check_vma=False,
    )
```

```python
import math

import jax
import jax.numpy as jnp
from jax import lax
from jax.experimental import pallas as pl
from jax.experimental.pallas import tpu as pltpu
from jax.sharding import PartitionSpec as P

TW = 8


score_scale = 0.02
ridge_term = 1.0
highest = lax.Precision.HIGHEST


def freq_ids(win_side):
    return jnp.arange(win_side, dtype=jnp.int32) - win_side // 2


def dft_tables(img_side, win_side):
    phase_int = (
        freq_ids(win_side)[:, None] * jnp.arange(img_side, dtype=jnp.int32)[None, :] % img_side
    )
    angles = phase_int.astype(jnp.float32) * (2.0 * math.pi / img_side)
    scale_by = 1.0 / math.sqrt(img_side)
    return (
        (jnp.cos(angles) * scale_by).astype(jnp.bfloat16),
        (-jnp.sin(angles) * scale_by).astype(jnp.bfloat16),
    )


def shift_tables(anchor, img_side, win_side, span_len):
    shifts = anchor[:, None] + jnp.arange(span_len, dtype=jnp.int32)[None, :] - span_len // 2
    phase_int = freq_ids(win_side)[None, :, None] * shifts[:, None, :] % img_side
    angles = phase_int.astype(jnp.float32) * (2.0 * math.pi / img_side)
    return (
        jnp.cos(angles).astype(jnp.bfloat16),
        jnp.sin(angles).astype(jnp.bfloat16),
        shifts.astype(jnp.float32),
    )


def ctf_table(bin_ids, win_side):
    freqs = freq_ids(win_side).astype(jnp.float32)
    radius = (freqs[:, None] * freqs[:, None] + freqs[None, :] * freqs[None, :]) / float(
        win_side * win_side
    )
    strength = 20.0 + 6.0 * bin_ids.astype(jnp.float32)
    return -jnp.sin(strength[:, None, None] * radius[None, :, :] + 0.1)


def rotate_grid(stack_in, rot_ids):
    flag_bits = rot_ids[:, None, None]
    result = jnp.where(flag_bits & 4 != 0, jnp.swapaxes(stack_in, 1, 2), stack_in)
    result = jnp.where(flag_bits & 1 != 0, result[:, ::-1, :], result)
    return jnp.where(flag_bits & 2 != 0, result[:, :, ::-1], result)


def transform(images, rot_ids, dft_cos, dft_sin):
    win_side = dft_cos.shape[0]
    stacked = jnp.concatenate([dft_cos, dft_sin], axis=0)
    flag_bits = rot_ids[:, None, None]
    col_table = jnp.where(flag_bits & 2 != 0, stacked[None, :, ::-1], stacked[None])
    plain = jnp.einsum("nyx,nkx->nyk", images, col_table, preferred_element_type=jnp.float32)
    turned = jnp.einsum("nxy,nkx->nyk", images, col_table, preferred_element_type=jnp.float32)
    half_done = jnp.where(flag_bits & 4 != 0, turned, plain).astype(jnp.bfloat16)
    row_cos = jnp.where(flag_bits & 1 != 0, dft_cos[None, :, ::-1], dft_cos[None])
    row_sin = jnp.where(flag_bits & 1 != 0, dft_sin[None, :, ::-1], dft_sin[None])
    from_cos = jnp.einsum("njy,nyk->njk", row_cos, half_done, preferred_element_type=jnp.float32)
    from_sin = jnp.einsum("njy,nyk->njk", row_sin, half_done, preferred_element_type=jnp.float32)
    real_part = from_cos[..., :win_side] - from_sin[..., win_side:]
    imag_part = from_cos[..., win_side:] + from_sin[..., :win_side]
    return jnp.stack([real_part, imag_part], axis=1).astype(jnp.bfloat16)


def evaluate(fourier, chosen, ctf_map, row_cos, row_sin, col_cos, col_sin, row_shift, col_shift):
    span_len = col_cos.shape[2]
    coef_re = fourier[:, 0].astype(jnp.float32)
    coef_im = fourier[:, 1].astype(jnp.float32)
    pred_re = ctf_map * chosen[:, 0].astype(jnp.float32)
    pred_im = ctf_map * chosen[:, 1].astype(jnp.float32)
    prod_re = (coef_re * pred_re + coef_im * pred_im).astype(jnp.bfloat16)
    prod_im = (coef_im * pred_re - coef_re * pred_im).astype(jnp.bfloat16)
    shift_col = jnp.concatenate([col_cos, col_sin], axis=2)
    from_real = jnp.einsum("nuv,nvb->nub", prod_re, shift_col, preferred_element_type=jnp.float32)
    from_imag = jnp.einsum("nuv,nvb->nub", prod_im, shift_col, preferred_element_type=jnp.float32)
    part_re = from_real[..., :span_len] - from_imag[..., span_len:]
    part_im = from_real[..., span_len:] + from_imag[..., :span_len]
    cos_rows = row_cos.astype(jnp.float32)
    sin_rows = row_sin.astype(jnp.float32)
    cos_cols = col_cos.astype(jnp.float32)
    sin_cols = col_sin.astype(jnp.float32)
    correl = jnp.einsum("nua,nub->nab", cos_rows, part_re, precision=highest) - jnp.einsum(
        "nua,nub->nab", sin_rows, part_im, precision=highest
    )
    score = score_scale * correl.reshape(fourier.shape[0], span_len * span_len)
    peak = jnp.max(score, axis=1, keepdims=True)
    evidence = peak[:, 0] + jnp.log(jnp.sum(jnp.exp(score - peak), axis=1))
    weight = jnp.exp(score - evidence[:, None]).reshape(fourier.shape[0], span_len, span_len)
    mean_row = jnp.sum(jnp.sum(weight, axis=2) * row_shift, axis=1)
    mean_col = jnp.sum(jnp.sum(weight, axis=1) * col_shift, axis=1)
    qpart_re = jnp.einsum("nab,nvb->nav", weight, cos_cols, precision=highest)
    qpart_im = jnp.einsum("nab,nvb->nav", weight, sin_cols, precision=highest)
    rows_both = jnp.concatenate([cos_rows, sin_rows], axis=2)
    for_real = jnp.concatenate([qpart_re, -qpart_im], axis=1)
    for_imag = jnp.concatenate([qpart_im, qpart_re], axis=1)
    back_re = jnp.einsum("nua,nav->nuv", rows_both, for_real, precision=highest)
    back_im = jnp.einsum("nua,nav->nuv", rows_both, for_imag, precision=highest)
    term_re = ctf_map * (coef_re * back_re - coef_im * back_im)
    term_im = ctf_map * (coef_re * back_im + coef_im * back_re)
    class_terms = jnp.stack([term_re, term_im, ctf_map * ctf_map], axis=1)
    particle_info = jnp.stack([evidence, mean_row, mean_col], axis=1)
    return (class_terms, particle_info)


def _split3(value):
    high = value.astype(jnp.bfloat16)
    rest = value - high.astype(jnp.float32)
    middle = rest.astype(jnp.bfloat16)
    low = (rest - middle.astype(jnp.float32)).astype(jnp.bfloat16)
    return high, middle, low


def _exact_dot(lhs, rhs):
    if lhs.dtype == jnp.bfloat16:
        parts = [jnp.dot(lhs, piece, preferred_element_type=jnp.float32) for piece in _split3(rhs)]
    else:
        parts = [jnp.dot(piece, rhs, preferred_element_type=jnp.float32) for piece in _split3(lhs)]
    return parts[0] + parts[1] + parts[2]


def _one_slot(meta_ref, slot, coef_ref, ref_ref, ctf_ref, pack_ref, j, total_ref, info_ref):
    span = 8
    per_owner = ref_ref.shape[0]
    bins = ctf_ref.shape[0]
    tag = meta_ref[0, slot]
    cls = jnp.minimum(jnp.maximum(tag - 1, 0), per_owner - 1)
    bin_id = jnp.minimum(jnp.maximum(meta_ref[1, slot], 0), bins - 1)
    keep = (jnp.full((1, 128), tag, jnp.int32) > 0).astype(jnp.float32)
    coef_re = coef_ref[0, 0].astype(jnp.float32)
    coef_im = coef_ref[0, 1].astype(jnp.float32)
    ctf = ctf_ref[bin_id]
    pred_re = ctf * ref_ref[cls, 0].astype(jnp.float32)
    pred_im = ctf * ref_ref[cls, 1].astype(jnp.float32)
    prod_re = (coef_re * pred_re + coef_im * pred_im).astype(jnp.bfloat16)
    prod_im = (coef_im * pred_re - coef_re * pred_im).astype(jnp.bfloat16)
    rows = pack_ref[j, 0]
    cols = pack_ref[j, 1]
    cols_b = pack_ref[j, 2]
    flat = pack_ref[j, 3]
    both = jnp.concatenate([prod_re, prod_im], axis=1)
    mix = jnp.concatenate([cols, cols_b], axis=0)
    part = jnp.dot(both, mix, preferred_element_type=jnp.float32)
    corr = _exact_dot(flat[0:16], part)
    upper = corr[0:8]
    lower = pltpu.roll(corr[8:16], 128 - span, 1)
    lane = lax.broadcasted_iota(jnp.int32, (8, 128), 1)
    sub = lax.broadcasted_iota(jnp.int32, (8, 128), 0)
    inside = lane < span
    score = jnp.where(inside, score_scale * (upper - lower), -jnp.inf)
    peak = jnp.max(jnp.max(score, axis=1, keepdims=True), axis=0, keepdims=True)
    total = jnp.sum(jnp.sum(jnp.exp(score - peak), axis=1, keepdims=True), axis=0, keepdims=True)
    evidence = peak + jnp.log(total)
    weight = jnp.where(inside, jnp.exp(score - evidence), 0.0)
    row_shift = (jnp.full((8, 128), meta_ref[2, slot], jnp.int32) + sub - span // 2).astype(jnp.float32)
    col_shift = (jnp.full((8, 128), meta_ref[3, slot], jnp.int32) + lane - span // 2).astype(jnp.float32)
    by_row = jnp.sum(weight, axis=1, keepdims=True)
    mean_row = jnp.sum(by_row * row_shift[:, 0:1], axis=0, keepdims=True)
    by_col = jnp.sum(weight, axis=0, keepdims=True)
    mean_col = jnp.sum(jnp.where(inside[0:1], by_col * col_shift[0:1], 0.0), axis=1, keepdims=True)
    info_ref[j] = jnp.where(
        sub == 0,
        jnp.where(lane == 0, evidence, jnp.where(lane == 1, mean_row, jnp.where(lane == 2, mean_col, 0.0))),
        0.0,
    )
    shifted = pltpu.roll(weight, span, 1)
    stacked_w = jnp.concatenate([weight, shifted], axis=0)
    pad = jnp.zeros((112, 128), jnp.bfloat16)
    col_rows = jnp.concatenate([flat[16:32], pad], axis=0)
    qpart = _exact_dot(stacked_w, col_rows)
    q_re = qpart[0:8]
    q_im = qpart[8:16]
    zeros = jnp.zeros((112, 128), jnp.float32)
    for_re = jnp.concatenate([q_re, -q_im, zeros], axis=0)
    for_im = jnp.concatenate([q_im, q_re, zeros], axis=0)
    back_re = _exact_dot(rows, for_re)
    back_im = _exact_dot(rows, for_im)
    term_re = ctf * (coef_re * back_re - coef_im * back_im)
    term_im = ctf * (coef_re * back_im + coef_im * back_re)
    total_ref[cls, 0] = total_ref[cls, 0] + term_re * keep
    total_ref[cls, 1] = total_ref[cls, 1] + term_im * keep
    total_ref[cls, 2] = total_ref[cls, 2] + ctf * ctf * keep


def _group_kernel(meta_ref, *refs):
    group = len(refs) - 5
    coef_refs = refs[:group]
    ref_ref, ctf_ref, pack_ref, total_ref, info_ref = refs[group:]
    g = pl.program_id(0)

    @pl.when(g == 0)
    def _():
        total_ref[...] = jnp.zeros(total_ref.shape, total_ref.dtype)

    info_ref[...] = jnp.zeros(info_ref.shape, info_ref.dtype)

    @pl.when(g * group < meta_ref[4, 0])
    def _():
        for j in range(group):
            _one_slot(
                meta_ref, g * group + j, coef_refs[j], ref_ref, ctf_ref, pack_ref, j,
                total_ref, info_ref,
            )


def group_eval(meta, order, coef, refs, ctf_tab, pack, group, interpret=False):
    slots = coef.shape[0]
    per_owner = refs.shape[0]
    win = coef.shape[2]
    bins = ctf_tab.shape[0]
    table = jnp.concatenate([meta, order[None]], axis=0)

    def coef_map(j):
        return lambda g, table: (table[5, g * group + j], 0, 0, 0)

    grid_spec = pltpu.PrefetchScalarGridSpec(
        num_scalar_prefetch=1,
        grid=(slots // group,),
        in_specs=[pl.BlockSpec((1, 2, win, win), coef_map(j)) for j in range(group)]
        + [
            pl.BlockSpec((per_owner, 2, win, win), lambda g, table: (0, 0, 0, 0)),
            pl.BlockSpec((bins, win, win), lambda g, table: (0, 0, 0)),
            pl.BlockSpec((group, 4, win, win), lambda g, table: (g, 0, 0, 0)),
        ],
        out_specs=[
            pl.BlockSpec((per_owner, 3, win, win), lambda g, table: (0, 0, 0, 0)),
            pl.BlockSpec((group, 8, 128), lambda g, table: (g, 0, 0)),
        ],
    )
    return pl.pallas_call(
        _group_kernel,
        grid_spec=grid_spec,
        out_shape=[
            jax.ShapeDtypeStruct((per_owner, 3, win, win), jnp.float32),
            jax.ShapeDtypeStruct((slots, 8, 128), jnp.float32),
        ],
        compiler_params=pltpu.CompilerParams(dimension_semantics=("arbitrary",)),
        interpret=interpret,
    )(table, *([coef] * group), refs, ctf_tab, pack)


def phase_rows(anchor, img_side, win_side):
    shifts = anchor[:, None] + jnp.arange(TW, dtype=jnp.int32)[None, :] - TW // 2
    phase_int = shifts[:, :, None] * freq_ids(win_side)[None, None, :] % img_side
    angles = phase_int.astype(jnp.float32) * (2.0 * math.pi / img_side)
    return jnp.concatenate(
        [jnp.cos(angles).astype(jnp.bfloat16), jnp.sin(angles).astype(jnp.bfloat16)], axis=1
    )


def phase_pack(tag_flat, img_side, win_side):
    rows_t = phase_rows(tag_flat[:, 2], img_side, win_side)
    cols_t = phase_rows(tag_flat[:, 3], img_side, win_side)
    cols_bt = jnp.concatenate([-cols_t[:, TW:], cols_t[:, :TW]], axis=1)
    spare = jnp.zeros((rows_t.shape[0], win_side - 4 * TW, win_side), jnp.bfloat16)
    flat = jnp.concatenate([rows_t, cols_t, spare], axis=1)
    planes = [
        jnp.pad(jnp.swapaxes(t, 1, 2), ((0, 0), (0, 0), (0, win_side - 2 * TW)))
        for t in (rows_t, cols_t, cols_bt)
    ]
    return jnp.stack(planes + [flat], axis=1)


def on_device(images, references, particle_class, rotation, defocus_bin, window_anchor):
    part_count = images.shape[0]
    img_side = images.shape[1]
    win_side = references.shape[2]
    per_owner = references.shape[0]
    owners = lax.axis_size("dom")
    capacity = max(2, 2 * part_count // owners)
    slot_count = owners * capacity
    target = particle_class // per_owner
    local_class = particle_class - target * per_owner
    positions = jnp.arange(part_count, dtype=jnp.int32)
    same_owner = (target[:, None] == target[None, :]) & (positions[None, :] < positions[:, None])
    slot_rank = jnp.sum(same_owner.astype(jnp.int32), axis=1)
    slot_place = target * capacity + slot_rank
    slot_tags = jnp.stack(
        [local_class + 1, defocus_bin, window_anchor[0], window_anchor[1]], axis=1
    ).astype(jnp.bfloat16)
    tag_buffer = (
        jnp.zeros((slot_count, 4), jnp.bfloat16)
        .at[slot_place]
        .set(slot_tags)
        .reshape(owners, capacity, 4)
    )
    dft_cos, dft_sin = dft_tables(img_side, win_side)
    fourier_own = transform(images, rotation, dft_cos, dft_sin)
    buffer = (
        jnp.zeros((slot_count, 2, win_side, win_side), jnp.bfloat16).at[slot_place].set(fourier_own)
    )
    buffer = buffer.reshape(owners, capacity, 2, win_side, win_side)
    ctf_bins = ctf_table(jnp.arange(16, dtype=jnp.int32), win_side)
    coeff_block = lax.all_to_all(buffer, "dom", split_axis=0, concat_axis=0, tiled=True)
    tag_block = lax.all_to_all(tag_buffer, "dom", split_axis=0, concat_axis=0, tiled=True)
    tag_flat = tag_block.reshape(slot_count, 4).astype(jnp.int32)
    live = (tag_flat[:, 0] > 0).astype(jnp.int32)
    order = jnp.argsort(1 - live, stable=True).astype(jnp.int32)
    tag_sorted = tag_flat[order]
    count = jnp.sum(live)
    meta = jnp.concatenate(
        [tag_sorted.T, jnp.full((1, slot_count), count, jnp.int32)], axis=0
    )
    pack = phase_pack(tag_sorted, img_side, win_side)
    group = 4 if slot_count % 4 == 0 else 1
    partial_value, info_sorted = group_eval(
        meta,
        order,
        coeff_block.reshape(slot_count, 2, win_side, win_side),
        references,
        ctf_bins,
        pack,
        group,
    )
    info = jnp.zeros((slot_count, 3), jnp.float32).at[order].set(info_sorted[:, 0, :3])
    returned = lax.all_to_all(
        info.reshape(owners, capacity, 3), "dom", split_axis=0, concat_axis=0, tiled=True
    )
    summed = lax.psum_scatter(partial_value, "cls", scatter_dimension=2, tiled=True)
    divisor = summed[:, 2] + ridge_term
    new_refs = summed[:, :2] / divisor[:, None]
    particle_info = returned.reshape(slot_count, 3)[slot_place]
    return (new_refs, particle_info.T)


def solution(mesh):
    return jax.shard_map(
        on_device,
        mesh=mesh,
        in_specs=(
            P(("copies", "dom", "cls"), None, None),
            P(("copies", "dom"), None, None, None),
            P(("copies", "dom", "cls")),
            P(("copies", "dom", "cls")),
            P(("copies", "dom", "cls")),
            P(None, ("copies", "dom", "cls")),
        ),
        out_specs=(P(("copies", "dom"), None, "cls", None), P(None, ("copies", "dom", "cls"))),
        check_vma=False,
    )
```

```python
import math

import jax
import jax.numpy as jnp
from jax import lax
from jax.experimental import pallas as pl
from jax.experimental.pallas import tpu as pltpu
from jax.sharding import PartitionSpec as P

TW = 8


score_scale = 0.02
ridge_term = 1.0
highest = lax.Precision.HIGHEST


def freq_ids(win_side):
    return jnp.arange(win_side, dtype=jnp.int32) - win_side // 2


def dft_tables(img_side, win_side):
    phase_int = (
        freq_ids(win_side)[:, None] * jnp.arange(img_side, dtype=jnp.int32)[None, :] % img_side
    )
    angles = phase_int.astype(jnp.float32) * (2.0 * math.pi / img_side)
    scale_by = 1.0 / math.sqrt(img_side)
    return (
        (jnp.cos(angles) * scale_by).astype(jnp.bfloat16),
        (-jnp.sin(angles) * scale_by).astype(jnp.bfloat16),
    )


def shift_tables(anchor, img_side, win_side, span_len):
    shifts = anchor[:, None] + jnp.arange(span_len, dtype=jnp.int32)[None, :] - span_len // 2
    phase_int = freq_ids(win_side)[None, :, None] * shifts[:, None, :] % img_side
    angles = phase_int.astype(jnp.float32) * (2.0 * math.pi / img_side)
    return (
        jnp.cos(angles).astype(jnp.bfloat16),
        jnp.sin(angles).astype(jnp.bfloat16),
        shifts.astype(jnp.float32),
    )


def ctf_table(bin_ids, win_side):
    freqs = freq_ids(win_side).astype(jnp.float32)
    radius = (freqs[:, None] * freqs[:, None] + freqs[None, :] * freqs[None, :]) / float(
        win_side * win_side
    )
    strength = 20.0 + 6.0 * bin_ids.astype(jnp.float32)
    return -jnp.sin(strength[:, None, None] * radius[None, :, :] + 0.1)


def rotate_grid(stack_in, rot_ids):
    flag_bits = rot_ids[:, None, None]
    result = jnp.where(flag_bits & 4 != 0, jnp.swapaxes(stack_in, 1, 2), stack_in)
    result = jnp.where(flag_bits & 1 != 0, result[:, ::-1, :], result)
    return jnp.where(flag_bits & 2 != 0, result[:, :, ::-1], result)


def transform(images, rot_ids, dft_cos, dft_sin):
    win_side = dft_cos.shape[0]
    stacked = jnp.concatenate([dft_cos, dft_sin], axis=0)
    flag_bits = rot_ids[:, None, None]
    col_table = jnp.where(flag_bits & 2 != 0, stacked[None, :, ::-1], stacked[None])
    plain = jnp.einsum("nyx,nkx->nyk", images, col_table, preferred_element_type=jnp.float32)
    turned = jnp.einsum("nxy,nkx->nyk", images, col_table, preferred_element_type=jnp.float32)
    half_done = jnp.where(flag_bits & 4 != 0, turned, plain).astype(jnp.bfloat16)
    row_cos = jnp.where(flag_bits & 1 != 0, dft_cos[None, :, ::-1], dft_cos[None])
    row_sin = jnp.where(flag_bits & 1 != 0, dft_sin[None, :, ::-1], dft_sin[None])
    from_cos = jnp.einsum("njy,nyk->njk", row_cos, half_done, preferred_element_type=jnp.float32)
    from_sin = jnp.einsum("njy,nyk->njk", row_sin, half_done, preferred_element_type=jnp.float32)
    real_part = from_cos[..., :win_side] - from_sin[..., win_side:]
    imag_part = from_cos[..., win_side:] + from_sin[..., :win_side]
    return jnp.stack([real_part, imag_part], axis=1).astype(jnp.bfloat16)


def evaluate(fourier, chosen, ctf_map, row_cos, row_sin, col_cos, col_sin, row_shift, col_shift):
    span_len = col_cos.shape[2]
    coef_re = fourier[:, 0].astype(jnp.float32)
    coef_im = fourier[:, 1].astype(jnp.float32)
    pred_re = ctf_map * chosen[:, 0].astype(jnp.float32)
    pred_im = ctf_map * chosen[:, 1].astype(jnp.float32)
    prod_re = (coef_re * pred_re + coef_im * pred_im).astype(jnp.bfloat16)
    prod_im = (coef_im * pred_re - coef_re * pred_im).astype(jnp.bfloat16)
    shift_col = jnp.concatenate([col_cos, col_sin], axis=2)
    from_real = jnp.einsum("nuv,nvb->nub", prod_re, shift_col, preferred_element_type=jnp.float32)
    from_imag = jnp.einsum("nuv,nvb->nub", prod_im, shift_col, preferred_element_type=jnp.float32)
    part_re = from_real[..., :span_len] - from_imag[..., span_len:]
    part_im = from_real[..., span_len:] + from_imag[..., :span_len]
    cos_rows = row_cos.astype(jnp.float32)
    sin_rows = row_sin.astype(jnp.float32)
    cos_cols = col_cos.astype(jnp.float32)
    sin_cols = col_sin.astype(jnp.float32)
    correl = jnp.einsum("nua,nub->nab", cos_rows, part_re, precision=highest) - jnp.einsum(
        "nua,nub->nab", sin_rows, part_im, precision=highest
    )
    score = score_scale * correl.reshape(fourier.shape[0], span_len * span_len)
    peak = jnp.max(score, axis=1, keepdims=True)
    evidence = peak[:, 0] + jnp.log(jnp.sum(jnp.exp(score - peak), axis=1))
    weight = jnp.exp(score - evidence[:, None]).reshape(fourier.shape[0], span_len, span_len)
    mean_row = jnp.sum(jnp.sum(weight, axis=2) * row_shift, axis=1)
    mean_col = jnp.sum(jnp.sum(weight, axis=1) * col_shift, axis=1)
    qpart_re = jnp.einsum("nab,nvb->nav", weight, cos_cols, precision=highest)
    qpart_im = jnp.einsum("nab,nvb->nav", weight, sin_cols, precision=highest)
    rows_both = jnp.concatenate([cos_rows, sin_rows], axis=2)
    for_real = jnp.concatenate([qpart_re, -qpart_im], axis=1)
    for_imag = jnp.concatenate([qpart_im, qpart_re], axis=1)
    back_re = jnp.einsum("nua,nav->nuv", rows_both, for_real, precision=highest)
    back_im = jnp.einsum("nua,nav->nuv", rows_both, for_imag, precision=highest)
    term_re = ctf_map * (coef_re * back_re - coef_im * back_im)
    term_im = ctf_map * (coef_re * back_im + coef_im * back_re)
    class_terms = jnp.stack([term_re, term_im, ctf_map * ctf_map], axis=1)
    particle_info = jnp.stack([evidence, mean_row, mean_col], axis=1)
    return (class_terms, particle_info)


def _split3(value):
    high = value.astype(jnp.bfloat16)
    rest = value - high.astype(jnp.float32)
    middle = rest.astype(jnp.bfloat16)
    low = (rest - middle.astype(jnp.float32)).astype(jnp.bfloat16)
    return high, middle, low


def _exact_dot(lhs, rhs):
    if lhs.dtype == jnp.bfloat16:
        parts = [jnp.dot(lhs, piece, preferred_element_type=jnp.float32) for piece in _split3(rhs)]
    else:
        parts = [jnp.dot(piece, rhs, preferred_element_type=jnp.float32) for piece in _split3(lhs)]
    return parts[0] + parts[1] + parts[2]


def _group_kernel(meta_ref, *refs):
    group = len(refs) - 5
    coef_refs = refs[:group]
    ref_ref, ctf_ref, pack_ref, total_ref, info_ref = refs[group:]
    g = pl.program_id(0)
    span = 8
    per_owner = ref_ref.shape[0]
    bins = ctf_ref.shape[0]

    @pl.when(g == 0)
    def _():
        total_ref[...] = jnp.zeros(total_ref.shape, total_ref.dtype)

    info_ref[...] = jnp.zeros(info_ref.shape, info_ref.dtype)

    @pl.when(g * group < meta_ref[4, 0])
    def _():
        lane = lax.broadcasted_iota(jnp.int32, (8, 128), 1)
        sub = lax.broadcasted_iota(jnp.int32, (8, 128), 0)
        inside = lane < span
        st = []
        for j in range(group):
            slot = g * group + j
            tag = meta_ref[0, slot]
            cls = jnp.minimum(jnp.maximum(tag - 1, 0), per_owner - 1)
            bin_id = jnp.minimum(jnp.maximum(meta_ref[1, slot], 0), bins - 1)
            keep = (jnp.full((1, 128), tag, jnp.int32) > 0).astype(jnp.float32)
            coef_re = coef_refs[j][0, 0].astype(jnp.float32)
            coef_im = coef_refs[j][0, 1].astype(jnp.float32)
            ctf = ctf_ref[bin_id]
            pred_re = ctf * ref_ref[cls, 0].astype(jnp.float32)
            pred_im = ctf * ref_ref[cls, 1].astype(jnp.float32)
            prod_re = (coef_re * pred_re + coef_im * pred_im).astype(jnp.bfloat16)
            prod_im = (coef_im * pred_re - coef_re * pred_im).astype(jnp.bfloat16)
            both = jnp.concatenate([prod_re, prod_im], axis=1)
            mix = jnp.concatenate([pack_ref[j, 1], pack_ref[j, 2]], axis=0)
            part = jnp.dot(both, mix, preferred_element_type=jnp.float32)
            st.append(dict(slot=slot, cls=cls, keep=keep, ctf=ctf, coef_re=coef_re, coef_im=coef_im, part=part))
        for j, d in enumerate(st):
            p_hi, p_mid, p_lo = [piece.astype(jnp.float32) for piece in _split3(d["part"])]
            packed = (p_hi + pltpu.roll(p_mid, 2 * span, 1) + pltpu.roll(p_lo, 4 * span, 1)).astype(jnp.bfloat16)
            d["corr3"] = jnp.dot(pack_ref[j, 3][0:16], packed, preferred_element_type=jnp.float32)
        for j, d in enumerate(st):
            corr3 = d["corr3"]
            corr = (corr3 + pltpu.roll(corr3, 128 - 2 * span, 1)) + pltpu.roll(corr3, 128 - 4 * span, 1)
            upper = corr[0:8]
            lower = pltpu.roll(corr[8:16], 128 - span, 1)
            score = jnp.where(inside, score_scale * (upper - lower), -jnp.inf)
            peak = jnp.max(jnp.max(score, axis=1, keepdims=True), axis=0, keepdims=True)
            total = jnp.sum(jnp.sum(jnp.exp(score - peak), axis=1, keepdims=True), axis=0, keepdims=True)
            evidence = peak + jnp.log(total)
            weight = jnp.where(inside, jnp.exp(score - evidence), 0.0)
            slot = d["slot"]
            row_shift = (jnp.full((8, 128), meta_ref[2, slot], jnp.int32) + sub - span // 2).astype(jnp.float32)
            col_shift = (jnp.full((8, 128), meta_ref[3, slot], jnp.int32) + lane - span // 2).astype(jnp.float32)
            by_row = jnp.sum(weight, axis=1, keepdims=True)
            mean_row = jnp.sum(by_row * row_shift[:, 0:1], axis=0, keepdims=True)
            by_col = jnp.sum(weight, axis=0, keepdims=True)
            mean_col = jnp.sum(jnp.where(inside[0:1], by_col * col_shift[0:1], 0.0), axis=1, keepdims=True)
            info_ref[j] = jnp.where(
                sub == 0,
                jnp.where(lane == 0, evidence, jnp.where(lane == 1, mean_row, jnp.where(lane == 2, mean_col, 0.0))),
                0.0,
            )
            shifted = pltpu.roll(weight, span, 1)
            stacked_w = jnp.concatenate([weight, shifted], axis=0)
            pad = jnp.zeros((112, 128), jnp.bfloat16)
            col_rows = jnp.concatenate([pack_ref[j, 3][16:32], pad], axis=0)
            w_pieces = jnp.concatenate(_split3(stacked_w), axis=0)
            d["q3"] = jnp.dot(w_pieces, col_rows, preferred_element_type=jnp.float32)
        for j, d in enumerate(st):
            q3 = d["q3"]
            qpart = (q3[0:16] + q3[16:32]) + q3[32:48]
            q_re = qpart[0:8]
            q_im = qpart[8:16]
            spare = jnp.zeros((80, 128), jnp.bfloat16)
            rhs_re = jnp.concatenate(list(_split3(jnp.concatenate([q_re, -q_im], axis=0))) + [spare], axis=0)
            rhs_im = jnp.concatenate(list(_split3(jnp.concatenate([q_im, q_re], axis=0))) + [spare], axis=0)
            d["back"] = jnp.dot(
                pack_ref[j, 0], jnp.concatenate([rhs_re, rhs_im], axis=1), preferred_element_type=jnp.float32
            )
        for d in st:
            back_re = d["back"][:, 0:128]
            back_im = d["back"][:, 128:256]
            ctf, coef_re, coef_im, keep, cls = d["ctf"], d["coef_re"], d["coef_im"], d["keep"], d["cls"]
            term_re = ctf * (coef_re * back_re - coef_im * back_im)
            term_im = ctf * (coef_re * back_im + coef_im * back_re)
            total_ref[cls, 0] = total_ref[cls, 0] + term_re * keep
            total_ref[cls, 1] = total_ref[cls, 1] + term_im * keep
            total_ref[cls, 2] = total_ref[cls, 2] + ctf * ctf * keep


def group_eval(meta, order, coef, refs, ctf_tab, pack, group, interpret=False):
    slots = coef.shape[0]
    per_owner = refs.shape[0]
    win = coef.shape[2]
    bins = ctf_tab.shape[0]
    table = jnp.concatenate([meta, order[None]], axis=0)

    def coef_map(j):
        return lambda g, table: (table[5, g * group + j], 0, 0, 0)

    grid_spec = pltpu.PrefetchScalarGridSpec(
        num_scalar_prefetch=1,
        grid=(slots // group,),
        in_specs=[pl.BlockSpec((1, 2, win, win), coef_map(j)) for j in range(group)]
        + [
            pl.BlockSpec((per_owner, 2, win, win), lambda g, table: (0, 0, 0, 0)),
            pl.BlockSpec((bins, win, win), lambda g, table: (0, 0, 0)),
            pl.BlockSpec((group, 4, win, win), lambda g, table: (g, 0, 0, 0)),
        ],
        out_specs=[
            pl.BlockSpec((per_owner, 3, win, win), lambda g, table: (0, 0, 0, 0)),
            pl.BlockSpec((group, 8, 128), lambda g, table: (g, 0, 0)),
        ],
    )
    return pl.pallas_call(
        _group_kernel,
        grid_spec=grid_spec,
        out_shape=[
            jax.ShapeDtypeStruct((per_owner, 3, win, win), jnp.float32),
            jax.ShapeDtypeStruct((slots, 8, 128), jnp.float32),
        ],
        compiler_params=pltpu.CompilerParams(dimension_semantics=("arbitrary",)),
        interpret=interpret,
    )(table, *([coef] * group), refs, ctf_tab, pack)


def phase_rows(anchor, img_side, win_side):
    shifts = anchor[:, None] + jnp.arange(TW, dtype=jnp.int32)[None, :] - TW // 2
    phase_int = shifts[:, :, None] * freq_ids(win_side)[None, None, :] % img_side
    angles = phase_int.astype(jnp.float32) * (2.0 * math.pi / img_side)
    return jnp.concatenate(
        [jnp.cos(angles).astype(jnp.bfloat16), jnp.sin(angles).astype(jnp.bfloat16)], axis=1
    )


def phase_pack(tag_flat, img_side, win_side):
    rows_t = phase_rows(tag_flat[:, 2], img_side, win_side)
    cols_t = phase_rows(tag_flat[:, 3], img_side, win_side)
    cols_bt = jnp.concatenate([-cols_t[:, TW:], cols_t[:, :TW]], axis=1)
    spare = jnp.zeros((rows_t.shape[0], win_side - 4 * TW, win_side), jnp.bfloat16)
    flat = jnp.concatenate([rows_t, cols_t, spare], axis=1)
    rows3 = jnp.concatenate([rows_t, rows_t, rows_t], axis=1)
    planes = [
        jnp.pad(jnp.swapaxes(t, 1, 2), ((0, 0), (0, 0), (0, win_side - t.shape[1])))
        for t in (rows3, cols_t, cols_bt)
    ]
    return jnp.stack(planes + [flat], axis=1)


def on_device(images, references, particle_class, rotation, defocus_bin, window_anchor):
    part_count = images.shape[0]
    img_side = images.shape[1]
    win_side = references.shape[2]
    per_owner = references.shape[0]
    owners = lax.axis_size("dom")
    capacity = max(2, 2 * part_count // owners)
    slot_count = owners * capacity
    target = particle_class // per_owner
    local_class = particle_class - target * per_owner
    positions = jnp.arange(part_count, dtype=jnp.int32)
    same_owner = (target[:, None] == target[None, :]) & (positions[None, :] < positions[:, None])
    slot_rank = jnp.sum(same_owner.astype(jnp.int32), axis=1)
    slot_place = target * capacity + slot_rank
    slot_tags = jnp.stack(
        [local_class + 1, defocus_bin, window_anchor[0], window_anchor[1]], axis=1
    ).astype(jnp.bfloat16)
    tag_buffer = (
        jnp.zeros((slot_count, 4), jnp.bfloat16)
        .at[slot_place]
        .set(slot_tags)
        .reshape(owners, capacity, 4)
    )
    dft_cos, dft_sin = dft_tables(img_side, win_side)
    fourier_own = transform(images, rotation, dft_cos, dft_sin)
    buffer = (
        jnp.zeros((slot_count, 2, win_side, win_side), jnp.bfloat16).at[slot_place].set(fourier_own)
    )
    buffer = buffer.reshape(owners, capacity, 2, win_side, win_side)
    ctf_bins = ctf_table(jnp.arange(16, dtype=jnp.int32), win_side)
    coeff_block = lax.all_to_all(buffer, "dom", split_axis=0, concat_axis=0, tiled=True)
    tag_block = lax.all_to_all(tag_buffer, "dom", split_axis=0, concat_axis=0, tiled=True)
    tag_flat = tag_block.reshape(slot_count, 4).astype(jnp.int32)
    live = (tag_flat[:, 0] > 0).astype(jnp.int32)
    order = jnp.argsort(1 - live, stable=True).astype(jnp.int32)
    tag_sorted = tag_flat[order]
    count = jnp.sum(live)
    meta = jnp.concatenate(
        [tag_sorted.T, jnp.full((1, slot_count), count, jnp.int32)], axis=0
    )
    pack = phase_pack(tag_sorted, img_side, win_side)
    group = 4 if slot_count % 4 == 0 else 1
    partial_value, info_sorted = group_eval(
        meta,
        order,
        coeff_block.reshape(slot_count, 2, win_side, win_side),
        references,
        ctf_bins,
        pack,
        group,
    )
    info = jnp.zeros((slot_count, 3), jnp.float32).at[order].set(info_sorted[:, 0, :3])
    returned = lax.all_to_all(
        info.reshape(owners, capacity, 3), "dom", split_axis=0, concat_axis=0, tiled=True
    )
    summed = lax.psum_scatter(partial_value, "cls", scatter_dimension=2, tiled=True)
    divisor = summed[:, 2] + ridge_term
    new_refs = summed[:, :2] / divisor[:, None]
    particle_info = returned.reshape(slot_count, 3)[slot_place]
    return (new_refs, particle_info.T)


def solution(mesh):
    return jax.shard_map(
        on_device,
        mesh=mesh,
        in_specs=(
            P(("copies", "dom", "cls"), None, None),
            P(("copies", "dom"), None, None, None),
            P(("copies", "dom", "cls")),
            P(("copies", "dom", "cls")),
            P(("copies", "dom", "cls")),
            P(None, ("copies", "dom", "cls")),
        ),
        out_specs=(P(("copies", "dom"), None, "cls", None), P(None, ("copies", "dom", "cls"))),
        check_vma=False,
    )
```

```python
import math

import jax
import jax.numpy as jnp
from jax import lax
from jax.experimental import pallas as pl
from jax.experimental.pallas import tpu as pltpu
from jax.sharding import PartitionSpec as P


TW = 8


score_scale = 0.02
ridge_term = 1.0


def freq_ids(win_side):
    return jnp.arange(win_side, dtype=jnp.int32) - win_side // 2


def dft_tables(img_side, win_side):
    phase_int = (
        freq_ids(win_side)[:, None] * jnp.arange(img_side, dtype=jnp.int32)[None, :] % img_side
    )
    angles = phase_int.astype(jnp.float32) * (2.0 * math.pi / img_side)
    scale_by = 1.0 / math.sqrt(img_side)
    return (
        (jnp.cos(angles) * scale_by).astype(jnp.bfloat16),
        (-jnp.sin(angles) * scale_by).astype(jnp.bfloat16),
    )


def ctf_table(bin_ids, win_side):
    freqs = freq_ids(win_side).astype(jnp.float32)
    radius = (freqs[:, None] * freqs[:, None] + freqs[None, :] * freqs[None, :]) / float(
        win_side * win_side
    )
    strength = 20.0 + 6.0 * bin_ids.astype(jnp.float32)
    return -jnp.sin(strength[:, None, None] * radius[None, :, :] + 0.1)


def transform(images, rot_ids, dft_cos, dft_sin):
    win_side = dft_cos.shape[0]
    stacked = jnp.concatenate([dft_cos, dft_sin], axis=0)
    flag_bits = rot_ids[:, None, None]
    col_table = jnp.where(flag_bits & 2 != 0, stacked[None, :, ::-1], stacked[None])
    plain = jnp.einsum("nyx,nkx->nyk", images, col_table, preferred_element_type=jnp.float32)
    turned = jnp.einsum("nxy,nkx->nyk", images, col_table, preferred_element_type=jnp.float32)
    half_done = jnp.where(flag_bits & 4 != 0, turned, plain).astype(jnp.bfloat16)
    row_cos = jnp.where(flag_bits & 1 != 0, dft_cos[None, :, ::-1], dft_cos[None])
    row_sin = jnp.where(flag_bits & 1 != 0, dft_sin[None, :, ::-1], dft_sin[None])
    from_cos = jnp.einsum("njy,nyk->njk", row_cos, half_done, preferred_element_type=jnp.float32)
    from_sin = jnp.einsum("njy,nyk->njk", row_sin, half_done, preferred_element_type=jnp.float32)
    real_part = from_cos[..., :win_side] - from_sin[..., win_side:]
    imag_part = from_cos[..., win_side:] + from_sin[..., :win_side]
    return jnp.stack([real_part, imag_part], axis=1).astype(jnp.bfloat16)


def _split3(value):
    high = value.astype(jnp.bfloat16)
    rest = value - high.astype(jnp.float32)
    middle = rest.astype(jnp.bfloat16)
    low = (rest - middle.astype(jnp.float32)).astype(jnp.bfloat16)
    return high, middle, low


def _group_kernel(meta_ref, *refs):
    group = len(refs) - 5
    coef_refs = refs[:group]
    ref_ref, ctf_ref, pack_ref, total_ref, info_ref = refs[group:]
    g = pl.program_id(0)
    span = 8
    per_owner = ref_ref.shape[0]
    bins = ctf_ref.shape[0]

    @pl.when(g == 0)
    def _():
        total_ref[...] = jnp.zeros(total_ref.shape, total_ref.dtype)

    info_ref[...] = jnp.zeros(info_ref.shape, info_ref.dtype)

    @pl.when(g * group < meta_ref[4, 0])
    def _():
        lane = lax.broadcasted_iota(jnp.int32, (8, 128), 1)
        sub = lax.broadcasted_iota(jnp.int32, (8, 128), 0)
        inside = lane < span
        st = []
        for j in range(group):
            slot = g * group + j
            tag = meta_ref[0, slot]
            cls = jnp.minimum(jnp.maximum(tag - 1, 0), per_owner - 1)
            bin_id = jnp.minimum(jnp.maximum(meta_ref[1, slot], 0), bins - 1)
            keep = (jnp.full((1, 128), tag, jnp.int32) > 0).astype(jnp.float32)
            coef_re = coef_refs[j][0, 0].astype(jnp.float32)
            coef_im = coef_refs[j][0, 1].astype(jnp.float32)
            ctf = ctf_ref[bin_id]
            pred_re = ctf * ref_ref[cls, 0].astype(jnp.float32)
            pred_im = ctf * ref_ref[cls, 1].astype(jnp.float32)
            prod_re = (coef_re * pred_re + coef_im * pred_im).astype(jnp.bfloat16)
            prod_im = (coef_im * pred_re - coef_re * pred_im).astype(jnp.bfloat16)
            both = jnp.concatenate([prod_re, prod_im], axis=1)
            mix = jnp.concatenate([pack_ref[j, 1], pack_ref[j, 2]], axis=0)
            part = jnp.dot(both, mix, preferred_element_type=jnp.float32)
            st.append(dict(slot=slot, cls=cls, keep=keep, ctf=ctf, coef_re=coef_re, coef_im=coef_im, part=part))
        for j, d in enumerate(st):
            p_hi, p_mid, p_lo = [piece.astype(jnp.float32) for piece in _split3(d["part"])]
            packed = (p_hi + pltpu.roll(p_mid, 2 * span, 1) + pltpu.roll(p_lo, 4 * span, 1)).astype(jnp.bfloat16)
            d["corr3"] = jnp.dot(pack_ref[j, 3][0:16], packed, preferred_element_type=jnp.float32)
        for j, d in enumerate(st):
            corr3 = d["corr3"]
            corr = (corr3 + pltpu.roll(corr3, 128 - 2 * span, 1)) + pltpu.roll(corr3, 128 - 4 * span, 1)
            upper = corr[0:8]
            lower = pltpu.roll(corr[8:16], 128 - span, 1)
            score = jnp.where(inside, score_scale * (upper - lower), -jnp.inf)
            peak = jnp.max(jnp.max(score, axis=1, keepdims=True), axis=0, keepdims=True)
            total = jnp.sum(jnp.sum(jnp.exp(score - peak), axis=1, keepdims=True), axis=0, keepdims=True)
            evidence = peak + jnp.log(total)
            weight = jnp.where(inside, jnp.exp(score - evidence), 0.0)
            slot = d["slot"]
            row_shift = (jnp.full((8, 128), meta_ref[2, slot], jnp.int32) + sub - span // 2).astype(jnp.float32)
            col_shift = (jnp.full((8, 128), meta_ref[3, slot], jnp.int32) + lane - span // 2).astype(jnp.float32)
            by_row = jnp.sum(weight, axis=1, keepdims=True)
            mean_row = jnp.sum(by_row * row_shift[:, 0:1], axis=0, keepdims=True)
            by_col = jnp.sum(weight, axis=0, keepdims=True)
            mean_col = jnp.sum(jnp.where(inside[0:1], by_col * col_shift[0:1], 0.0), axis=1, keepdims=True)
            info_ref[j] = jnp.where(
                sub == 0,
                jnp.where(lane == 0, evidence, jnp.where(lane == 1, mean_row, jnp.where(lane == 2, mean_col, 0.0))),
                0.0,
            )
            shifted = pltpu.roll(weight, span, 1)
            stacked_w = jnp.concatenate([weight, shifted], axis=0)
            pad = jnp.zeros((112, 128), jnp.bfloat16)
            col_rows = jnp.concatenate([pack_ref[j, 3][16:32], pad], axis=0)
            w_pieces = jnp.concatenate(_split3(stacked_w), axis=0)
            d["q3"] = jnp.dot(w_pieces, col_rows, preferred_element_type=jnp.float32)
        for j, d in enumerate(st):
            q3 = d["q3"]
            qpart = (q3[0:16] + q3[16:32]) + q3[32:48]
            q_re = qpart[0:8]
            q_im = qpart[8:16]
            spare = jnp.zeros((80, 128), jnp.bfloat16)
            rhs_re = jnp.concatenate(list(_split3(jnp.concatenate([q_re, -q_im], axis=0))) + [spare], axis=0)
            rhs_im = jnp.concatenate(list(_split3(jnp.concatenate([q_im, q_re], axis=0))) + [spare], axis=0)
            d["back"] = jnp.dot(
                pack_ref[j, 0], jnp.concatenate([rhs_re, rhs_im], axis=1), preferred_element_type=jnp.float32
            )
        for d in st:
            back_re = d["back"][:, 0:128]
            back_im = d["back"][:, 128:256]
            ctf, coef_re, coef_im, keep, cls = d["ctf"], d["coef_re"], d["coef_im"], d["keep"], d["cls"]
            term_re = ctf * (coef_re * back_re - coef_im * back_im)
            term_im = ctf * (coef_re * back_im + coef_im * back_re)
            total_ref[cls, 0] = total_ref[cls, 0] + term_re * keep
            total_ref[cls, 1] = total_ref[cls, 1] + term_im * keep
            total_ref[cls, 2] = total_ref[cls, 2] + ctf * ctf * keep


def group_eval(meta, order, coef, refs, ctf_tab, pack, group, interpret=False):
    slots = coef.shape[0]
    per_owner = refs.shape[0]
    win = coef.shape[2]
    bins = ctf_tab.shape[0]
    table = jnp.concatenate([meta, order[None]], axis=0)

    def coef_map(j):
        return lambda g, table: (table[5, g * group + j], 0, 0, 0)

    grid_spec = pltpu.PrefetchScalarGridSpec(
        num_scalar_prefetch=1,
        grid=(slots // group,),
        in_specs=[pl.BlockSpec((1, 2, win, win), coef_map(j)) for j in range(group)]
        + [
            pl.BlockSpec((per_owner, 2, win, win), lambda g, table: (0, 0, 0, 0)),
            pl.BlockSpec((bins, win, win), lambda g, table: (0, 0, 0)),
            pl.BlockSpec((group, 4, win, win), lambda g, table: (g, 0, 0, 0)),
        ],
        out_specs=[
            pl.BlockSpec((per_owner, 3, win, win), lambda g, table: (0, 0, 0, 0)),
            pl.BlockSpec((group, 8, 128), lambda g, table: (g, 0, 0)),
        ],
    )
    return pl.pallas_call(
        _group_kernel,
        grid_spec=grid_spec,
        out_shape=[
            jax.ShapeDtypeStruct((per_owner, 3, win, win), jnp.float32),
            jax.ShapeDtypeStruct((slots, 8, 128), jnp.float32),
        ],
        compiler_params=pltpu.CompilerParams(dimension_semantics=("arbitrary",)),
        interpret=interpret,
    )(table, *([coef] * group), refs, ctf_tab, pack)


def phase_rows(anchor, img_side, win_side):
    shifts = anchor[:, None] + jnp.arange(TW, dtype=jnp.int32)[None, :] - TW // 2
    phase_int = shifts[:, :, None] * freq_ids(win_side)[None, None, :] % img_side
    angles = phase_int.astype(jnp.float32) * (2.0 * math.pi / img_side)
    return jnp.concatenate(
        [jnp.cos(angles).astype(jnp.bfloat16), jnp.sin(angles).astype(jnp.bfloat16)], axis=1
    )


def phase_pack(tag_flat, img_side, win_side):
    rows_t = phase_rows(tag_flat[:, 2], img_side, win_side)
    cols_t = phase_rows(tag_flat[:, 3], img_side, win_side)
    cols_bt = jnp.concatenate([-cols_t[:, TW:], cols_t[:, :TW]], axis=1)
    spare = jnp.zeros((rows_t.shape[0], win_side - 4 * TW, win_side), jnp.bfloat16)
    flat = jnp.concatenate([rows_t, cols_t, spare], axis=1)
    rows3 = jnp.concatenate([rows_t, rows_t, rows_t], axis=1)
    planes = [
        jnp.pad(jnp.swapaxes(t, 1, 2), ((0, 0), (0, 0), (0, win_side - t.shape[1])))
        for t in (rows3, cols_t, cols_bt)
    ]
    return jnp.stack(planes + [flat], axis=1)


def on_device(images, references, particle_class, rotation, defocus_bin, window_anchor):
    part_count = images.shape[0]
    img_side = images.shape[1]
    win_side = references.shape[2]
    per_owner = references.shape[0]
    owners = lax.axis_size("dom")
    capacity = max(2, 2 * part_count // owners)
    slot_count = owners * capacity
    target = particle_class // per_owner
    local_class = particle_class - target * per_owner
    positions = jnp.arange(part_count, dtype=jnp.int32)
    same_owner = (target[:, None] == target[None, :]) & (positions[None, :] < positions[:, None])
    slot_rank = jnp.sum(same_owner.astype(jnp.int32), axis=1)
    slot_place = target * capacity + slot_rank
    slot_tags = jnp.stack(
        [local_class + 1, defocus_bin, window_anchor[0], window_anchor[1]], axis=1
    ).astype(jnp.bfloat16)
    tag_buffer = (
        jnp.zeros((slot_count, 4), jnp.bfloat16)
        .at[slot_place]
        .set(slot_tags)
        .reshape(owners, capacity, 4)
    )
    dft_cos, dft_sin = dft_tables(img_side, win_side)
    fourier_own = transform(images, rotation, dft_cos, dft_sin)
    hits = slot_place[None, :] == jnp.arange(slot_count, dtype=jnp.int32)[:, None]
    source = jnp.argmax(hits, axis=1)
    filled = jnp.any(hits, axis=1)
    buffer = jnp.where(filled[:, None, None, None], fourier_own[source], jnp.zeros((), jnp.bfloat16))
    buffer = buffer.reshape(owners, capacity, 2, win_side, win_side)
    coeff_block = lax.all_to_all(buffer, "dom", split_axis=0, concat_axis=0, tiled=True)
    ctf_bins = ctf_table(jnp.arange(16, dtype=jnp.int32), win_side)
    tag_block = lax.all_to_all(tag_buffer, "dom", split_axis=0, concat_axis=0, tiled=True)
    tag_flat = tag_block.reshape(slot_count, 4).astype(jnp.int32)
    live = (tag_flat[:, 0] > 0).astype(jnp.int32)
    order = jnp.argsort(1 - live, stable=True).astype(jnp.int32)
    tag_sorted = tag_flat[order]
    count = jnp.sum(live)
    meta = jnp.concatenate(
        [tag_sorted.T, jnp.full((1, slot_count), count, jnp.int32)], axis=0
    )
    pack = phase_pack(tag_sorted, img_side, win_side)
    group = 4 if slot_count % 4 == 0 else 1
    partial_value, info_sorted = group_eval(
        meta,
        order,
        coeff_block.reshape(slot_count, 2, win_side, win_side),
        references,
        ctf_bins,
        pack,
        group,
    )
    info = jnp.zeros((slot_count, 3), jnp.float32).at[order].set(info_sorted[:, 0, :3])
    returned = lax.all_to_all(
        info.reshape(owners, capacity, 3), "dom", split_axis=0, concat_axis=0, tiled=True
    )
    summed = lax.psum_scatter(partial_value, "cls", scatter_dimension=2, tiled=True)
    divisor = summed[:, 2] + ridge_term
    new_refs = summed[:, :2] / divisor[:, None]
    particle_info = returned.reshape(slot_count, 3)[slot_place]
    return (new_refs, particle_info.T)


def solution(mesh):
    return jax.shard_map(
        on_device,
        mesh=mesh,
        in_specs=(
            P(("copies", "dom", "cls"), None, None),
            P(("copies", "dom"), None, None, None),
            P(("copies", "dom", "cls")),
            P(("copies", "dom", "cls")),
            P(("copies", "dom", "cls")),
            P(None, ("copies", "dom", "cls")),
        ),
        out_specs=(P(("copies", "dom"), None, "cls", None), P(None, ("copies", "dom", "cls"))),
        check_vma=False,
    )
```

```python
import math

import jax
import jax.numpy as jnp
from jax import lax
from jax.experimental import pallas as pl
from jax.experimental.pallas import tpu as pltpu
from jax.sharding import PartitionSpec as P


TW = 8


score_scale = 0.02
ridge_term = 1.0


def freq_ids(win_side):
    return jnp.arange(win_side, dtype=jnp.int32) - win_side // 2


def dft_tables(img_side, win_side):
    phase_int = (
        freq_ids(win_side)[:, None] * jnp.arange(img_side, dtype=jnp.int32)[None, :] % img_side
    )
    angles = phase_int.astype(jnp.float32) * (2.0 * math.pi / img_side)
    scale_by = 1.0 / math.sqrt(img_side)
    return (
        (jnp.cos(angles) * scale_by).astype(jnp.bfloat16),
        (-jnp.sin(angles) * scale_by).astype(jnp.bfloat16),
    )


def ctf_table(bin_ids, win_side):
    freqs = freq_ids(win_side).astype(jnp.float32)
    radius = (freqs[:, None] * freqs[:, None] + freqs[None, :] * freqs[None, :]) / float(
        win_side * win_side
    )
    strength = 20.0 + 6.0 * bin_ids.astype(jnp.float32)
    return -jnp.sin(strength[:, None, None] * radius[None, :, :] + 0.1)


def transform(images, rot_ids, dft_cos, dft_sin):
    win_side = dft_cos.shape[0]
    stacked = jnp.concatenate([dft_cos, dft_sin], axis=0)
    flag_bits = rot_ids[:, None, None]
    col_table = jnp.where(flag_bits & 2 != 0, stacked[None, :, ::-1], stacked[None])
    plain = jnp.einsum("nyx,nkx->nyk", images, col_table, preferred_element_type=jnp.float32)
    turned = jnp.einsum("nxy,nkx->nyk", images, col_table, preferred_element_type=jnp.float32)
    half_done = jnp.where(flag_bits & 4 != 0, turned, plain).astype(jnp.bfloat16)
    row_cos = jnp.where(flag_bits & 1 != 0, dft_cos[None, :, ::-1], dft_cos[None])
    row_sin = jnp.where(flag_bits & 1 != 0, dft_sin[None, :, ::-1], dft_sin[None])
    from_cos = jnp.einsum("njy,nyk->njk", row_cos, half_done, preferred_element_type=jnp.float32)
    from_sin = jnp.einsum("njy,nyk->njk", row_sin, half_done, preferred_element_type=jnp.float32)
    real_part = from_cos[..., :win_side] - from_sin[..., win_side:]
    imag_part = from_cos[..., win_side:] + from_sin[..., :win_side]
    return jnp.stack([real_part, imag_part], axis=1).astype(jnp.bfloat16)


def _split3(value):
    high = value.astype(jnp.bfloat16)
    rest = value - high.astype(jnp.float32)
    middle = rest.astype(jnp.bfloat16)
    low = (rest - middle.astype(jnp.float32)).astype(jnp.bfloat16)
    return high, middle, low


def _group_kernel(meta_ref, *refs):
    group = len(refs) - 5
    coef_refs = refs[:group]
    ref_ref, ctf_ref, pack_ref, total_ref, info_ref = refs[group:]
    g = pl.program_id(0)
    span = 8
    per_owner = ref_ref.shape[0]
    bins = ctf_ref.shape[0]

    @pl.when(g == 0)
    def _():
        total_ref[...] = jnp.zeros(total_ref.shape, total_ref.dtype)

    info_ref[...] = jnp.zeros(info_ref.shape, info_ref.dtype)

    @pl.when(g * group < meta_ref[4, 0])
    def _():
        lane = lax.broadcasted_iota(jnp.int32, (8, 128), 1)
        sub = lax.broadcasted_iota(jnp.int32, (8, 128), 0)
        inside = lane < span
        st = []
        for j in range(group):
            slot = g * group + j
            tag = meta_ref[0, slot]
            cls = jnp.minimum(jnp.maximum(tag - 1, 0), per_owner - 1)
            bin_id = jnp.minimum(jnp.maximum(meta_ref[1, slot], 0), bins - 1)
            keep = (jnp.full((1, 128), tag, jnp.int32) > 0).astype(jnp.float32)
            coef_re = coef_refs[j][0, 0].astype(jnp.float32)
            coef_im = coef_refs[j][0, 1].astype(jnp.float32)
            ctf = ctf_ref[bin_id]
            pred_re = ctf * ref_ref[cls, 0].astype(jnp.float32)
            pred_im = ctf * ref_ref[cls, 1].astype(jnp.float32)
            prod_re = (coef_re * pred_re + coef_im * pred_im).astype(jnp.bfloat16)
            prod_im = (coef_im * pred_re - coef_re * pred_im).astype(jnp.bfloat16)
            both = jnp.concatenate([prod_re, prod_im], axis=1)
            mix = jnp.concatenate([pack_ref[j, 1], pack_ref[j, 2]], axis=0)
            part = jnp.dot(both, mix, preferred_element_type=jnp.float32)
            st.append(dict(slot=slot, cls=cls, keep=keep, ctf=ctf, coef_re=coef_re, coef_im=coef_im, part=part))
        for j, d in enumerate(st):
            p_hi, p_mid, p_lo = [piece.astype(jnp.float32) for piece in _split3(d["part"])]
            packed = (p_hi + pltpu.roll(p_mid, 2 * span, 1) + pltpu.roll(p_lo, 4 * span, 1)).astype(jnp.bfloat16)
            d["corr3"] = jnp.dot(pack_ref[j, 3][0:16], packed, preferred_element_type=jnp.float32)
        for j, d in enumerate(st):
            corr3 = d["corr3"]
            corr = (corr3 + pltpu.roll(corr3, 128 - 2 * span, 1)) + pltpu.roll(corr3, 128 - 4 * span, 1)
            upper = corr[0:8]
            lower = pltpu.roll(corr[8:16], 128 - span, 1)
            score = jnp.where(inside, score_scale * (upper - lower), -jnp.inf)
            peak = jnp.max(jnp.max(score, axis=1, keepdims=True), axis=0, keepdims=True)
            total = jnp.sum(jnp.sum(jnp.exp(score - peak), axis=1, keepdims=True), axis=0, keepdims=True)
            evidence = peak + jnp.log(total)
            weight = jnp.where(inside, jnp.exp(score - evidence), 0.0)
            slot = d["slot"]
            row_shift = (jnp.full((8, 128), meta_ref[2, slot], jnp.int32) + sub - span // 2).astype(jnp.float32)
            col_shift = (jnp.full((8, 128), meta_ref[3, slot], jnp.int32) + lane - span // 2).astype(jnp.float32)
            by_row = jnp.sum(weight, axis=1, keepdims=True)
            mean_row = jnp.sum(by_row * row_shift[:, 0:1], axis=0, keepdims=True)
            by_col = jnp.sum(weight, axis=0, keepdims=True)
            mean_col = jnp.sum(jnp.where(inside[0:1], by_col * col_shift[0:1], 0.0), axis=1, keepdims=True)
            info_ref[j] = jnp.where(
                sub == 0,
                jnp.where(lane == 0, evidence, jnp.where(lane == 1, mean_row, jnp.where(lane == 2, mean_col, 0.0))),
                0.0,
            )
            shifted = pltpu.roll(weight, span, 1)
            stacked_w = jnp.concatenate([weight, shifted], axis=0)
            pad = jnp.zeros((112, 128), jnp.bfloat16)
            col_rows = jnp.concatenate([pack_ref[j, 3][16:32], pad], axis=0)
            w_pieces = jnp.concatenate(_split3(stacked_w), axis=0)
            d["q3"] = jnp.dot(w_pieces, col_rows, preferred_element_type=jnp.float32)
        for j, d in enumerate(st):
            q3 = d["q3"]
            qpart = (q3[0:16] + q3[16:32]) + q3[32:48]
            q_re = qpart[0:8]
            q_im = qpart[8:16]
            spare = jnp.zeros((80, 128), jnp.bfloat16)
            rhs_re = jnp.concatenate(list(_split3(jnp.concatenate([q_re, -q_im], axis=0))) + [spare], axis=0)
            rhs_im = jnp.concatenate(list(_split3(jnp.concatenate([q_im, q_re], axis=0))) + [spare], axis=0)
            d["back"] = jnp.dot(
                pack_ref[j, 0], jnp.concatenate([rhs_re, rhs_im], axis=1), preferred_element_type=jnp.float32
            )
        for d in st:
            back_re = d["back"][:, 0:128]
            back_im = d["back"][:, 128:256]
            ctf, coef_re, coef_im, keep, cls = d["ctf"], d["coef_re"], d["coef_im"], d["keep"], d["cls"]
            term_re = ctf * (coef_re * back_re - coef_im * back_im)
            term_im = ctf * (coef_re * back_im + coef_im * back_re)
            total_ref[cls, 0] = total_ref[cls, 0] + term_re * keep
            total_ref[cls, 1] = total_ref[cls, 1] + term_im * keep
            total_ref[cls, 2] = total_ref[cls, 2] + ctf * ctf * keep


def group_eval(meta, order, coef, refs, ctf_tab, pack, group, interpret=False):
    slots = coef.shape[0]
    per_owner = refs.shape[0]
    win = coef.shape[2]
    bins = ctf_tab.shape[0]
    table = jnp.concatenate([meta, order[None]], axis=0)

    def coef_map(j):
        return lambda g, table: (table[5, g * group + j], 0, 0, 0)

    grid_spec = pltpu.PrefetchScalarGridSpec(
        num_scalar_prefetch=1,
        grid=(slots // group,),
        in_specs=[pl.BlockSpec((1, 2, win, win), coef_map(j)) for j in range(group)]
        + [
            pl.BlockSpec((per_owner, 2, win, win), lambda g, table: (0, 0, 0, 0)),
            pl.BlockSpec((bins, win, win), lambda g, table: (0, 0, 0)),
            pl.BlockSpec((group, 4, win, win), lambda g, table: (g, 0, 0, 0)),
        ],
        out_specs=[
            pl.BlockSpec((per_owner, 3, win, win), lambda g, table: (0, 0, 0, 0)),
            pl.BlockSpec((group, 8, 128), lambda g, table: (g, 0, 0)),
        ],
    )
    return pl.pallas_call(
        _group_kernel,
        grid_spec=grid_spec,
        out_shape=[
            jax.ShapeDtypeStruct((per_owner, 3, win, win), jnp.float32),
            jax.ShapeDtypeStruct((slots, 8, 128), jnp.float32),
        ],
        compiler_params=pltpu.CompilerParams(dimension_semantics=("arbitrary",)),
        interpret=interpret,
    )(table, *([coef] * group), refs, ctf_tab, pack)


def phase_rows(anchor, img_side, win_side):
    shifts = anchor[:, None] + jnp.arange(TW, dtype=jnp.int32)[None, :] - TW // 2
    phase_int = shifts[:, :, None] * freq_ids(win_side)[None, None, :] % img_side
    angles = phase_int.astype(jnp.float32) * (2.0 * math.pi / img_side)
    return jnp.concatenate(
        [jnp.cos(angles).astype(jnp.bfloat16), jnp.sin(angles).astype(jnp.bfloat16)], axis=1
    )


def phase_pack(tag_flat, img_side, win_side):
    rows_t = phase_rows(tag_flat[:, 2], img_side, win_side)
    cols_t = phase_rows(tag_flat[:, 3], img_side, win_side)
    cols_bt = jnp.concatenate([-cols_t[:, TW:], cols_t[:, :TW]], axis=1)
    spare = jnp.zeros((rows_t.shape[0], win_side - 4 * TW, win_side), jnp.bfloat16)
    flat = jnp.concatenate([rows_t, cols_t, spare], axis=1)
    rows3 = jnp.concatenate([rows_t, rows_t, rows_t], axis=1)
    planes = [
        jnp.pad(jnp.swapaxes(t, 1, 2), ((0, 0), (0, 0), (0, win_side - t.shape[1])))
        for t in (rows3, cols_t, cols_bt)
    ]
    return jnp.stack(planes + [flat], axis=1)


def on_device(images, references, particle_class, rotation, defocus_bin, window_anchor):
    part_count = images.shape[0]
    img_side = images.shape[1]
    win_side = references.shape[2]
    per_owner = references.shape[0]
    owners = lax.axis_size("dom")
    capacity = max(2, 2 * part_count // owners)
    slot_count = owners * capacity
    target = particle_class // per_owner
    positions = jnp.arange(part_count, dtype=jnp.int32)
    same_owner = (target[:, None] == target[None, :]) & (positions[None, :] < positions[:, None])
    slot_rank = jnp.sum(same_owner.astype(jnp.int32), axis=1)
    slot_place = target * capacity + slot_rank
    own_meta = jnp.stack([particle_class, defocus_bin, window_anchor[0], window_anchor[1]], axis=1)
    all_meta = lax.all_gather(own_meta, "dom")
    dft_cos, dft_sin = dft_tables(img_side, win_side)
    fourier_own = transform(images, rotation, dft_cos, dft_sin)
    hits = (slot_place[None, :] == jnp.arange(slot_count, dtype=jnp.int32)[:, None]).astype(jnp.bfloat16)
    buffer = jnp.einsum("qi,irjk->qrjk", hits, fourier_own)
    buffer = buffer.reshape(owners, capacity, 2, win_side, win_side)
    coeff_block = lax.all_to_all(buffer, "dom", split_axis=0, concat_axis=0, tiled=True)
    ctf_bins = ctf_table(jnp.arange(16, dtype=jnp.int32), win_side)
    me = lax.axis_index("dom")
    src_target = all_meta[:, :, 0] // per_owner
    earlier = positions[None, None, :] < positions[None, :, None]
    src_rank = jnp.sum(
        ((src_target[:, :, None] == src_target[:, None, :]) & earlier).astype(jnp.int32), axis=2
    )
    ranks = jnp.arange(capacity, dtype=jnp.int32)
    chosen = (src_target[:, None, :] == me) & (src_rank[:, None, :] == ranks[None, :, None])
    fields = all_meta.at[:, :, 0].set(all_meta[:, :, 0] - me * per_owner + 1)
    tag_block = jnp.sum(jnp.where(chosen[..., None], fields[:, None, :, :], 0), axis=2)
    tag_flat = tag_block.reshape(slot_count, 4).astype(jnp.int32)
    live = (tag_flat[:, 0] > 0).astype(jnp.int32)
    order = jnp.argsort(1 - live, stable=True).astype(jnp.int32)
    tag_sorted = tag_flat[order]
    count = jnp.sum(live)
    meta = jnp.concatenate(
        [tag_sorted.T, jnp.full((1, slot_count), count, jnp.int32)], axis=0
    )
    pack = phase_pack(tag_sorted, img_side, win_side)
    group = 4 if slot_count % 4 == 0 else 1
    partial_value, info_sorted = group_eval(
        meta,
        order,
        coeff_block.reshape(slot_count, 2, win_side, win_side),
        references,
        ctf_bins,
        pack,
        group,
    )
    info = jnp.zeros((slot_count, 3), jnp.float32).at[order].set(info_sorted[:, 0, :3])
    returned = lax.all_to_all(
        info.reshape(owners, capacity, 3), "dom", split_axis=0, concat_axis=0, tiled=True
    )
    summed = lax.psum_scatter(partial_value, "cls", scatter_dimension=2, tiled=True)
    divisor = summed[:, 2] + ridge_term
    new_refs = summed[:, :2] / divisor[:, None]
    particle_info = returned.reshape(slot_count, 3)[slot_place]
    return (new_refs, particle_info.T)


def solution(mesh):
    return jax.shard_map(
        on_device,
        mesh=mesh,
        in_specs=(
            P(("copies", "dom", "cls"), None, None),
            P(("copies", "dom"), None, None, None),
            P(("copies", "dom", "cls")),
            P(("copies", "dom", "cls")),
            P(("copies", "dom", "cls")),
            P(None, ("copies", "dom", "cls")),
        ),
        out_specs=(P(("copies", "dom"), None, "cls", None), P(None, ("copies", "dom", "cls"))),
        check_vma=False,
    )
```

```python
import math

import jax
import jax.numpy as jnp
from jax import lax
from jax.experimental import pallas as pl
from jax.experimental.pallas import tpu as pltpu
from jax.sharding import PartitionSpec as P


TW = 8


score_scale = 0.02
ridge_term = 1.0


def freq_ids(win_side):
    return jnp.arange(win_side, dtype=jnp.int32) - win_side // 2


def dft_tables(img_side, win_side):
    phase_int = (
        freq_ids(win_side)[:, None] * jnp.arange(img_side, dtype=jnp.int32)[None, :] % img_side
    )
    angles = phase_int.astype(jnp.float32) * (2.0 * math.pi / img_side)
    scale_by = 1.0 / math.sqrt(img_side)
    return (
        (jnp.cos(angles) * scale_by).astype(jnp.bfloat16),
        (-jnp.sin(angles) * scale_by).astype(jnp.bfloat16),
    )


def ctf_table(bin_ids, win_side):
    freqs = freq_ids(win_side).astype(jnp.float32)
    radius = (freqs[:, None] * freqs[:, None] + freqs[None, :] * freqs[None, :]) / float(
        win_side * win_side
    )
    strength = 20.0 + 6.0 * bin_ids.astype(jnp.float32)
    return -jnp.sin(strength[:, None, None] * radius[None, :, :] + 0.1)


def transform(images, rot_ids, dft_cos, dft_sin):
    win_side = dft_cos.shape[0]
    stacked = jnp.concatenate([dft_cos, dft_sin], axis=0)
    flag_bits = rot_ids[:, None, None]
    col_table = jnp.where(flag_bits & 2 != 0, stacked[None, :, ::-1], stacked[None])
    plain = jnp.einsum("nyx,nkx->nyk", images, col_table, preferred_element_type=jnp.float32)
    turned = jnp.einsum("nxy,nkx->nyk", images, col_table, preferred_element_type=jnp.float32)
    half_done = jnp.where(flag_bits & 4 != 0, turned, plain).astype(jnp.bfloat16)
    row_cos = jnp.where(flag_bits & 1 != 0, dft_cos[None, :, ::-1], dft_cos[None])
    row_sin = jnp.where(flag_bits & 1 != 0, dft_sin[None, :, ::-1], dft_sin[None])
    from_cos = jnp.einsum("njy,nyk->njk", row_cos, half_done, preferred_element_type=jnp.float32)
    from_sin = jnp.einsum("njy,nyk->njk", row_sin, half_done, preferred_element_type=jnp.float32)
    real_part = from_cos[..., :win_side] - from_sin[..., win_side:]
    imag_part = from_cos[..., win_side:] + from_sin[..., :win_side]
    return jnp.stack([real_part, imag_part], axis=1).astype(jnp.bfloat16)


def _split3(value):
    high = value.astype(jnp.bfloat16)
    rest = value - high.astype(jnp.float32)
    middle = rest.astype(jnp.bfloat16)
    low = (rest - middle.astype(jnp.float32)).astype(jnp.bfloat16)
    return high, middle, low


def _group_kernel(meta_ref, *refs):
    group = len(refs) - 5
    coef_refs = refs[:group]
    ref_ref, ctf_ref, pack_ref, total_ref, info_ref = refs[group:]
    g = pl.program_id(0)
    span = 8
    per_owner = ref_ref.shape[0]
    bins = ctf_ref.shape[0]

    @pl.when(g == 0)
    def _():
        total_ref[...] = jnp.zeros(total_ref.shape, total_ref.dtype)

    info_ref[...] = jnp.zeros(info_ref.shape, info_ref.dtype)

    @pl.when(g * group < meta_ref[4, 0])
    def _():
        lane = lax.broadcasted_iota(jnp.int32, (8, 128), 1)
        sub = lax.broadcasted_iota(jnp.int32, (8, 128), 0)
        inside = lane < span
        st = []
        for j in range(group):
            slot = g * group + j
            tag = meta_ref[0, slot]
            cls = jnp.minimum(jnp.maximum(tag - 1, 0), per_owner - 1)
            bin_id = jnp.minimum(jnp.maximum(meta_ref[1, slot], 0), bins - 1)
            keep = (jnp.full((1, 128), tag, jnp.int32) > 0).astype(jnp.float32)
            coef_re = coef_refs[j][0, 0].astype(jnp.float32)
            coef_im = coef_refs[j][0, 1].astype(jnp.float32)
            ctf = ctf_ref[bin_id]
            pred_re = ctf * ref_ref[cls, 0].astype(jnp.float32)
            pred_im = ctf * ref_ref[cls, 1].astype(jnp.float32)
            prod_re = (coef_re * pred_re + coef_im * pred_im).astype(jnp.bfloat16)
            prod_im = (coef_im * pred_re - coef_re * pred_im).astype(jnp.bfloat16)
            both = jnp.concatenate([prod_re, prod_im], axis=1)
            mix = jnp.concatenate([pack_ref[j, 1], pack_ref[j, 2]], axis=0)
            part = jnp.dot(both, mix, preferred_element_type=jnp.float32)
            st.append(dict(slot=slot, cls=cls, keep=keep, ctf=ctf, coef_re=coef_re, coef_im=coef_im, part=part))
        for j, d in enumerate(st):
            p_hi, p_mid, p_lo = [piece.astype(jnp.float32) for piece in _split3(d["part"])]
            packed = (p_hi + pltpu.roll(p_mid, 2 * span, 1) + pltpu.roll(p_lo, 4 * span, 1)).astype(jnp.bfloat16)
            d["corr3"] = jnp.dot(pack_ref[j, 3][0:16], packed, preferred_element_type=jnp.float32)
        for j, d in enumerate(st):
            corr3 = d["corr3"]
            corr = (corr3 + pltpu.roll(corr3, 128 - 2 * span, 1)) + pltpu.roll(corr3, 128 - 4 * span, 1)
            upper = corr[0:8]
            lower = pltpu.roll(corr[8:16], 128 - span, 1)
            score = jnp.where(inside, score_scale * (upper - lower), -jnp.inf)
            peak = jnp.max(jnp.max(score, axis=1, keepdims=True), axis=0, keepdims=True)
            total = jnp.sum(jnp.sum(jnp.exp(score - peak), axis=1, keepdims=True), axis=0, keepdims=True)
            evidence = peak + jnp.log(total)
            weight = jnp.where(inside, jnp.exp(score - evidence), 0.0)
            slot = d["slot"]
            row_shift = (jnp.full((8, 128), meta_ref[2, slot], jnp.int32) + sub - span // 2).astype(jnp.float32)
            col_shift = (jnp.full((8, 128), meta_ref[3, slot], jnp.int32) + lane - span // 2).astype(jnp.float32)
            by_row = jnp.sum(weight, axis=1, keepdims=True)
            mean_row = jnp.sum(by_row * row_shift[:, 0:1], axis=0, keepdims=True)
            by_col = jnp.sum(weight, axis=0, keepdims=True)
            mean_col = jnp.sum(jnp.where(inside[0:1], by_col * col_shift[0:1], 0.0), axis=1, keepdims=True)
            info_ref[j] = jnp.where(
                sub == 0,
                jnp.where(lane == 0, evidence, jnp.where(lane == 1, mean_row, jnp.where(lane == 2, mean_col, 0.0))),
                0.0,
            )
            shifted = pltpu.roll(weight, span, 1)
            stacked_w = jnp.concatenate([weight, shifted], axis=0)
            pad = jnp.zeros((112, 128), jnp.bfloat16)
            col_rows = jnp.concatenate([pack_ref[j, 3][16:32], pad], axis=0)
            w_pieces = jnp.concatenate(_split3(stacked_w), axis=0)
            d["q3"] = jnp.dot(w_pieces, col_rows, preferred_element_type=jnp.float32)
        for j, d in enumerate(st):
            q3 = d["q3"]
            qpart = (q3[0:16] + q3[16:32]) + q3[32:48]
            q_re = qpart[0:8]
            q_im = qpart[8:16]
            spare = jnp.zeros((80, 128), jnp.bfloat16)
            rhs_re = jnp.concatenate(list(_split3(jnp.concatenate([q_re, -q_im], axis=0))) + [spare], axis=0)
            rhs_im = jnp.concatenate(list(_split3(jnp.concatenate([q_im, q_re], axis=0))) + [spare], axis=0)
            d["back"] = jnp.dot(
                pack_ref[j, 0], jnp.concatenate([rhs_re, rhs_im], axis=1), preferred_element_type=jnp.float32
            )
        for d in st:
            back_re = d["back"][:, 0:128]
            back_im = d["back"][:, 128:256]
            ctf, coef_re, coef_im, keep, cls = d["ctf"], d["coef_re"], d["coef_im"], d["keep"], d["cls"]
            term_re = ctf * (coef_re * back_re - coef_im * back_im)
            term_im = ctf * (coef_re * back_im + coef_im * back_re)
            total_ref[cls, 0] = total_ref[cls, 0] + term_re * keep
            total_ref[cls, 1] = total_ref[cls, 1] + term_im * keep
            total_ref[cls, 2] = total_ref[cls, 2] + ctf * ctf * keep


def group_eval(meta, order, coef, refs, ctf_tab, pack, group, interpret=False):
    slots = coef.shape[0]
    per_owner = refs.shape[0]
    win = coef.shape[2]
    bins = ctf_tab.shape[0]
    table = jnp.concatenate([meta, order[None]], axis=0)

    def coef_map(j):
        return lambda g, table: (table[5, g * group + j], 0, 0, 0)

    grid_spec = pltpu.PrefetchScalarGridSpec(
        num_scalar_prefetch=1,
        grid=(slots // group,),
        in_specs=[pl.BlockSpec((1, 2, win, win), coef_map(j)) for j in range(group)]
        + [
            pl.BlockSpec((per_owner, 2, win, win), lambda g, table: (0, 0, 0, 0)),
            pl.BlockSpec((bins, win, win), lambda g, table: (0, 0, 0)),
            pl.BlockSpec((group, 4, win, win), lambda g, table: (g, 0, 0, 0)),
        ],
        out_specs=[
            pl.BlockSpec((per_owner, 3, win, win), lambda g, table: (0, 0, 0, 0)),
            pl.BlockSpec((group, 8, 128), lambda g, table: (g, 0, 0)),
        ],
    )
    return pl.pallas_call(
        _group_kernel,
        grid_spec=grid_spec,
        out_shape=[
            jax.ShapeDtypeStruct((per_owner, 3, win, win), jnp.float32),
            jax.ShapeDtypeStruct((slots, 8, 128), jnp.float32),
        ],
        compiler_params=pltpu.CompilerParams(dimension_semantics=("arbitrary",)),
        interpret=interpret,
    )(table, *([coef] * group), refs, ctf_tab, pack)


def phase_rows(anchor, img_side, win_side):
    shifts = anchor[:, None] + jnp.arange(TW, dtype=jnp.int32)[None, :] - TW // 2
    phase_int = shifts[:, :, None] * freq_ids(win_side)[None, None, :] % img_side
    angles = phase_int.astype(jnp.float32) * (2.0 * math.pi / img_side)
    return jnp.concatenate(
        [jnp.cos(angles).astype(jnp.bfloat16), jnp.sin(angles).astype(jnp.bfloat16)], axis=1
    )


def phase_pack(tag_flat, img_side, win_side):
    rows_t = phase_rows(tag_flat[:, 2], img_side, win_side)
    cols_t = phase_rows(tag_flat[:, 3], img_side, win_side)
    cols_bt = jnp.concatenate([-cols_t[:, TW:], cols_t[:, :TW]], axis=1)
    spare = jnp.zeros((rows_t.shape[0], win_side - 4 * TW, win_side), jnp.bfloat16)
    flat = jnp.concatenate([rows_t, cols_t, spare], axis=1)
    rows3 = jnp.concatenate([rows_t, rows_t, rows_t], axis=1)
    planes = [
        jnp.pad(jnp.swapaxes(t, 1, 2), ((0, 0), (0, 0), (0, win_side - t.shape[1])))
        for t in (rows3, cols_t, cols_bt)
    ]
    return jnp.stack(planes + [flat], axis=1)


def on_device(images, references, particle_class, rotation, defocus_bin, window_anchor):
    part_count = images.shape[0]
    img_side = images.shape[1]
    win_side = references.shape[2]
    per_owner = references.shape[0]
    owners = lax.axis_size("dom")
    capacity = max(2, 2 * part_count // owners)
    slot_count = owners * capacity
    target = particle_class // per_owner
    local_class = particle_class - target * per_owner
    positions = jnp.arange(part_count, dtype=jnp.int32)
    same_owner = (target[:, None] == target[None, :]) & (positions[None, :] < positions[:, None])
    slot_rank = jnp.sum(same_owner.astype(jnp.int32), axis=1)
    slot_place = target * capacity + slot_rank
    slot_tags = jnp.stack(
        [local_class + 1, defocus_bin, window_anchor[0], window_anchor[1]], axis=1
    ).astype(jnp.bfloat16)
    tag_buffer = (
        jnp.zeros((slot_count, 4), jnp.bfloat16)
        .at[slot_place]
        .set(slot_tags)
        .reshape(owners, capacity, 4)
    )
    dft_cos, dft_sin = dft_tables(img_side, win_side)
    fourier_own = transform(images, rotation, dft_cos, dft_sin)
    hits = (slot_place[None, :] == jnp.arange(slot_count, dtype=jnp.int32)[:, None]).astype(jnp.bfloat16)
    buffer = jnp.einsum("qi,irjk->qrjk", hits, fourier_own)
    buffer = buffer.reshape(owners, capacity, 2, win_side, win_side)
    coeff_block = lax.all_to_all(buffer, "dom", split_axis=0, concat_axis=0, tiled=True)
    ctf_bins = ctf_table(jnp.arange(16, dtype=jnp.int32), win_side)
    tag_block = lax.all_to_all(tag_buffer, "dom", split_axis=0, concat_axis=0, tiled=True)
    tag_flat = tag_block.reshape(slot_count, 4).astype(jnp.int32)
    live = (tag_flat[:, 0] > 0).astype(jnp.int32)
    order = jnp.argsort(1 - live, stable=True).astype(jnp.int32)
    tag_sorted = tag_flat[order]
    count = jnp.sum(live)
    meta = jnp.concatenate(
        [tag_sorted.T, jnp.full((1, slot_count), count, jnp.int32)], axis=0
    )
    pack = phase_pack(tag_sorted, img_side, win_side)
    group = 8 if slot_count % 8 == 0 else 1
    partial_value, info_sorted = group_eval(
        meta,
        order,
        coeff_block.reshape(slot_count, 2, win_side, win_side),
        references,
        ctf_bins,
        pack,
        group,
    )
    info = jnp.zeros((slot_count, 3), jnp.float32).at[order].set(info_sorted[:, 0, :3])
    returned = lax.all_to_all(
        info.reshape(owners, capacity, 3), "dom", split_axis=0, concat_axis=0, tiled=True
    )
    summed = lax.psum_scatter(partial_value, "cls", scatter_dimension=2, tiled=True)
    divisor = summed[:, 2] + ridge_term
    new_refs = summed[:, :2] / divisor[:, None]
    particle_info = returned.reshape(slot_count, 3)[slot_place]
    return (new_refs, particle_info.T)


def solution(mesh):
    return jax.shard_map(
        on_device,
        mesh=mesh,
        in_specs=(
            P(("copies", "dom", "cls"), None, None),
            P(("copies", "dom"), None, None, None),
            P(("copies", "dom", "cls")),
            P(("copies", "dom", "cls")),
            P(("copies", "dom", "cls")),
            P(None, ("copies", "dom", "cls")),
        ),
        out_specs=(P(("copies", "dom"), None, "cls", None), P(None, ("copies", "dom", "cls"))),
        check_vma=False,
    )
```

```python
import math

import jax
import jax.numpy as jnp
from jax import lax
from jax.experimental import pallas as pl
from jax.experimental.pallas import tpu as pltpu
from jax.sharding import PartitionSpec as P


TW = 8


score_scale = 0.02
ridge_term = 1.0


def freq_ids(win_side):
    return jnp.arange(win_side, dtype=jnp.int32) - win_side // 2


def dft_tables(img_side, win_side):
    phase_int = (
        freq_ids(win_side)[:, None] * jnp.arange(img_side, dtype=jnp.int32)[None, :] % img_side
    )
    angles = phase_int.astype(jnp.float32) * (2.0 * math.pi / img_side)
    scale_by = 1.0 / math.sqrt(img_side)
    return (
        (jnp.cos(angles) * scale_by).astype(jnp.bfloat16),
        (-jnp.sin(angles) * scale_by).astype(jnp.bfloat16),
    )


def ctf_table(bin_ids, win_side):
    freqs = freq_ids(win_side).astype(jnp.float32)
    radius = (freqs[:, None] * freqs[:, None] + freqs[None, :] * freqs[None, :]) / float(
        win_side * win_side
    )
    strength = 20.0 + 6.0 * bin_ids.astype(jnp.float32)
    return -jnp.sin(strength[:, None, None] * radius[None, :, :] + 0.1)


def transform(images, rot_ids, dft_cos, dft_sin):
    win_side = dft_cos.shape[0]
    stacked = jnp.concatenate([dft_cos, dft_sin], axis=0)
    flag_bits = rot_ids[:, None, None]
    col_table = jnp.where(flag_bits & 2 != 0, stacked[None, :, ::-1], stacked[None])
    plain = jnp.einsum("nyx,nkx->nyk", images, col_table, preferred_element_type=jnp.float32)
    turned = jnp.einsum("nxy,nkx->nyk", images, col_table, preferred_element_type=jnp.float32)
    half_done = jnp.where(flag_bits & 4 != 0, turned, plain).astype(jnp.bfloat16)
    row_cos = jnp.where(flag_bits & 1 != 0, dft_cos[None, :, ::-1], dft_cos[None])
    row_sin = jnp.where(flag_bits & 1 != 0, dft_sin[None, :, ::-1], dft_sin[None])
    from_cos = jnp.einsum("njy,nyk->njk", row_cos, half_done, preferred_element_type=jnp.float32)
    from_sin = jnp.einsum("njy,nyk->njk", row_sin, half_done, preferred_element_type=jnp.float32)
    real_part = from_cos[..., :win_side] - from_sin[..., win_side:]
    imag_part = from_cos[..., win_side:] + from_sin[..., :win_side]
    return jnp.stack([real_part, imag_part], axis=1).astype(jnp.bfloat16)


def _split3(value):
    high = value.astype(jnp.bfloat16)
    rest = value - high.astype(jnp.float32)
    middle = rest.astype(jnp.bfloat16)
    low = (rest - middle.astype(jnp.float32)).astype(jnp.bfloat16)
    return high, middle, low


def _group_kernel(meta_ref, *refs):
    group = len(refs) - 5
    coef_refs = refs[:group]
    ref_ref, ctf_ref, pack_ref, total_ref, info_ref = refs[group:]
    g = pl.program_id(0)
    span = 8
    per_owner = ref_ref.shape[0]
    bins = ctf_ref.shape[0]

    @pl.when(g == 0)
    def _():
        total_ref[...] = jnp.zeros(total_ref.shape, total_ref.dtype)

    info_ref[...] = jnp.zeros(info_ref.shape, info_ref.dtype)

    @pl.when(g * group < meta_ref[4, 0])
    def _():
        lane = lax.broadcasted_iota(jnp.int32, (8, 128), 1)
        sub = lax.broadcasted_iota(jnp.int32, (8, 128), 0)
        inside = lane < span
        win = ctf_ref.shape[1]
        half = win // 2
        row = lax.broadcasted_iota(jnp.int32, (win, win), 0)
        col = lax.broadcasted_iota(jnp.int32, (win, win), 1)
        mirror = (col == (win - row) % win).astype(jnp.bfloat16)
        pick = (col == row - half - 1).astype(jnp.bfloat16)
        upper_rows = row <= half
        edge = (row > half) & (col == 0)
        kept = []
        for j in range(group):
            block = coef_refs[j][0]
            spare = jnp.zeros((win - block.shape[1], win), jnp.bfloat16)
            full_re = jnp.concatenate([block[0], spare], axis=0)
            full_im = jnp.concatenate([block[1], spare], axis=0)
            zero = jnp.zeros((), jnp.bfloat16)
            top_re = jnp.where(upper_rows, full_re, zero)
            top_im = jnp.where(upper_rows, full_im, zero)
            turned = jnp.dot(
                mirror, jnp.concatenate([top_re, top_im], axis=1), preferred_element_type=jnp.float32
            ).astype(jnp.bfloat16)
            stacked = jnp.concatenate([turned[:, 0:win], turned[:, win : 2 * win]], axis=0)
            flipped = jnp.dot(stacked, mirror, preferred_element_type=jnp.float32)
            column = lax.dot_general(
                pick, jnp.concatenate([full_re, full_im], axis=0), (((1,), (1,)), ((), ())),
                preferred_element_type=jnp.float32,
            )
            col_re = pltpu.roll(column[:, 0:win], win - half - 1, 1)
            col_im = pltpu.roll(column[:, win : 2 * win], win - half - 1, 1)
            coef_re = jnp.where(edge, col_re, jnp.where(upper_rows, top_re.astype(jnp.float32), flipped[0:win]))
            coef_im = jnp.where(edge, col_im, jnp.where(upper_rows, top_im.astype(jnp.float32), -flipped[win : 2 * win]))
            kept.append((coef_re, coef_im))
        st = []
        for j in range(group):
            slot = g * group + j
            tag = meta_ref[0, slot]
            cls = jnp.minimum(jnp.maximum(tag - 1, 0), per_owner - 1)
            bin_id = jnp.minimum(jnp.maximum(meta_ref[1, slot], 0), bins - 1)
            keep = (jnp.full((1, 128), tag, jnp.int32) > 0).astype(jnp.float32)
            coef_re, coef_im = kept[j]
            ctf = ctf_ref[bin_id]
            pred_re = ctf * ref_ref[cls, 0].astype(jnp.float32)
            pred_im = ctf * ref_ref[cls, 1].astype(jnp.float32)
            prod_re = (coef_re * pred_re + coef_im * pred_im).astype(jnp.bfloat16)
            prod_im = (coef_im * pred_re - coef_re * pred_im).astype(jnp.bfloat16)
            both = jnp.concatenate([prod_re, prod_im], axis=1)
            mix = jnp.concatenate([pack_ref[j, 1], pack_ref[j, 2]], axis=0)
            part = jnp.dot(both, mix, preferred_element_type=jnp.float32)
            st.append(dict(slot=slot, cls=cls, keep=keep, ctf=ctf, coef_re=coef_re, coef_im=coef_im, part=part))
        for j, d in enumerate(st):
            p_hi, p_mid, p_lo = [piece.astype(jnp.float32) for piece in _split3(d["part"])]
            packed = (p_hi + pltpu.roll(p_mid, 2 * span, 1) + pltpu.roll(p_lo, 4 * span, 1)).astype(jnp.bfloat16)
            d["corr3"] = jnp.dot(pack_ref[j, 3][0:16], packed, preferred_element_type=jnp.float32)
        for j, d in enumerate(st):
            corr3 = d["corr3"]
            corr = (corr3 + pltpu.roll(corr3, 128 - 2 * span, 1)) + pltpu.roll(corr3, 128 - 4 * span, 1)
            upper = corr[0:8]
            lower = pltpu.roll(corr[8:16], 128 - span, 1)
            score = jnp.where(inside, score_scale * (upper - lower), -jnp.inf)
            peak = jnp.max(jnp.max(score, axis=1, keepdims=True), axis=0, keepdims=True)
            total = jnp.sum(jnp.sum(jnp.exp(score - peak), axis=1, keepdims=True), axis=0, keepdims=True)
            evidence = peak + jnp.log(total)
            weight = jnp.where(inside, jnp.exp(score - evidence), 0.0)
            slot = d["slot"]
            row_shift = (jnp.full((8, 128), meta_ref[2, slot], jnp.int32) + sub - span // 2).astype(jnp.float32)
            col_shift = (jnp.full((8, 128), meta_ref[3, slot], jnp.int32) + lane - span // 2).astype(jnp.float32)
            by_row = jnp.sum(weight, axis=1, keepdims=True)
            mean_row = jnp.sum(by_row * row_shift[:, 0:1], axis=0, keepdims=True)
            by_col = jnp.sum(weight, axis=0, keepdims=True)
            mean_col = jnp.sum(jnp.where(inside[0:1], by_col * col_shift[0:1], 0.0), axis=1, keepdims=True)
            info_ref[j] = jnp.where(
                sub == 0,
                jnp.where(lane == 0, evidence, jnp.where(lane == 1, mean_row, jnp.where(lane == 2, mean_col, 0.0))),
                0.0,
            )
            shifted = pltpu.roll(weight, span, 1)
            stacked_w = jnp.concatenate([weight, shifted], axis=0)
            pad = jnp.zeros((112, 128), jnp.bfloat16)
            col_rows = jnp.concatenate([pack_ref[j, 3][16:32], pad], axis=0)
            w_pieces = jnp.concatenate(_split3(stacked_w), axis=0)
            d["q3"] = jnp.dot(w_pieces, col_rows, preferred_element_type=jnp.float32)
        for j, d in enumerate(st):
            q3 = d["q3"]
            qpart = (q3[0:16] + q3[16:32]) + q3[32:48]
            q_re = qpart[0:8]
            q_im = qpart[8:16]
            spare = jnp.zeros((80, 128), jnp.bfloat16)
            rhs_re = jnp.concatenate(list(_split3(jnp.concatenate([q_re, -q_im], axis=0))) + [spare], axis=0)
            rhs_im = jnp.concatenate(list(_split3(jnp.concatenate([q_im, q_re], axis=0))) + [spare], axis=0)
            d["back"] = jnp.dot(
                pack_ref[j, 0], jnp.concatenate([rhs_re, rhs_im], axis=1), preferred_element_type=jnp.float32
            )
        for d in st:
            back_re = d["back"][:, 0:128]
            back_im = d["back"][:, 128:256]
            ctf, coef_re, coef_im, keep, cls = d["ctf"], d["coef_re"], d["coef_im"], d["keep"], d["cls"]
            term_re = ctf * (coef_re * back_re - coef_im * back_im)
            term_im = ctf * (coef_re * back_im + coef_im * back_re)
            total_ref[cls, 0] = total_ref[cls, 0] + term_re * keep
            total_ref[cls, 1] = total_ref[cls, 1] + term_im * keep
            total_ref[cls, 2] = total_ref[cls, 2] + ctf * ctf * keep


def group_eval(meta, order, coef, refs, ctf_tab, pack, group, interpret=False):
    slots = coef.shape[0]
    per_owner = refs.shape[0]
    win = coef.shape[3]
    rows_sent = coef.shape[2]
    bins = ctf_tab.shape[0]
    table = jnp.concatenate([meta, order[None]], axis=0)

    def coef_map(j):
        return lambda g, table: (table[5, g * group + j], 0, 0, 0)

    grid_spec = pltpu.PrefetchScalarGridSpec(
        num_scalar_prefetch=1,
        grid=(slots // group,),
        in_specs=[pl.BlockSpec((1, 2, rows_sent, win), coef_map(j)) for j in range(group)]
        + [
            pl.BlockSpec((per_owner, 2, win, win), lambda g, table: (0, 0, 0, 0)),
            pl.BlockSpec((bins, win, win), lambda g, table: (0, 0, 0)),
            pl.BlockSpec((group, 4, win, win), lambda g, table: (g, 0, 0, 0)),
        ],
        out_specs=[
            pl.BlockSpec((per_owner, 3, win, win), lambda g, table: (0, 0, 0, 0)),
            pl.BlockSpec((group, 8, 128), lambda g, table: (g, 0, 0)),
        ],
    )
    return pl.pallas_call(
        _group_kernel,
        grid_spec=grid_spec,
        out_shape=[
            jax.ShapeDtypeStruct((per_owner, 3, win, win), jnp.float32),
            jax.ShapeDtypeStruct((slots, 8, 128), jnp.float32),
        ],
        compiler_params=pltpu.CompilerParams(dimension_semantics=("arbitrary",)),
        interpret=interpret,
    )(table, *([coef] * group), refs, ctf_tab, pack)


def phase_rows(anchor, img_side, win_side):
    shifts = anchor[:, None] + jnp.arange(TW, dtype=jnp.int32)[None, :] - TW // 2
    phase_int = shifts[:, :, None] * freq_ids(win_side)[None, None, :] % img_side
    angles = phase_int.astype(jnp.float32) * (2.0 * math.pi / img_side)
    return jnp.concatenate(
        [jnp.cos(angles).astype(jnp.bfloat16), jnp.sin(angles).astype(jnp.bfloat16)], axis=1
    )


def phase_pack(tag_flat, img_side, win_side):
    rows_t = phase_rows(tag_flat[:, 2], img_side, win_side)
    cols_t = phase_rows(tag_flat[:, 3], img_side, win_side)
    cols_bt = jnp.concatenate([-cols_t[:, TW:], cols_t[:, :TW]], axis=1)
    spare = jnp.zeros((rows_t.shape[0], win_side - 4 * TW, win_side), jnp.bfloat16)
    flat = jnp.concatenate([rows_t, cols_t, spare], axis=1)
    rows3 = jnp.concatenate([rows_t, rows_t, rows_t], axis=1)
    planes = [
        jnp.pad(jnp.swapaxes(t, 1, 2), ((0, 0), (0, 0), (0, win_side - t.shape[1])))
        for t in (rows3, cols_t, cols_bt)
    ]
    return jnp.stack(planes + [flat], axis=1)


def on_device(images, references, particle_class, rotation, defocus_bin, window_anchor):
    part_count = images.shape[0]
    img_side = images.shape[1]
    win_side = references.shape[2]
    per_owner = references.shape[0]
    owners = lax.axis_size("dom")
    capacity = max(2, 2 * part_count // owners)
    slot_count = owners * capacity
    target = particle_class // per_owner
    local_class = particle_class - target * per_owner
    positions = jnp.arange(part_count, dtype=jnp.int32)
    same_owner = (target[:, None] == target[None, :]) & (positions[None, :] < positions[:, None])
    slot_rank = jnp.sum(same_owner.astype(jnp.int32), axis=1)
    slot_place = target * capacity + slot_rank
    slot_tags = jnp.stack(
        [local_class + 1, defocus_bin, window_anchor[0], window_anchor[1]], axis=1
    ).astype(jnp.bfloat16)
    tag_buffer = (
        jnp.zeros((slot_count, 4), jnp.bfloat16)
        .at[slot_place]
        .set(slot_tags)
        .reshape(owners, capacity, 4)
    )
    dft_cos, dft_sin = dft_tables(img_side, win_side)
    fourier_own = transform(images, rotation, dft_cos, dft_sin)
    half = win_side // 2
    edge = fourier_own[:, :, half + 1 :, 0]
    edge = jnp.pad(edge, ((0, 0), (0, 0), (0, win_side - edge.shape[2])))
    compact = jnp.concatenate([fourier_own[:, :, : half + 1, :], edge[:, :, None, :]], axis=2)
    hits = (slot_place[None, :] == jnp.arange(slot_count, dtype=jnp.int32)[:, None]).astype(jnp.bfloat16)
    buffer = jnp.einsum("qi,irjk->qrjk", hits, compact)
    buffer = buffer.reshape(owners, capacity, 2, half + 2, win_side)
    coeff_block = lax.all_to_all(buffer, "dom", split_axis=0, concat_axis=0, tiled=True)
    ctf_bins = ctf_table(jnp.arange(16, dtype=jnp.int32), win_side)
    tag_block = lax.all_to_all(tag_buffer, "dom", split_axis=0, concat_axis=0, tiled=True)
    tag_flat = tag_block.reshape(slot_count, 4).astype(jnp.int32)
    live = (tag_flat[:, 0] > 0).astype(jnp.int32)
    order = jnp.argsort(1 - live, stable=True).astype(jnp.int32)
    tag_sorted = tag_flat[order]
    count = jnp.sum(live)
    meta = jnp.concatenate(
        [tag_sorted.T, jnp.full((1, slot_count), count, jnp.int32)], axis=0
    )
    pack = phase_pack(tag_sorted, img_side, win_side)
    group = 8 if slot_count % 8 == 0 else 1
    partial_value, info_sorted = group_eval(
        meta,
        order,
        coeff_block.reshape(slot_count, 2, win_side // 2 + 2, win_side),
        references,
        ctf_bins,
        pack,
        group,
    )
    info = jnp.zeros((slot_count, 3), jnp.float32).at[order].set(info_sorted[:, 0, :3])
    returned = lax.all_to_all(
        info.reshape(owners, capacity, 3), "dom", split_axis=0, concat_axis=0, tiled=True
    )
    summed = lax.psum_scatter(partial_value, "cls", scatter_dimension=2, tiled=True)
    divisor = summed[:, 2] + ridge_term
    new_refs = summed[:, :2] / divisor[:, None]
    particle_info = returned.reshape(slot_count, 3)[slot_place]
    return (new_refs, particle_info.T)


def solution(mesh):
    return jax.shard_map(
        on_device,
        mesh=mesh,
        in_specs=(
            P(("copies", "dom", "cls"), None, None),
            P(("copies", "dom"), None, None, None),
            P(("copies", "dom", "cls")),
            P(("copies", "dom", "cls")),
            P(("copies", "dom", "cls")),
            P(None, ("copies", "dom", "cls")),
        ),
        out_specs=(P(("copies", "dom"), None, "cls", None), P(None, ("copies", "dom", "cls"))),
        check_vma=False,
    )
```

```python
import math

import jax
import jax.numpy as jnp
from jax import lax
from jax.experimental import pallas as pl
from jax.experimental.pallas import tpu as pltpu
from jax.sharding import PartitionSpec as P


TW = 8


score_scale = 0.02
ridge_term = 1.0


def freq_ids(win_side):
    return jnp.arange(win_side, dtype=jnp.int32) - win_side // 2


def dft_tables(img_side, win_side):
    phase_int = (
        freq_ids(win_side)[:, None] * jnp.arange(img_side, dtype=jnp.int32)[None, :] % img_side
    )
    angles = phase_int.astype(jnp.float32) * (2.0 * math.pi / img_side)
    scale_by = 1.0 / math.sqrt(img_side)
    return (
        (jnp.cos(angles) * scale_by).astype(jnp.bfloat16),
        (-jnp.sin(angles) * scale_by).astype(jnp.bfloat16),
    )


def ctf_table(bin_ids, win_side):
    freqs = freq_ids(win_side).astype(jnp.float32)
    radius = (freqs[:, None] * freqs[:, None] + freqs[None, :] * freqs[None, :]) / float(
        win_side * win_side
    )
    strength = 20.0 + 6.0 * bin_ids.astype(jnp.float32)
    return -jnp.sin(strength[:, None, None] * radius[None, :, :] + 0.1)


def transform(images, rot_ids, dft_cos, dft_sin):
    win_side = dft_cos.shape[0]
    stacked = jnp.concatenate([dft_cos, dft_sin], axis=0)
    flag_bits = rot_ids[:, None, None]
    col_table = jnp.where(flag_bits & 2 != 0, stacked[None, :, ::-1], stacked[None])
    plain = jnp.einsum("nyx,nkx->nyk", images, col_table, preferred_element_type=jnp.float32)
    turned = jnp.einsum("nxy,nkx->nyk", images, col_table, preferred_element_type=jnp.float32)
    half_done = jnp.where(flag_bits & 4 != 0, turned, plain).astype(jnp.bfloat16)
    row_cos = jnp.where(flag_bits & 1 != 0, dft_cos[None, :, ::-1], dft_cos[None])
    row_sin = jnp.where(flag_bits & 1 != 0, dft_sin[None, :, ::-1], dft_sin[None])
    from_cos = jnp.einsum("njy,nyk->njk", row_cos, half_done, preferred_element_type=jnp.float32)
    from_sin = jnp.einsum("njy,nyk->njk", row_sin, half_done, preferred_element_type=jnp.float32)
    real_part = from_cos[..., :win_side] - from_sin[..., win_side:]
    imag_part = from_cos[..., win_side:] + from_sin[..., :win_side]
    return jnp.stack([real_part, imag_part], axis=1).astype(jnp.bfloat16)


def _split3(value):
    high = value.astype(jnp.bfloat16)
    rest = value - high.astype(jnp.float32)
    middle = rest.astype(jnp.bfloat16)
    low = (rest - middle.astype(jnp.float32)).astype(jnp.bfloat16)
    return high, middle, low


def _group_kernel(meta_ref, *refs):
    group = len(refs) - 6
    coef_refs = refs[:group]
    ref_ref, ctf_ref, pack_ref, flat_ref, total_ref, info_ref = refs[group:]
    g = pl.program_id(0)
    span = 8
    per_owner = ref_ref.shape[0]
    bins = ctf_ref.shape[0]

    @pl.when(g == 0)
    def _():
        total_ref[...] = jnp.zeros(total_ref.shape, total_ref.dtype)

    info_ref[...] = jnp.zeros(info_ref.shape, info_ref.dtype)

    @pl.when(g * group < meta_ref[4, 0])
    def _():
        lane = lax.broadcasted_iota(jnp.int32, (8, 128), 1)
        sub = lax.broadcasted_iota(jnp.int32, (8, 128), 0)
        inside = lane < span
        win = ctf_ref.shape[1]
        half = win // 2
        row = lax.broadcasted_iota(jnp.int32, (win, win), 0)
        col = lax.broadcasted_iota(jnp.int32, (win, win), 1)
        mirror = (col == (win - row) % win).astype(jnp.bfloat16)
        pick = (col == row - half - 1).astype(jnp.bfloat16)
        upper_rows = row <= half
        edge = (row > half) & (col == 0)
        kept = []
        for j in range(group):
            block = coef_refs[j][0]
            spare = jnp.zeros((win - block.shape[1], win), jnp.bfloat16)
            full_re = jnp.concatenate([block[0], spare], axis=0)
            full_im = jnp.concatenate([block[1], spare], axis=0)
            zero = jnp.zeros((), jnp.bfloat16)
            top_re = jnp.where(upper_rows, full_re, zero)
            top_im = jnp.where(upper_rows, full_im, zero)
            turned = jnp.dot(
                mirror, jnp.concatenate([top_re, top_im], axis=1), preferred_element_type=jnp.float32
            ).astype(jnp.bfloat16)
            stacked = jnp.concatenate([turned[:, 0:win], turned[:, win : 2 * win]], axis=0)
            flipped = jnp.dot(stacked, mirror, preferred_element_type=jnp.float32)
            column = lax.dot_general(
                pick, jnp.concatenate([full_re, full_im], axis=0), (((1,), (1,)), ((), ())),
                preferred_element_type=jnp.float32,
            )
            col_re = pltpu.roll(column[:, 0:win], win - half - 1, 1)
            col_im = pltpu.roll(column[:, win : 2 * win], win - half - 1, 1)
            coef_re = jnp.where(edge, col_re, jnp.where(upper_rows, top_re.astype(jnp.float32), flipped[0:win]))
            coef_im = jnp.where(edge, col_im, jnp.where(upper_rows, top_im.astype(jnp.float32), -flipped[win : 2 * win]))
            kept.append((coef_re, coef_im))
        st = []
        for j in range(group):
            slot = g * group + j
            tag = meta_ref[0, slot]
            cls = jnp.minimum(jnp.maximum(tag - 1, 0), per_owner - 1)
            bin_id = jnp.minimum(jnp.maximum(meta_ref[1, slot], 0), bins - 1)
            keep = (jnp.full((1, 128), tag, jnp.int32) > 0).astype(jnp.float32)
            coef_re, coef_im = kept[j]
            ctf = ctf_ref[bin_id]
            pred_re = ctf * ref_ref[cls, 0].astype(jnp.float32)
            pred_im = ctf * ref_ref[cls, 1].astype(jnp.float32)
            prod_re = (coef_re * pred_re + coef_im * pred_im).astype(jnp.bfloat16)
            prod_im = (coef_im * pred_re - coef_re * pred_im).astype(jnp.bfloat16)
            both = jnp.concatenate([prod_re, prod_im], axis=1)
            lanes = pack_ref[j].astype(jnp.float32)
            wide = lax.broadcasted_iota(jnp.int32, lanes.shape, 1)
            zero = jnp.zeros((), jnp.float32)
            cols = jnp.where(wide < 2 * span, pltpu.roll(lanes, 128 - 6 * span, 1), zero)
            cols_b = jnp.where(wide < 2 * span, pltpu.roll(lanes, 128 - 8 * span, 1), zero)
            mix = jnp.concatenate([cols, cols_b], axis=0).astype(jnp.bfloat16)
            part = jnp.dot(both, mix, preferred_element_type=jnp.float32)
            st.append(dict(slot=slot, cls=cls, keep=keep, ctf=ctf, coef_re=coef_re, coef_im=coef_im, part=part))
        for j, d in enumerate(st):
            p_hi, p_mid, p_lo = [piece.astype(jnp.float32) for piece in _split3(d["part"])]
            packed = (p_hi + pltpu.roll(p_mid, 2 * span, 1) + pltpu.roll(p_lo, 4 * span, 1)).astype(jnp.bfloat16)
            d["corr3"] = jnp.dot(flat_ref[j][0:16], packed, preferred_element_type=jnp.float32)
        for j, d in enumerate(st):
            corr3 = d["corr3"]
            corr = (corr3 + pltpu.roll(corr3, 128 - 2 * span, 1)) + pltpu.roll(corr3, 128 - 4 * span, 1)
            upper = corr[0:8]
            lower = pltpu.roll(corr[8:16], 128 - span, 1)
            score = jnp.where(inside, score_scale * (upper - lower), -jnp.inf)
            peak = jnp.max(jnp.max(score, axis=1, keepdims=True), axis=0, keepdims=True)
            total = jnp.sum(jnp.sum(jnp.exp(score - peak), axis=1, keepdims=True), axis=0, keepdims=True)
            evidence = peak + jnp.log(total)
            weight = jnp.where(inside, jnp.exp(score - evidence), 0.0)
            slot = d["slot"]
            row_shift = (jnp.full((8, 128), meta_ref[2, slot], jnp.int32) + sub - span // 2).astype(jnp.float32)
            col_shift = (jnp.full((8, 128), meta_ref[3, slot], jnp.int32) + lane - span // 2).astype(jnp.float32)
            by_row = jnp.sum(weight, axis=1, keepdims=True)
            mean_row = jnp.sum(by_row * row_shift[:, 0:1], axis=0, keepdims=True)
            by_col = jnp.sum(weight, axis=0, keepdims=True)
            mean_col = jnp.sum(jnp.where(inside[0:1], by_col * col_shift[0:1], 0.0), axis=1, keepdims=True)
            info_ref[j] = jnp.where(
                sub == 0,
                jnp.where(lane == 0, evidence, jnp.where(lane == 1, mean_row, jnp.where(lane == 2, mean_col, 0.0))),
                0.0,
            )
            shifted = pltpu.roll(weight, span, 1)
            stacked_w = jnp.concatenate([weight, shifted], axis=0)
            pad = jnp.zeros((112, 128), jnp.bfloat16)
            col_rows = jnp.concatenate([flat_ref[j][16:32], pad], axis=0)
            w_pieces = jnp.concatenate(_split3(stacked_w), axis=0)
            d["q3"] = jnp.dot(w_pieces, col_rows, preferred_element_type=jnp.float32)
        for j, d in enumerate(st):
            q3 = d["q3"]
            qpart = (q3[0:16] + q3[16:32]) + q3[32:48]
            q_re = qpart[0:8]
            q_im = qpart[8:16]
            spare = jnp.zeros((80, 128), jnp.bfloat16)
            rhs_re = jnp.concatenate(list(_split3(jnp.concatenate([q_re, -q_im], axis=0))) + [spare], axis=0)
            rhs_im = jnp.concatenate(list(_split3(jnp.concatenate([q_im, q_re], axis=0))) + [spare], axis=0)
            lanes = pack_ref[j]
            wide = lax.broadcasted_iota(jnp.int32, lanes.shape, 1)
            rows3 = jnp.where(wide < 6 * span, lanes, jnp.zeros((), jnp.bfloat16))
            d["back"] = jnp.dot(
                rows3, jnp.concatenate([rhs_re, rhs_im], axis=1), preferred_element_type=jnp.float32
            )
        for d in st:
            back_re = d["back"][:, 0:128]
            back_im = d["back"][:, 128:256]
            ctf, coef_re, coef_im, keep, cls = d["ctf"], d["coef_re"], d["coef_im"], d["keep"], d["cls"]
            term_re = ctf * (coef_re * back_re - coef_im * back_im)
            term_im = ctf * (coef_re * back_im + coef_im * back_re)
            total_ref[cls, 0] = total_ref[cls, 0] + term_re * keep
            total_ref[cls, 1] = total_ref[cls, 1] + term_im * keep
            total_ref[cls, 2] = total_ref[cls, 2] + ctf * ctf * keep


def group_eval(meta, order, coef, refs, ctf_tab, pack, flat, group, interpret=False):
    slots = coef.shape[0]
    per_owner = refs.shape[0]
    win = coef.shape[3]
    rows_sent = coef.shape[2]
    bins = ctf_tab.shape[0]
    table = jnp.concatenate([meta, order[None]], axis=0)

    def coef_map(j):
        return lambda g, table: (table[5, g * group + j], 0, 0, 0)

    grid_spec = pltpu.PrefetchScalarGridSpec(
        num_scalar_prefetch=1,
        grid=(slots // group,),
        in_specs=[pl.BlockSpec((1, 2, rows_sent, win), coef_map(j)) for j in range(group)]
        + [
            pl.BlockSpec((per_owner, 2, win, win), lambda g, table: (0, 0, 0, 0)),
            pl.BlockSpec((bins, win, win), lambda g, table: (0, 0, 0)),
            pl.BlockSpec((group, win, win), lambda g, table: (g, 0, 0)),
            pl.BlockSpec((group, flat.shape[1], win), lambda g, table: (g, 0, 0)),
        ],
        out_specs=[
            pl.BlockSpec((per_owner, 3, win, win), lambda g, table: (0, 0, 0, 0)),
            pl.BlockSpec((group, 8, 128), lambda g, table: (g, 0, 0)),
        ],
    )
    return pl.pallas_call(
        _group_kernel,
        grid_spec=grid_spec,
        out_shape=[
            jax.ShapeDtypeStruct((per_owner, 3, win, win), jnp.float32),
            jax.ShapeDtypeStruct((slots, 8, 128), jnp.float32),
        ],
        compiler_params=pltpu.CompilerParams(dimension_semantics=("arbitrary",)),
        interpret=interpret,
    )(table, *([coef] * group), refs, ctf_tab, pack, flat)


def phase_rows(anchor, img_side, win_side):
    shifts = anchor[:, None] + jnp.arange(TW, dtype=jnp.int32)[None, :] - TW // 2
    phase_int = shifts[:, :, None] * freq_ids(win_side)[None, None, :] % img_side
    angles = phase_int.astype(jnp.float32) * (2.0 * math.pi / img_side)
    return jnp.concatenate(
        [jnp.cos(angles).astype(jnp.bfloat16), jnp.sin(angles).astype(jnp.bfloat16)], axis=1
    )


def phase_pack(tag_flat, img_side, win_side):
    rows_t = phase_rows(tag_flat[:, 2], img_side, win_side)
    cols_t = phase_rows(tag_flat[:, 3], img_side, win_side)
    cols_bt = jnp.concatenate([-cols_t[:, TW:], cols_t[:, :TW]], axis=1)
    flat = jnp.concatenate([rows_t, cols_t], axis=1)
    stacked = jnp.concatenate([rows_t, rows_t, rows_t, cols_t, cols_bt], axis=1)
    stacked = jnp.pad(stacked, ((0, 0), (0, win_side - stacked.shape[1]), (0, 0)))
    return jnp.swapaxes(stacked, 1, 2), flat[:, : 4 * TW]


def on_device(images, references, particle_class, rotation, defocus_bin, window_anchor):
    part_count = images.shape[0]
    img_side = images.shape[1]
    win_side = references.shape[2]
    per_owner = references.shape[0]
    owners = lax.axis_size("dom")
    capacity = max(2, 2 * part_count // owners)
    slot_count = owners * capacity
    target = particle_class // per_owner
    local_class = particle_class - target * per_owner
    positions = jnp.arange(part_count, dtype=jnp.int32)
    same_owner = (target[:, None] == target[None, :]) & (positions[None, :] < positions[:, None])
    slot_rank = jnp.sum(same_owner.astype(jnp.int32), axis=1)
    slot_place = target * capacity + slot_rank
    slot_tags = jnp.stack(
        [local_class + 1, defocus_bin, window_anchor[0], window_anchor[1]], axis=1
    ).astype(jnp.bfloat16)
    tag_buffer = (
        jnp.zeros((slot_count, 4), jnp.bfloat16)
        .at[slot_place]
        .set(slot_tags)
        .reshape(owners, capacity, 4)
    )
    dft_cos, dft_sin = dft_tables(img_side, win_side)
    fourier_own = transform(images, rotation, dft_cos, dft_sin)
    half = win_side // 2
    edge = fourier_own[:, :, half + 1 :, 0]
    edge = jnp.pad(edge, ((0, 0), (0, 0), (0, win_side - edge.shape[2])))
    compact = jnp.concatenate([fourier_own[:, :, : half + 1, :], edge[:, :, None, :]], axis=2)
    hits = (slot_place[None, :] == jnp.arange(slot_count, dtype=jnp.int32)[:, None]).astype(jnp.bfloat16)
    buffer = jnp.einsum("qi,irjk->qrjk", hits, compact)
    buffer = buffer.reshape(owners, capacity, 2, half + 2, win_side)
    coeff_block = lax.all_to_all(buffer, "dom", split_axis=0, concat_axis=0, tiled=True)
    ctf_bins = ctf_table(jnp.arange(16, dtype=jnp.int32), win_side)
    tag_block = lax.all_to_all(tag_buffer, "dom", split_axis=0, concat_axis=0, tiled=True)
    tag_flat = tag_block.reshape(slot_count, 4).astype(jnp.int32)
    live = (tag_flat[:, 0] > 0).astype(jnp.int32)
    order = jnp.argsort(1 - live, stable=True).astype(jnp.int32)
    tag_sorted = tag_flat[order]
    count = jnp.sum(live)
    meta = jnp.concatenate(
        [tag_sorted.T, jnp.full((1, slot_count), count, jnp.int32)], axis=0
    )
    pack, flat = phase_pack(tag_sorted, img_side, win_side)
    group = 8 if slot_count % 8 == 0 else 1
    partial_value, info_sorted = group_eval(
        meta,
        order,
        coeff_block.reshape(slot_count, 2, win_side // 2 + 2, win_side),
        references,
        ctf_bins,
        pack,
        flat,
        group,
    )
    info = jnp.zeros((slot_count, 3), jnp.float32).at[order].set(info_sorted[:, 0, :3])
    returned = lax.all_to_all(
        info.reshape(owners, capacity, 3), "dom", split_axis=0, concat_axis=0, tiled=True
    )
    summed = lax.psum_scatter(partial_value, "cls", scatter_dimension=2, tiled=True)
    divisor = summed[:, 2] + ridge_term
    new_refs = summed[:, :2] / divisor[:, None]
    particle_info = returned.reshape(slot_count, 3)[slot_place]
    return (new_refs, particle_info.T)


def solution(mesh):
    return jax.shard_map(
        on_device,
        mesh=mesh,
        in_specs=(
            P(("copies", "dom", "cls"), None, None),
            P(("copies", "dom"), None, None, None),
            P(("copies", "dom", "cls")),
            P(("copies", "dom", "cls")),
            P(("copies", "dom", "cls")),
            P(None, ("copies", "dom", "cls")),
        ),
        out_specs=(P(("copies", "dom"), None, "cls", None), P(None, ("copies", "dom", "cls"))),
        check_vma=False,
    )
```

```python
import math

import jax
import jax.numpy as jnp
from jax import lax
from jax.experimental import pallas as pl
from jax.experimental.pallas import tpu as pltpu
from jax.sharding import PartitionSpec as P


TW = 8


score_scale = 0.02
ridge_term = 1.0


def freq_ids(win_side):
    return jnp.arange(win_side, dtype=jnp.int32) - win_side // 2


def dft_tables(img_side, win_side):
    phase_int = (
        freq_ids(win_side)[:, None] * jnp.arange(img_side, dtype=jnp.int32)[None, :] % img_side
    )
    angles = phase_int.astype(jnp.float32) * (2.0 * math.pi / img_side)
    scale_by = 1.0 / math.sqrt(img_side)
    return (
        (jnp.cos(angles) * scale_by).astype(jnp.bfloat16),
        (-jnp.sin(angles) * scale_by).astype(jnp.bfloat16),
    )


def ctf_table(bin_ids, win_side):
    freqs = freq_ids(win_side).astype(jnp.float32)
    radius = (freqs[:, None] * freqs[:, None] + freqs[None, :] * freqs[None, :]) / float(
        win_side * win_side
    )
    strength = 20.0 + 6.0 * bin_ids.astype(jnp.float32)
    return -jnp.sin(strength[:, None, None] * radius[None, :, :] + 0.1)


def transform(images, rot_ids, dft_cos, dft_sin):
    win_side = dft_cos.shape[0]
    stacked = jnp.concatenate([dft_cos, dft_sin], axis=0)
    flag_bits = rot_ids[:, None, None]
    col_table = jnp.where(flag_bits & 2 != 0, stacked[None, :, ::-1], stacked[None])
    plain = jnp.einsum("nyx,nkx->nyk", images, col_table, preferred_element_type=jnp.float32)
    turned = jnp.einsum("nxy,nkx->nyk", images, col_table, preferred_element_type=jnp.float32)
    half_done = jnp.where(flag_bits & 4 != 0, turned, plain).astype(jnp.bfloat16)
    row_cos = jnp.where(flag_bits & 1 != 0, dft_cos[None, :, ::-1], dft_cos[None])
    row_sin = jnp.where(flag_bits & 1 != 0, dft_sin[None, :, ::-1], dft_sin[None])
    from_cos = jnp.einsum("njy,nyk->njk", row_cos, half_done, preferred_element_type=jnp.float32)
    from_sin = jnp.einsum("njy,nyk->njk", row_sin, half_done, preferred_element_type=jnp.float32)
    real_part = from_cos[..., :win_side] - from_sin[..., win_side:]
    imag_part = from_cos[..., win_side:] + from_sin[..., :win_side]
    return jnp.stack([real_part, imag_part], axis=1).astype(jnp.bfloat16)


def _split3(value):
    high = value.astype(jnp.bfloat16)
    rest = value - high.astype(jnp.float32)
    middle = rest.astype(jnp.bfloat16)
    low = (rest - middle.astype(jnp.float32)).astype(jnp.bfloat16)
    return high, middle, low


def _group_kernel(meta_ref, *refs):
    group = len(refs) - 6
    coef_refs = refs[:group]
    ref_ref, ctf_ref, pack_ref, flat_ref, total_ref, info_ref = refs[group:]
    g = pl.program_id(0)
    span = 8
    per_owner = ref_ref.shape[0]
    bins = ctf_ref.shape[0]

    @pl.when(g == 0)
    def _():
        total_ref[...] = jnp.zeros(total_ref.shape, total_ref.dtype)

    info_ref[...] = jnp.zeros(info_ref.shape, info_ref.dtype)

    @pl.when(g * group < meta_ref[4, 0])
    def _():
        lane = lax.broadcasted_iota(jnp.int32, (8, 128), 1)
        sub = lax.broadcasted_iota(jnp.int32, (8, 128), 0)
        inside = lane < span
        win = ctf_ref.shape[1]
        half = win // 2
        row = lax.broadcasted_iota(jnp.int32, (win, win), 0)
        col = lax.broadcasted_iota(jnp.int32, (win, win), 1)
        mirror = (col == (win - row) % win).astype(jnp.bfloat16)
        pick = (col == row - half - 1).astype(jnp.bfloat16)
        upper_rows = row <= half
        edge = (row > half) & (col == 0)
        kept = []
        for j in range(group):
            block = coef_refs[j][0]
            spare = jnp.zeros((win - block.shape[1], win), jnp.bfloat16)
            full_re = jnp.concatenate([block[0], spare], axis=0)
            full_im = jnp.concatenate([block[1], spare], axis=0)
            zero = jnp.zeros((), jnp.bfloat16)
            top_re = jnp.where(upper_rows, full_re, zero)
            top_im = jnp.where(upper_rows, full_im, zero)
            turned = jnp.dot(
                mirror, jnp.concatenate([top_re, top_im], axis=1), preferred_element_type=jnp.float32
            ).astype(jnp.bfloat16)
            stacked = jnp.concatenate([turned[:, 0:win], turned[:, win : 2 * win]], axis=0)
            flipped = jnp.dot(stacked, mirror, preferred_element_type=jnp.float32)
            column = lax.dot_general(
                pick, jnp.concatenate([full_re, full_im], axis=0), (((1,), (1,)), ((), ())),
                preferred_element_type=jnp.float32,
            )
            col_re = pltpu.roll(column[:, 0:win], win - half - 1, 1)
            col_im = pltpu.roll(column[:, win : 2 * win], win - half - 1, 1)
            coef_re = jnp.where(edge, col_re, jnp.where(upper_rows, top_re.astype(jnp.float32), flipped[0:win]))
            coef_im = jnp.where(edge, col_im, jnp.where(upper_rows, top_im.astype(jnp.float32), -flipped[win : 2 * win]))
            kept.append((coef_re, coef_im))
        st = []
        for j in range(group):
            slot = g * group + j
            tag = meta_ref[0, slot]
            cls = jnp.minimum(jnp.maximum(tag - 1, 0), per_owner - 1)
            bin_id = jnp.minimum(jnp.maximum(meta_ref[1, slot], 0), bins - 1)
            keep = (jnp.full((1, 128), tag, jnp.int32) > 0).astype(jnp.float32)
            coef_re, coef_im = kept[j]
            ctf = ctf_ref[bin_id]
            pred_re = ctf * ref_ref[cls, 0].astype(jnp.float32)
            pred_im = ctf * ref_ref[cls, 1].astype(jnp.float32)
            prod_re = (coef_re * pred_re + coef_im * pred_im).astype(jnp.bfloat16)
            prod_im = (coef_im * pred_re - coef_re * pred_im).astype(jnp.bfloat16)
            both = jnp.concatenate([prod_re, prod_im], axis=1)
            lanes = pack_ref[j].astype(jnp.float32)
            wide = lax.broadcasted_iota(jnp.int32, lanes.shape, 1)
            zero = jnp.zeros((), jnp.float32)
            cols = jnp.where(wide < 2 * span, pltpu.roll(lanes, 128 - 6 * span, 1), zero)
            cols_b = jnp.where(wide < 2 * span, pltpu.roll(lanes, 128 - 8 * span, 1), zero)
            mix = jnp.concatenate([cols, cols_b], axis=0).astype(jnp.bfloat16)
            part = jnp.dot(both, mix, preferred_element_type=jnp.float32)
            st.append(dict(slot=slot, cls=cls, keep=keep, ctf=ctf, coef_re=coef_re, coef_im=coef_im, part=part))
        for j, d in enumerate(st):
            p_hi, p_mid, p_lo = [piece.astype(jnp.float32) for piece in _split3(d["part"])]
            packed = (p_hi + pltpu.roll(p_mid, 2 * span, 1) + pltpu.roll(p_lo, 4 * span, 1)).astype(jnp.bfloat16)
            d["corr3"] = jnp.dot(flat_ref[j][0:16], packed, preferred_element_type=jnp.float32)
        for j, d in enumerate(st):
            corr3 = d["corr3"]
            corr = (corr3 + pltpu.roll(corr3, 128 - 2 * span, 1)) + pltpu.roll(corr3, 128 - 4 * span, 1)
            upper = corr[0:8]
            lower = pltpu.roll(corr[8:16], 128 - span, 1)
            score = jnp.where(inside, score_scale * (upper - lower), -jnp.inf)
            peak = jnp.max(jnp.max(score, axis=1, keepdims=True), axis=0, keepdims=True)
            total = jnp.sum(jnp.sum(jnp.exp(score - peak), axis=1, keepdims=True), axis=0, keepdims=True)
            evidence = peak + jnp.log(total)
            weight = jnp.where(inside, jnp.exp(score - evidence), 0.0)
            slot = d["slot"]
            row_shift = (jnp.full((8, 128), meta_ref[2, slot], jnp.int32) + sub - span // 2).astype(jnp.float32)
            col_shift = (jnp.full((8, 128), meta_ref[3, slot], jnp.int32) + lane - span // 2).astype(jnp.float32)
            by_row = jnp.sum(weight, axis=1, keepdims=True)
            mean_row = jnp.sum(by_row * row_shift[:, 0:1], axis=0, keepdims=True)
            by_col = jnp.sum(weight, axis=0, keepdims=True)
            mean_col = jnp.sum(jnp.where(inside[0:1], by_col * col_shift[0:1], 0.0), axis=1, keepdims=True)
            info_ref[j] = jnp.where(
                sub == 0,
                jnp.where(lane == 0, evidence, jnp.where(lane == 1, mean_row, jnp.where(lane == 2, mean_col, 0.0))),
                0.0,
            )
            shifted = pltpu.roll(weight, span, 1)
            stacked_w = jnp.concatenate([weight, shifted], axis=0)
            pad = jnp.zeros((112, 128), jnp.bfloat16)
            col_rows = jnp.concatenate([flat_ref[j][16:32], pad], axis=0)
            w_pieces = jnp.concatenate(_split3(stacked_w), axis=0)
            d["q3"] = jnp.dot(w_pieces, col_rows, preferred_element_type=jnp.float32)
        for j, d in enumerate(st):
            q3 = d["q3"]
            qpart = (q3[0:16] + q3[16:32]) + q3[32:48]
            q_re = qpart[0:8]
            q_im = qpart[8:16]
            spare = jnp.zeros((80, 128), jnp.bfloat16)
            rhs_re = jnp.concatenate(list(_split3(jnp.concatenate([q_re, -q_im], axis=0))) + [spare], axis=0)
            rhs_im = jnp.concatenate(list(_split3(jnp.concatenate([q_im, q_re], axis=0))) + [spare], axis=0)
            lanes = pack_ref[j]
            wide = lax.broadcasted_iota(jnp.int32, lanes.shape, 1)
            rows3 = jnp.where(wide < 6 * span, lanes, jnp.zeros((), jnp.bfloat16))
            d["back"] = jnp.dot(
                rows3, jnp.concatenate([rhs_re, rhs_im], axis=1), preferred_element_type=jnp.float32
            )
        for d in st:
            back_re = d["back"][:, 0:128]
            back_im = d["back"][:, 128:256]
            ctf, coef_re, coef_im, keep, cls = d["ctf"], d["coef_re"], d["coef_im"], d["keep"], d["cls"]
            term_re = ctf * (coef_re * back_re - coef_im * back_im)
            term_im = ctf * (coef_re * back_im + coef_im * back_re)
            total_ref[cls, 0] = total_ref[cls, 0] + term_re * keep
            total_ref[cls, 1] = total_ref[cls, 1] + term_im * keep
            total_ref[cls, 2] = total_ref[cls, 2] + ctf * ctf * keep


def group_eval(meta, order, coef, refs, ctf_tab, pack, flat, group, interpret=False):
    slots = coef.shape[0]
    per_owner = refs.shape[0]
    win = coef.shape[3]
    rows_sent = coef.shape[2]
    bins = ctf_tab.shape[0]
    table = jnp.concatenate([meta, order[None]], axis=0)

    def coef_map(j):
        return lambda g, table: (table[5, g * group + j], 0, 0, 0)

    grid_spec = pltpu.PrefetchScalarGridSpec(
        num_scalar_prefetch=1,
        grid=(slots // group,),
        in_specs=[pl.BlockSpec((1, 2, rows_sent, win), coef_map(j)) for j in range(group)]
        + [
            pl.BlockSpec((per_owner, 2, win, win), lambda g, table: (0, 0, 0, 0)),
            pl.BlockSpec((bins, win, win), lambda g, table: (0, 0, 0)),
            pl.BlockSpec((group, win, win), lambda g, table: (g, 0, 0)),
            pl.BlockSpec((group, flat.shape[1], win), lambda g, table: (g, 0, 0)),
        ],
        out_specs=[
            pl.BlockSpec((per_owner, 3, win, win), lambda g, table: (0, 0, 0, 0)),
            pl.BlockSpec((group, 8, 128), lambda g, table: (g, 0, 0)),
        ],
    )
    return pl.pallas_call(
        _group_kernel,
        grid_spec=grid_spec,
        out_shape=[
            jax.ShapeDtypeStruct((per_owner, 3, win, win), jnp.float32),
            jax.ShapeDtypeStruct((slots, 8, 128), jnp.float32),
        ],
        compiler_params=pltpu.CompilerParams(dimension_semantics=("arbitrary",)),
        interpret=interpret,
    )(table, *([coef] * group), refs, ctf_tab, pack, flat)


def phase_rows(anchor, img_side, win_side):
    shifts = anchor[:, None] + jnp.arange(TW, dtype=jnp.int32)[None, :] - TW // 2
    phase_int = shifts[:, :, None] * freq_ids(win_side)[None, None, :] % img_side
    angles = phase_int.astype(jnp.float32) * (2.0 * math.pi / img_side)
    return jnp.concatenate(
        [jnp.cos(angles).astype(jnp.bfloat16), jnp.sin(angles).astype(jnp.bfloat16)], axis=1
    )


def phase_pack(tag_flat, img_side, win_side):
    rows_t = phase_rows(tag_flat[:, 2], img_side, win_side)
    cols_t = phase_rows(tag_flat[:, 3], img_side, win_side)
    cols_bt = jnp.concatenate([-cols_t[:, TW:], cols_t[:, :TW]], axis=1)
    flat = jnp.concatenate([rows_t, cols_t], axis=1)
    stacked = jnp.concatenate([rows_t, rows_t, rows_t, cols_t, cols_bt], axis=1)
    stacked = jnp.pad(stacked, ((0, 0), (0, win_side - stacked.shape[1]), (0, 0)))
    return jnp.swapaxes(stacked, 1, 2), flat[:, : 4 * TW]


def on_device(images, references, particle_class, rotation, defocus_bin, window_anchor):
    part_count = images.shape[0]
    img_side = images.shape[1]
    win_side = references.shape[2]
    per_owner = references.shape[0]
    owners = lax.axis_size("dom")
    capacity = max(2, 2 * part_count // owners)
    slot_count = owners * capacity
    target = particle_class // per_owner
    local_class = particle_class - target * per_owner
    positions = jnp.arange(part_count, dtype=jnp.int32)
    same_owner = (target[:, None] == target[None, :]) & (positions[None, :] < positions[:, None])
    slot_rank = jnp.sum(same_owner.astype(jnp.int32), axis=1)
    slot_place = target * capacity + slot_rank
    slot_tags = jnp.stack(
        [local_class + 1, defocus_bin, window_anchor[0], window_anchor[1]], axis=1
    ).astype(jnp.float32)
    matches = slot_place[None, :] == jnp.arange(slot_count, dtype=jnp.int32)[:, None]
    tag_buffer = jnp.sum(
        jnp.where(matches[:, :, None], slot_tags[None, :, :], 0.0), axis=1
    ).reshape(owners, capacity, 4)
    dft_cos, dft_sin = dft_tables(img_side, win_side)
    fourier_own = transform(images, rotation, dft_cos, dft_sin)
    half = win_side // 2
    edge = fourier_own[:, :, half + 1 :, 0]
    edge = jnp.pad(edge, ((0, 0), (0, 0), (0, win_side - edge.shape[2])))
    compact = jnp.concatenate([fourier_own[:, :, : half + 1, :], edge[:, :, None, :]], axis=2)
    hits = matches.astype(jnp.bfloat16)
    buffer = jnp.einsum("qi,irjk->qrjk", hits, compact)
    buffer = buffer.reshape(owners, capacity, 2, half + 2, win_side)
    coeff_block = lax.all_to_all(buffer, "dom", split_axis=0, concat_axis=0, tiled=True)
    ctf_bins = ctf_table(jnp.arange(16, dtype=jnp.int32), win_side)
    tag_block = lax.all_to_all(tag_buffer, "dom", split_axis=0, concat_axis=0, tiled=True)
    tag_flat = tag_block.reshape(slot_count, 4).astype(jnp.int32)
    live = (tag_flat[:, 0] > 0).astype(jnp.int32)
    order = jnp.argsort(1 - live, stable=True).astype(jnp.int32)
    tag_sorted = tag_flat[order]
    count = jnp.sum(live)
    meta = jnp.concatenate(
        [tag_sorted.T, jnp.full((1, slot_count), count, jnp.int32)], axis=0
    )
    pack, flat = phase_pack(tag_sorted, img_side, win_side)
    group = 8 if slot_count % 8 == 0 else 1
    partial_value, info_sorted = group_eval(
        meta,
        order,
        coeff_block.reshape(slot_count, 2, win_side // 2 + 2, win_side),
        references,
        ctf_bins,
        pack,
        flat,
        group,
    )
    info = jnp.zeros((slot_count, 3), jnp.float32).at[order].set(info_sorted[:, 0, :3])
    returned = lax.all_to_all(
        info.reshape(owners, capacity, 3), "dom", split_axis=0, concat_axis=0, tiled=True
    )
    summed = lax.psum_scatter(partial_value, "cls", scatter_dimension=2, tiled=True)
    divisor = summed[:, 2] + ridge_term
    new_refs = summed[:, :2] / divisor[:, None]
    particle_info = returned.reshape(slot_count, 3)[slot_place]
    return (new_refs, particle_info.T)


def solution(mesh):
    return jax.shard_map(
        on_device,
        mesh=mesh,
        in_specs=(
            P(("copies", "dom", "cls"), None, None),
            P(("copies", "dom"), None, None, None),
            P(("copies", "dom", "cls")),
            P(("copies", "dom", "cls")),
            P(("copies", "dom", "cls")),
            P(None, ("copies", "dom", "cls")),
        ),
        out_specs=(P(("copies", "dom"), None, "cls", None), P(None, ("copies", "dom", "cls"))),
        check_vma=False,
    )
```

```python
import math

import jax
import jax.numpy as jnp
from jax import lax
from jax.experimental import pallas as pl
from jax.experimental.pallas import tpu as pltpu
from jax.sharding import PartitionSpec as P


TW = 8


score_scale = 0.02
ridge_term = 1.0


def freq_ids(win_side):
    return jnp.arange(win_side, dtype=jnp.int32) - win_side // 2


def dft_tables(img_side, win_side):
    phase_int = (
        freq_ids(win_side)[:, None] * jnp.arange(img_side, dtype=jnp.int32)[None, :] % img_side
    )
    angles = phase_int.astype(jnp.float32) * (2.0 * math.pi / img_side)
    scale_by = 1.0 / math.sqrt(img_side)
    return (
        (jnp.cos(angles) * scale_by).astype(jnp.bfloat16),
        (-jnp.sin(angles) * scale_by).astype(jnp.bfloat16),
    )


def ctf_table(bin_ids, win_side):
    freqs = freq_ids(win_side).astype(jnp.float32)
    radius = (freqs[:, None] * freqs[:, None] + freqs[None, :] * freqs[None, :]) / float(
        win_side * win_side
    )
    strength = 20.0 + 6.0 * bin_ids.astype(jnp.float32)
    return -jnp.sin(strength[:, None, None] * radius[None, :, :] + 0.1)


def transform(images, rot_ids, dft_cos, dft_sin):
    win_side = dft_cos.shape[0]
    stacked = jnp.concatenate([dft_cos, dft_sin], axis=0)
    flag_bits = rot_ids[:, None, None]
    col_table = jnp.where(flag_bits & 2 != 0, stacked[None, :, ::-1], stacked[None])
    plain = jnp.einsum("nyx,nkx->nyk", images, col_table, preferred_element_type=jnp.float32)
    turned = jnp.einsum("nxy,nkx->nyk", images, col_table, preferred_element_type=jnp.float32)
    half_done = jnp.where(flag_bits & 4 != 0, turned, plain).astype(jnp.bfloat16)
    row_cos = jnp.where(flag_bits & 1 != 0, dft_cos[None, :, ::-1], dft_cos[None])
    row_sin = jnp.where(flag_bits & 1 != 0, dft_sin[None, :, ::-1], dft_sin[None])
    from_cos = jnp.einsum("njy,nyk->njk", row_cos, half_done, preferred_element_type=jnp.float32)
    from_sin = jnp.einsum("njy,nyk->njk", row_sin, half_done, preferred_element_type=jnp.float32)
    real_part = from_cos[..., :win_side] - from_sin[..., win_side:]
    imag_part = from_cos[..., win_side:] + from_sin[..., :win_side]
    return jnp.stack([real_part, imag_part], axis=1).astype(jnp.bfloat16)


def _split3(value):
    high = value.astype(jnp.bfloat16)
    rest = value - high.astype(jnp.float32)
    middle = rest.astype(jnp.bfloat16)
    low = (rest - middle.astype(jnp.float32)).astype(jnp.bfloat16)
    return high, middle, low


def _group_kernel(meta_ref, *refs):
    group = len(refs) - 6
    coef_refs = refs[:group]
    ref_ref, ctf_ref, pack_ref, flat_ref, total_ref, info_ref = refs[group:]
    g = pl.program_id(0)
    span = 8
    per_owner = ref_ref.shape[0]
    bins = ctf_ref.shape[0]

    @pl.when(g == 0)
    def _():
        total_ref[...] = jnp.zeros(total_ref.shape, total_ref.dtype)

    info_ref[...] = jnp.zeros(info_ref.shape, info_ref.dtype)

    @pl.when(g * group < meta_ref[4, 0])
    def _():
        lane = lax.broadcasted_iota(jnp.int32, (8, 128), 1)
        sub = lax.broadcasted_iota(jnp.int32, (8, 128), 0)
        inside = lane < span
        win = ctf_ref.shape[1]
        half = win // 2
        row = lax.broadcasted_iota(jnp.int32, (win, win), 0)
        col = lax.broadcasted_iota(jnp.int32, (win, win), 1)
        mirror = (col == (win - row) % win).astype(jnp.bfloat16)
        pick = (col == row - half - 1).astype(jnp.bfloat16)
        upper_rows = row <= half
        edge = (row > half) & (col == 0)
        tops = []
        fulls = []
        for j in range(group):
            block = coef_refs[j][0]
            spare = jnp.zeros((win - block.shape[1], win), jnp.bfloat16)
            full_re = jnp.concatenate([block[0], spare], axis=0)
            full_im = jnp.concatenate([block[1], spare], axis=0)
            zero = jnp.zeros((), jnp.bfloat16)
            tops.append((jnp.where(upper_rows, full_re, zero), jnp.where(upper_rows, full_im, zero)))
            fulls += [full_re, full_im]
        turned_all = jnp.dot(
            mirror, jnp.concatenate([t for pair in tops for t in pair], axis=1),
            preferred_element_type=jnp.float32,
        ).astype(jnp.bfloat16)
        column_all = lax.dot_general(
            pick, jnp.concatenate(fulls, axis=0), (((1,), (1,)), ((), ())),
            preferred_element_type=jnp.float32,
        )
        pieces = [
            (tops[j][0], tops[j][1], turned_all[:, 2 * j * win : (2 * j + 2) * win],
             column_all[:, 2 * j * win : (2 * j + 2) * win])
            for j in range(group)
        ]
        stacked = jnp.concatenate(
            [part for _, _, turned, _ in pieces for part in (turned[:, 0:win], turned[:, win : 2 * win])],
            axis=0,
        )
        flipped_all = jnp.dot(stacked, mirror, preferred_element_type=jnp.float32)
        kept = []
        for j, (top_re, top_im, turned, column) in enumerate(pieces):
            flip_re = flipped_all[(2 * j) * win : (2 * j + 1) * win]
            flip_im = flipped_all[(2 * j + 1) * win : (2 * j + 2) * win]
            col_re = pltpu.roll(column[:, 0:win], win - half - 1, 1)
            col_im = pltpu.roll(column[:, win : 2 * win], win - half - 1, 1)
            coef_re = jnp.where(edge, col_re, jnp.where(upper_rows, top_re.astype(jnp.float32), flip_re))
            coef_im = jnp.where(edge, col_im, jnp.where(upper_rows, top_im.astype(jnp.float32), -flip_im))
            kept.append((coef_re, coef_im))
        st = []
        for j in range(group):
            slot = g * group + j
            tag = meta_ref[0, slot]
            cls = jnp.minimum(jnp.maximum(tag - 1, 0), per_owner - 1)
            bin_id = jnp.minimum(jnp.maximum(meta_ref[1, slot], 0), bins - 1)
            keep = (jnp.full((1, 128), tag, jnp.int32) > 0).astype(jnp.float32)
            coef_re, coef_im = kept[j]
            ctf = ctf_ref[bin_id]
            pred_re = ctf * ref_ref[cls, 0].astype(jnp.float32)
            pred_im = ctf * ref_ref[cls, 1].astype(jnp.float32)
            prod_re = (coef_re * pred_re + coef_im * pred_im).astype(jnp.bfloat16)
            prod_im = (coef_im * pred_re - coef_re * pred_im).astype(jnp.bfloat16)
            both = jnp.concatenate([prod_re, prod_im], axis=1)
            lanes = pack_ref[j].astype(jnp.float32)
            wide = lax.broadcasted_iota(jnp.int32, lanes.shape, 1)
            zero = jnp.zeros((), jnp.float32)
            cols = jnp.where(wide < 2 * span, pltpu.roll(lanes, 128 - 6 * span, 1), zero)
            cols_b = jnp.where(wide < 2 * span, pltpu.roll(lanes, 128 - 8 * span, 1), zero)
            mix = jnp.concatenate([cols, cols_b], axis=0).astype(jnp.bfloat16)
            part = jnp.dot(both, mix, preferred_element_type=jnp.float32)
            st.append(dict(slot=slot, cls=cls, keep=keep, ctf=ctf, coef_re=coef_re, coef_im=coef_im, part=part))
        for j, d in enumerate(st):
            p_hi, p_mid, p_lo = [piece.astype(jnp.float32) for piece in _split3(d["part"])]
            packed = (p_hi + pltpu.roll(p_mid, 2 * span, 1) + pltpu.roll(p_lo, 4 * span, 1)).astype(jnp.bfloat16)
            d["corr3"] = jnp.dot(flat_ref[j][0:16], packed, preferred_element_type=jnp.float32)
        for j, d in enumerate(st):
            corr3 = d["corr3"]
            corr = (corr3 + pltpu.roll(corr3, 128 - 2 * span, 1)) + pltpu.roll(corr3, 128 - 4 * span, 1)
            upper = corr[0:8]
            lower = pltpu.roll(corr[8:16], 128 - span, 1)
            score = jnp.where(inside, score_scale * (upper - lower), -jnp.inf)
            peak = jnp.max(jnp.max(score, axis=1, keepdims=True), axis=0, keepdims=True)
            total = jnp.sum(jnp.sum(jnp.exp(score - peak), axis=1, keepdims=True), axis=0, keepdims=True)
            evidence = peak + jnp.log(total)
            weight = jnp.where(inside, jnp.exp(score - evidence), 0.0)
            slot = d["slot"]
            row_shift = (jnp.full((8, 128), meta_ref[2, slot], jnp.int32) + sub - span // 2).astype(jnp.float32)
            col_shift = (jnp.full((8, 128), meta_ref[3, slot], jnp.int32) + lane - span // 2).astype(jnp.float32)
            by_row = jnp.sum(weight, axis=1, keepdims=True)
            mean_row = jnp.sum(by_row * row_shift[:, 0:1], axis=0, keepdims=True)
            by_col = jnp.sum(weight, axis=0, keepdims=True)
            mean_col = jnp.sum(jnp.where(inside[0:1], by_col * col_shift[0:1], 0.0), axis=1, keepdims=True)
            info_ref[j] = jnp.where(
                sub == 0,
                jnp.where(lane == 0, evidence, jnp.where(lane == 1, mean_row, jnp.where(lane == 2, mean_col, 0.0))),
                0.0,
            )
            shifted = pltpu.roll(weight, span, 1)
            stacked_w = jnp.concatenate([weight, shifted], axis=0)
            pad = jnp.zeros((112, 128), jnp.bfloat16)
            col_rows = jnp.concatenate([flat_ref[j][16:32], pad], axis=0)
            w_pieces = jnp.concatenate(_split3(stacked_w), axis=0)
            d["q3"] = jnp.dot(w_pieces, col_rows, preferred_element_type=jnp.float32)
        for j, d in enumerate(st):
            q3 = d["q3"]
            qpart = (q3[0:16] + q3[16:32]) + q3[32:48]
            q_re = qpart[0:8]
            q_im = qpart[8:16]
            spare = jnp.zeros((80, 128), jnp.bfloat16)
            rhs_re = jnp.concatenate(list(_split3(jnp.concatenate([q_re, -q_im], axis=0))) + [spare], axis=0)
            rhs_im = jnp.concatenate(list(_split3(jnp.concatenate([q_im, q_re], axis=0))) + [spare], axis=0)
            lanes = pack_ref[j]
            wide = lax.broadcasted_iota(jnp.int32, lanes.shape, 1)
            rows3 = jnp.where(wide < 6 * span, lanes, jnp.zeros((), jnp.bfloat16))
            d["back"] = jnp.dot(
                rows3, jnp.concatenate([rhs_re, rhs_im], axis=1), preferred_element_type=jnp.float32
            )
        for d in st:
            back_re = d["back"][:, 0:128]
            back_im = d["back"][:, 128:256]
            ctf, coef_re, coef_im, keep, cls = d["ctf"], d["coef_re"], d["coef_im"], d["keep"], d["cls"]
            term_re = ctf * (coef_re * back_re - coef_im * back_im)
            term_im = ctf * (coef_re * back_im + coef_im * back_re)
            total_ref[cls, 0] = total_ref[cls, 0] + term_re * keep
            total_ref[cls, 1] = total_ref[cls, 1] + term_im * keep
            total_ref[cls, 2] = total_ref[cls, 2] + ctf * ctf * keep


def group_eval(meta, order, coef, refs, ctf_tab, pack, flat, group, interpret=False):
    slots = coef.shape[0]
    per_owner = refs.shape[0]
    win = coef.shape[3]
    rows_sent = coef.shape[2]
    bins = ctf_tab.shape[0]
    table = jnp.concatenate([meta, order[None]], axis=0)

    def coef_map(j):
        return lambda g, table: (table[5, g * group + j], 0, 0, 0)

    grid_spec = pltpu.PrefetchScalarGridSpec(
        num_scalar_prefetch=1,
        grid=(slots // group,),
        in_specs=[pl.BlockSpec((1, 2, rows_sent, win), coef_map(j)) for j in range(group)]
        + [
            pl.BlockSpec((per_owner, 2, win, win), lambda g, table: (0, 0, 0, 0)),
            pl.BlockSpec((bins, win, win), lambda g, table: (0, 0, 0)),
            pl.BlockSpec((group, win, win), lambda g, table: (g, 0, 0)),
            pl.BlockSpec((group, flat.shape[1], win), lambda g, table: (g, 0, 0)),
        ],
        out_specs=[
            pl.BlockSpec((per_owner, 3, win, win), lambda g, table: (0, 0, 0, 0)),
            pl.BlockSpec((group, 8, 128), lambda g, table: (g, 0, 0)),
        ],
    )
    return pl.pallas_call(
        _group_kernel,
        grid_spec=grid_spec,
        out_shape=[
            jax.ShapeDtypeStruct((per_owner, 3, win, win), jnp.float32),
            jax.ShapeDtypeStruct((slots, 8, 128), jnp.float32),
        ],
        compiler_params=pltpu.CompilerParams(dimension_semantics=("arbitrary",)),
        interpret=interpret,
    )(table, *([coef] * group), refs, ctf_tab, pack, flat)


def phase_rows(anchor, img_side, win_side):
    shifts = anchor[:, None] + jnp.arange(TW, dtype=jnp.int32)[None, :] - TW // 2
    phase_int = shifts[:, :, None] * freq_ids(win_side)[None, None, :] % img_side
    angles = phase_int.astype(jnp.float32) * (2.0 * math.pi / img_side)
    return jnp.concatenate(
        [jnp.cos(angles).astype(jnp.bfloat16), jnp.sin(angles).astype(jnp.bfloat16)], axis=1
    )


def phase_pack(tag_flat, img_side, win_side):
    rows_t = phase_rows(tag_flat[:, 2], img_side, win_side)
    cols_t = phase_rows(tag_flat[:, 3], img_side, win_side)
    cols_bt = jnp.concatenate([-cols_t[:, TW:], cols_t[:, :TW]], axis=1)
    flat = jnp.concatenate([rows_t, cols_t], axis=1)
    stacked = jnp.concatenate([rows_t, rows_t, rows_t, cols_t, cols_bt], axis=1)
    stacked = jnp.pad(stacked, ((0, 0), (0, win_side - stacked.shape[1]), (0, 0)))
    return jnp.swapaxes(stacked, 1, 2), flat[:, : 4 * TW]


def on_device(images, references, particle_class, rotation, defocus_bin, window_anchor):
    part_count = images.shape[0]
    img_side = images.shape[1]
    win_side = references.shape[2]
    per_owner = references.shape[0]
    owners = lax.axis_size("dom")
    capacity = max(2, 2 * part_count // owners)
    slot_count = owners * capacity
    target = particle_class // per_owner
    local_class = particle_class - target * per_owner
    positions = jnp.arange(part_count, dtype=jnp.int32)
    same_owner = (target[:, None] == target[None, :]) & (positions[None, :] < positions[:, None])
    slot_rank = jnp.sum(same_owner.astype(jnp.int32), axis=1)
    slot_place = target * capacity + slot_rank
    slot_tags = jnp.stack(
        [local_class + 1, defocus_bin, window_anchor[0], window_anchor[1]], axis=1
    ).astype(jnp.bfloat16)
    tag_buffer = (
        jnp.zeros((slot_count, 4), jnp.bfloat16)
        .at[slot_place]
        .set(slot_tags)
        .reshape(owners, capacity, 4)
    )
    dft_cos, dft_sin = dft_tables(img_side, win_side)
    fourier_own = transform(images, rotation, dft_cos, dft_sin)
    half = win_side // 2
    edge = fourier_own[:, :, half + 1 :, 0]
    edge = jnp.pad(edge, ((0, 0), (0, 0), (0, win_side - edge.shape[2])))
    compact = jnp.concatenate([fourier_own[:, :, : half + 1, :], edge[:, :, None, :]], axis=2)
    hits = (slot_place[None, :] == jnp.arange(slot_count, dtype=jnp.int32)[:, None]).astype(jnp.bfloat16)
    buffer = jnp.einsum("qi,irjk->qrjk", hits, compact)
    buffer = buffer.reshape(owners, capacity, 2, half + 2, win_side)
    coeff_block = lax.all_to_all(buffer, "dom", split_axis=0, concat_axis=0, tiled=True)
    ctf_bins = ctf_table(jnp.arange(16, dtype=jnp.int32), win_side)
    tag_block = lax.all_to_all(tag_buffer, "dom", split_axis=0, concat_axis=0, tiled=True)
    tag_flat = tag_block.reshape(slot_count, 4).astype(jnp.int32)
    live = (tag_flat[:, 0] > 0).astype(jnp.int32)
    order = jnp.argsort(1 - live, stable=True).astype(jnp.int32)
    tag_sorted = tag_flat[order]
    count = jnp.sum(live)
    meta = jnp.concatenate(
        [tag_sorted.T, jnp.full((1, slot_count), count, jnp.int32)], axis=0
    )
    pack, flat = phase_pack(tag_sorted, img_side, win_side)
    group = 8 if slot_count % 8 == 0 else 1
    partial_value, info_sorted = group_eval(
        meta,
        order,
        coeff_block.reshape(slot_count, 2, win_side // 2 + 2, win_side),
        references,
        ctf_bins,
        pack,
        flat,
        group,
    )
    info = jnp.zeros((slot_count, 3), jnp.float32).at[order].set(info_sorted[:, 0, :3])
    returned = lax.all_to_all(
        info.reshape(owners, capacity, 3), "dom", split_axis=0, concat_axis=0, tiled=True
    )
    summed = lax.psum_scatter(partial_value, "cls", scatter_dimension=2, tiled=True)
    divisor = summed[:, 2] + ridge_term
    new_refs = summed[:, :2] / divisor[:, None]
    particle_info = returned.reshape(slot_count, 3)[slot_place]
    return (new_refs, particle_info.T)


def solution(mesh):
    return jax.shard_map(
        on_device,
        mesh=mesh,
        in_specs=(
            P(("copies", "dom", "cls"), None, None),
            P(("copies", "dom"), None, None, None),
            P(("copies", "dom", "cls")),
            P(("copies", "dom", "cls")),
            P(("copies", "dom", "cls")),
            P(None, ("copies", "dom", "cls")),
        ),
        out_specs=(P(("copies", "dom"), None, "cls", None), P(None, ("copies", "dom", "cls"))),
        check_vma=False,
    )
```

```python
import math

import jax
import jax.numpy as jnp
from jax import lax
from jax.experimental import pallas as pl
from jax.experimental.pallas import tpu as pltpu
from jax.sharding import PartitionSpec as P


TW = 8


score_scale = 0.02
ridge_term = 1.0


def freq_ids(win_side):
    return jnp.arange(win_side, dtype=jnp.int32) - win_side // 2


def dft_tables(img_side, win_side):
    phase_int = (
        freq_ids(win_side)[:, None] * jnp.arange(img_side, dtype=jnp.int32)[None, :] % img_side
    )
    angles = phase_int.astype(jnp.float32) * (2.0 * math.pi / img_side)
    scale_by = 1.0 / math.sqrt(img_side)
    return (
        (jnp.cos(angles) * scale_by).astype(jnp.bfloat16),
        (-jnp.sin(angles) * scale_by).astype(jnp.bfloat16),
    )


def ctf_table(bin_ids, win_side):
    freqs = freq_ids(win_side).astype(jnp.float32)
    radius = (freqs[:, None] * freqs[:, None] + freqs[None, :] * freqs[None, :]) / float(
        win_side * win_side
    )
    strength = 20.0 + 6.0 * bin_ids.astype(jnp.float32)
    return -jnp.sin(strength[:, None, None] * radius[None, :, :] + 0.1)


def transform(images, rot_ids, dft_cos, dft_sin):
    win_side = dft_cos.shape[0]
    stacked = jnp.concatenate([dft_cos, dft_sin], axis=0)
    flag_bits = rot_ids[:, None, None]
    col_table = jnp.where(flag_bits & 2 != 0, stacked[None, :, ::-1], stacked[None])
    plain = jnp.einsum("nyx,nkx->nyk", images, col_table, preferred_element_type=jnp.float32)
    turned = jnp.einsum("nxy,nkx->nyk", images, col_table, preferred_element_type=jnp.float32)
    half_done = jnp.where(flag_bits & 4 != 0, turned, plain).astype(jnp.bfloat16)
    row_cos = jnp.where(flag_bits & 1 != 0, dft_cos[None, :, ::-1], dft_cos[None])
    row_sin = jnp.where(flag_bits & 1 != 0, dft_sin[None, :, ::-1], dft_sin[None])
    from_cos = jnp.einsum("njy,nyk->njk", row_cos, half_done, preferred_element_type=jnp.float32)
    from_sin = jnp.einsum("njy,nyk->njk", row_sin, half_done, preferred_element_type=jnp.float32)
    real_part = from_cos[..., :win_side] - from_sin[..., win_side:]
    imag_part = from_cos[..., win_side:] + from_sin[..., :win_side]
    return jnp.stack([real_part, imag_part], axis=1).astype(jnp.bfloat16)


def _split3(value):
    high = value.astype(jnp.bfloat16)
    rest = value - high.astype(jnp.float32)
    middle = rest.astype(jnp.bfloat16)
    low = (rest - middle.astype(jnp.float32)).astype(jnp.bfloat16)
    return high, middle, low


def _group_kernel(meta_ref, *refs):
    group = len(refs) - 6
    coef_refs = refs[:group]
    ref_ref, ctf_ref, pack_ref, flat_ref, total_ref, info_ref = refs[group:]
    g = pl.program_id(0)
    span = 8
    per_owner = ref_ref.shape[0]
    bins = ctf_ref.shape[0]

    @pl.when(g == 0)
    def _():
        total_ref[...] = jnp.zeros(total_ref.shape, total_ref.dtype)

    info_ref[...] = jnp.zeros(info_ref.shape, info_ref.dtype)

    @pl.when(g * group < meta_ref[4, 0])
    def _():
        lane = lax.broadcasted_iota(jnp.int32, (8, 128), 1)
        sub = lax.broadcasted_iota(jnp.int32, (8, 128), 0)
        inside = lane < span
        win = ctf_ref.shape[1]
        half = win // 2
        row = lax.broadcasted_iota(jnp.int32, (win, win), 0)
        col = lax.broadcasted_iota(jnp.int32, (win, win), 1)
        mirror = (col == (win - row) % win).astype(jnp.bfloat16)
        pick = (col == row - half - 1).astype(jnp.bfloat16)
        upper_rows = row <= half
        edge = (row > half) & (col == 0)
        pieces = []
        for j in range(group):
            block = coef_refs[j][0]
            spare = jnp.zeros((win - block.shape[1], win), jnp.bfloat16)
            full_re = jnp.concatenate([block[0], spare], axis=0)
            full_im = jnp.concatenate([block[1], spare], axis=0)
            zero = jnp.zeros((), jnp.bfloat16)
            top_re = jnp.where(upper_rows, full_re, zero)
            top_im = jnp.where(upper_rows, full_im, zero)
            turned = jnp.dot(
                mirror, jnp.concatenate([top_re, top_im], axis=1), preferred_element_type=jnp.float32
            ).astype(jnp.bfloat16)
            column = lax.dot_general(
                pick, jnp.concatenate([full_re, full_im], axis=0), (((1,), (1,)), ((), ())),
                preferred_element_type=jnp.float32,
            )
            pieces.append((top_re, top_im, turned, column))
        stacked = jnp.concatenate(
            [part for _, _, turned, _ in pieces for part in (turned[:, 0:win], turned[:, win : 2 * win])],
            axis=0,
        )
        flipped_all = jnp.dot(stacked, mirror, preferred_element_type=jnp.float32)
        kept = []
        for j, (top_re, top_im, turned, column) in enumerate(pieces):
            flip_re = flipped_all[(2 * j) * win : (2 * j + 1) * win]
            flip_im = flipped_all[(2 * j + 1) * win : (2 * j + 2) * win]
            col_re = pltpu.roll(column[:, 0:win], win - half - 1, 1)
            col_im = pltpu.roll(column[:, win : 2 * win], win - half - 1, 1)
            coef_re = jnp.where(edge, col_re, jnp.where(upper_rows, top_re.astype(jnp.float32), flip_re))
            coef_im = jnp.where(edge, col_im, jnp.where(upper_rows, top_im.astype(jnp.float32), -flip_im))
            kept.append((coef_re, coef_im))
        st = []
        for j in range(group):
            slot = g * group + j
            tag = meta_ref[0, slot]
            cls = jnp.minimum(jnp.maximum(tag - 1, 0), per_owner - 1)
            bin_id = jnp.minimum(jnp.maximum(meta_ref[1, slot], 0), bins - 1)
            keep = (jnp.full((1, 128), tag, jnp.int32) > 0).astype(jnp.float32)
            coef_re, coef_im = kept[j]
            ctf = ctf_ref[bin_id]
            pred_re = ctf * ref_ref[cls, 0].astype(jnp.float32)
            pred_im = ctf * ref_ref[cls, 1].astype(jnp.float32)
            prod_re = (coef_re * pred_re + coef_im * pred_im).astype(jnp.bfloat16)
            prod_im = (coef_im * pred_re - coef_re * pred_im).astype(jnp.bfloat16)
            both = jnp.concatenate([prod_re, prod_im], axis=1)
            lanes = pack_ref[j].astype(jnp.float32)
            wide = lax.broadcasted_iota(jnp.int32, lanes.shape, 1)
            zero = jnp.zeros((), jnp.float32)
            cols = jnp.where(wide < 2 * span, pltpu.roll(lanes, 128 - 6 * span, 1), zero)
            cols_b = jnp.where(wide < 2 * span, pltpu.roll(lanes, 128 - 8 * span, 1), zero)
            mix = jnp.concatenate([cols, cols_b], axis=0).astype(jnp.bfloat16)
            part = jnp.dot(both, mix, preferred_element_type=jnp.float32)
            st.append(dict(slot=slot, cls=cls, keep=keep, ctf=ctf, coef_re=coef_re, coef_im=coef_im, part=part))
        for j, d in enumerate(st):
            p_hi, p_mid, p_lo = [piece.astype(jnp.float32) for piece in _split3(d["part"])]
            packed = (p_hi + pltpu.roll(p_mid, 2 * span, 1) + pltpu.roll(p_lo, 4 * span, 1)).astype(jnp.bfloat16)
            d["corr3"] = jnp.dot(flat_ref[j][0:16], packed, preferred_element_type=jnp.float32)
        for j, d in enumerate(st):
            corr3 = d["corr3"]
            corr = (corr3 + pltpu.roll(corr3, 128 - 2 * span, 1)) + pltpu.roll(corr3, 128 - 4 * span, 1)
            upper = corr[0:8]
            lower = pltpu.roll(corr[8:16], 128 - span, 1)
            score = jnp.where(inside, score_scale * (upper - lower), -jnp.inf)
            peak = jnp.max(jnp.max(score, axis=1, keepdims=True), axis=0, keepdims=True)
            total = jnp.sum(jnp.sum(jnp.exp(score - peak), axis=1, keepdims=True), axis=0, keepdims=True)
            evidence = peak + jnp.log(total)
            weight = jnp.where(inside, jnp.exp(score - evidence), 0.0)
            slot = d["slot"]
            row_shift = (jnp.full((8, 128), meta_ref[2, slot], jnp.int32) + sub - span // 2).astype(jnp.float32)
            col_shift = (jnp.full((8, 128), meta_ref[3, slot], jnp.int32) + lane - span // 2).astype(jnp.float32)
            by_row = jnp.sum(weight, axis=1, keepdims=True)
            mean_row = jnp.sum(by_row * row_shift[:, 0:1], axis=0, keepdims=True)
            by_col = jnp.sum(weight, axis=0, keepdims=True)
            mean_col = jnp.sum(jnp.where(inside[0:1], by_col * col_shift[0:1], 0.0), axis=1, keepdims=True)
            info_ref[j] = jnp.where(
                sub == 0,
                jnp.where(lane == 0, evidence, jnp.where(lane == 1, mean_row, jnp.where(lane == 2, mean_col, 0.0))),
                0.0,
            )
            shifted = pltpu.roll(weight, span, 1)
            stacked_w = jnp.concatenate([weight, shifted], axis=0)
            pad = jnp.zeros((112, 128), jnp.bfloat16)
            col_rows = jnp.concatenate([flat_ref[j][16:32], pad], axis=0)
            w_pieces = jnp.concatenate(_split3(stacked_w), axis=0)
            d["q3"] = jnp.dot(w_pieces, col_rows, preferred_element_type=jnp.float32)
        for j, d in enumerate(st):
            q3 = d["q3"]
            qpart = (q3[0:16] + q3[16:32]) + q3[32:48]
            q_re = qpart[0:8]
            q_im = qpart[8:16]
            spare = jnp.zeros((80, 128), jnp.bfloat16)
            rhs_re = jnp.concatenate(list(_split3(jnp.concatenate([q_re, -q_im], axis=0))) + [spare], axis=0)
            rhs_im = jnp.concatenate(list(_split3(jnp.concatenate([q_im, q_re], axis=0))) + [spare], axis=0)
            lanes = pack_ref[j]
            wide = lax.broadcasted_iota(jnp.int32, lanes.shape, 1)
            rows3 = jnp.where(wide < 6 * span, lanes, jnp.zeros((), jnp.bfloat16))
            d["back"] = jnp.dot(
                rows3, jnp.concatenate([rhs_re, rhs_im], axis=1), preferred_element_type=jnp.float32
            )
        for d in st:
            back_re = d["back"][:, 0:128]
            back_im = d["back"][:, 128:256]
            ctf, coef_re, coef_im, keep, cls = d["ctf"], d["coef_re"], d["coef_im"], d["keep"], d["cls"]
            term_re = ctf * (coef_re * back_re - coef_im * back_im)
            term_im = ctf * (coef_re * back_im + coef_im * back_re)
            total_ref[cls, 0] = total_ref[cls, 0] + term_re * keep
            total_ref[cls, 1] = total_ref[cls, 1] + term_im * keep
            total_ref[cls, 2] = total_ref[cls, 2] + ctf * ctf * keep


def group_eval(meta, order, coef, refs, ctf_tab, pack, flat, group, interpret=False):
    slots = coef.shape[0]
    per_owner = refs.shape[0]
    win = coef.shape[3]
    rows_sent = coef.shape[2]
    bins = ctf_tab.shape[0]
    table = jnp.concatenate([meta, order[None]], axis=0)

    def coef_map(j):
        return lambda g, table: (table[5, g * group + j], 0, 0, 0)

    grid_spec = pltpu.PrefetchScalarGridSpec(
        num_scalar_prefetch=1,
        grid=(slots // group,),
        in_specs=[pl.BlockSpec((1, 2, rows_sent, win), coef_map(j)) for j in range(group)]
        + [
            pl.BlockSpec((per_owner, 2, win, win), lambda g, table: (0, 0, 0, 0)),
            pl.BlockSpec((bins, win, win), lambda g, table: (0, 0, 0)),
            pl.BlockSpec((group, win, win), lambda g, table: (g, 0, 0)),
            pl.BlockSpec((group, flat.shape[1], win), lambda g, table: (g, 0, 0)),
        ],
        out_specs=[
            pl.BlockSpec((per_owner, 3, win, win), lambda g, table: (0, 0, 0, 0)),
            pl.BlockSpec((group, 8, 128), lambda g, table: (g, 0, 0)),
        ],
    )
    return pl.pallas_call(
        _group_kernel,
        grid_spec=grid_spec,
        out_shape=[
            jax.ShapeDtypeStruct((per_owner, 3, win, win), jnp.float32),
            jax.ShapeDtypeStruct((slots, 8, 128), jnp.float32),
        ],
        compiler_params=pltpu.CompilerParams(dimension_semantics=("arbitrary",)),
        interpret=interpret,
    )(table, *([coef] * group), refs, ctf_tab, pack, flat)


def phase_rows(anchor, img_side, win_side):
    shifts = anchor[:, None] + jnp.arange(TW, dtype=jnp.int32)[None, :] - TW // 2
    phase_int = shifts[:, :, None] * freq_ids(win_side)[None, None, :] % img_side
    angles = phase_int.astype(jnp.float32) * (2.0 * math.pi / img_side)
    return jnp.concatenate(
        [jnp.cos(angles).astype(jnp.bfloat16), jnp.sin(angles).astype(jnp.bfloat16)], axis=1
    )


def phase_pack(tag_flat, img_side, win_side):
    rows_t = phase_rows(tag_flat[:, 2], img_side, win_side)
    cols_t = phase_rows(tag_flat[:, 3], img_side, win_side)
    cols_bt = jnp.concatenate([-cols_t[:, TW:], cols_t[:, :TW]], axis=1)
    flat = jnp.concatenate([rows_t, cols_t], axis=1)
    stacked = jnp.concatenate([rows_t, rows_t, rows_t, cols_t, cols_bt], axis=1)
    stacked = jnp.pad(stacked, ((0, 0), (0, win_side - stacked.shape[1]), (0, 0)))
    return jnp.swapaxes(stacked, 1, 2), flat[:, : 4 * TW]


def on_device(images, references, particle_class, rotation, defocus_bin, window_anchor):
    part_count = images.shape[0]
    img_side = images.shape[1]
    win_side = references.shape[2]
    per_owner = references.shape[0]
    owners = lax.axis_size("dom")
    capacity = max(2, 2 * part_count // owners)
    slot_count = owners * capacity
    target = particle_class // per_owner
    local_class = particle_class - target * per_owner
    positions = jnp.arange(part_count, dtype=jnp.int32)
    same_owner = (target[:, None] == target[None, :]) & (positions[None, :] < positions[:, None])
    slot_rank = jnp.sum(same_owner.astype(jnp.int32), axis=1)
    slot_place = target * capacity + slot_rank
    slot_tags = jnp.stack(
        [local_class + 1, defocus_bin, window_anchor[0], window_anchor[1]], axis=1
    ).astype(jnp.bfloat16)
    tag_buffer = (
        jnp.zeros((slot_count, 4), jnp.bfloat16)
        .at[slot_place]
        .set(slot_tags)
        .reshape(owners, capacity, 4)
    )
    dft_cos, dft_sin = dft_tables(img_side, win_side)
    fourier_own = transform(images, rotation, dft_cos, dft_sin)
    half = win_side // 2
    edge = fourier_own[:, :, half + 1 :, 0]
    edge = jnp.pad(edge, ((0, 0), (0, 0), (0, win_side - edge.shape[2])))
    compact = jnp.concatenate([fourier_own[:, :, : half + 1, :], edge[:, :, None, :]], axis=2)
    hits = (slot_place[None, :] == jnp.arange(slot_count, dtype=jnp.int32)[:, None]).astype(jnp.bfloat16)
    buffer = jnp.einsum("qi,irjk->qrjk", hits, compact)
    buffer = buffer.reshape(owners, capacity, 2, half + 2, win_side)
    coeff_block = lax.all_to_all(buffer, "dom", split_axis=0, concat_axis=0, tiled=True)
    ctf_bins = ctf_table(jnp.arange(16, dtype=jnp.int32), win_side)
    tag_block = lax.all_to_all(tag_buffer, "dom", split_axis=0, concat_axis=0, tiled=True)
    tag_flat = tag_block.reshape(slot_count, 4).astype(jnp.int32)
    live = (tag_flat[:, 0] > 0).astype(jnp.int32)
    order = jnp.argsort(1 - live, stable=True).astype(jnp.int32)
    tag_sorted = tag_flat[order]
    count = jnp.sum(live)
    meta = jnp.concatenate(
        [tag_sorted.T, jnp.full((1, slot_count), count, jnp.int32)], axis=0
    )
    pack, flat = phase_pack(tag_sorted, img_side, win_side)
    group = 16 if slot_count % 16 == 0 else 1
    partial_value, info_sorted = group_eval(
        meta,
        order,
        coeff_block.reshape(slot_count, 2, win_side // 2 + 2, win_side),
        references,
        ctf_bins,
        pack,
        flat,
        group,
    )
    info = jnp.zeros((slot_count, 3), jnp.float32).at[order].set(info_sorted[:, 0, :3])
    returned = lax.all_to_all(
        info.reshape(owners, capacity, 3), "dom", split_axis=0, concat_axis=0, tiled=True
    )
    summed = lax.psum_scatter(partial_value, "cls", scatter_dimension=2, tiled=True)
    divisor = summed[:, 2] + ridge_term
    new_refs = summed[:, :2] / divisor[:, None]
    particle_info = returned.reshape(slot_count, 3)[slot_place]
    return (new_refs, particle_info.T)


def solution(mesh):
    return jax.shard_map(
        on_device,
        mesh=mesh,
        in_specs=(
            P(("copies", "dom", "cls"), None, None),
            P(("copies", "dom"), None, None, None),
            P(("copies", "dom", "cls")),
            P(("copies", "dom", "cls")),
            P(("copies", "dom", "cls")),
            P(None, ("copies", "dom", "cls")),
        ),
        out_specs=(P(("copies", "dom"), None, "cls", None), P(None, ("copies", "dom", "cls"))),
        check_vma=False,
    )
```
